32 devices in a mesh: groups: 2 (over y), lat: 4 (over x, core), lon: 4 (over z).
Axes of the slice: x: 2, y: 2, z: 4, core: 2. Of those that a mesh axis runs over, the one named last changes fastest.
Arguments:
- tracers: float32 [256, 256, 128], P(('groups', 'lat'), 'lon'), parts along dimension 0, may hold values from 0.3 to 12.6, as said below
- shifts: float32 [4, 3, 16, 32], P('groups'), parts along dimension 0, may hold values from 0 to 1
- diffusivity: float32 [128], P('lat'), may hold values from 0.02 to 0.2, as said below
- source_patch: int32 [4, 16, 32], P('groups'), parts along dimension 0, may hold values from 0 to 511, as said below
Outputs:
- advanced: float32 [256, 256, 128], P(('groups', 'lat'), 'lon'), parts along dimension 0
The draws below stay inside these ranges and needn't reach their ends.
There are 2 independent parts, one for each index of `groups`. The reference program is written for one: setup_inputs(seed, part) draws one part's arguments, and reference() takes and returns one part's arrays. A program takes and returns all parts, laid end to end along the dimension named above; an argument that names none is the same for every part. Nothing has to cross between parts.
Inputs may be any that keep to these rules, and one draw needn't show every extreme that they name: `source_patch`: entry [s, r, c] is the global index of the departure patch of destination patch (r, c) in step s; the departure patch lies in the same tile of 8 patch columns as the destination, and in the same band of 4 patch rows or in one of the two bands on either side. For each step, tile, destination band and other source band, at most 4 destination patches take their departure patch there, and every destination band has a source band that gives exactly 4. `tracers`: positive mixing ratios. `diffusivity`: positive diffusion numbers.
All inputs are finite; a program needn't handle non-finite values.
Results may differ from the reference program's by a relative error of at most 0.0003.
Values sent between devices are 32-bit elements; how exact they have to be, the bound alone decides.
No kernel may reach another device: no remote copies, remote signals or barrier semaphores. Data moves between devices by JAX's collectives and lax.ppermute only.
A program may use at most 64 MiB of HBM per device.

```python
import math
import jax
import jax.numpy as jnp
from jax import lax

TR = 32
LEV = 4
STEPS = 2
CAP = 4
CLAT = 32
CLON = 64
NLAT = 128
NLON = 256
PLAT = 16
PLON = 32


def draw_tracers(key, part):
    key_list = jax.random.split(jax.random.fold_in(key, 11), 2)
    tracer_scale = jnp.exp(jax.random.uniform(key_list[0], (TR,), jnp.float32, math.log(0.61), math.log(2.78)))
    channel = jnp.tile(tracer_scale, LEV)
    level_sign = jnp.where(jnp.arange(LEV) % 2 == 0, 1.0, -1.0).astype(jnp.float32)
    value_sign = jnp.repeat(level_sign, TR)
    inner_place = (jnp.arange(NLAT) % 8).astype(jnp.float32) / 7.0
    profile = 1.0 + (inner_place[:, None] - 0.5) * value_sign[None, :]
    base_value = jax.random.uniform(key_list[1], (NLAT, NLON, LEV * TR), jnp.float32, 1.0, 3.0)
    return (base_value * profile[:, None, :] * channel[None, None, :]).astype(jnp.float32)


def draw_diffusivity(key, part):
    inner_place = jnp.arange(NLAT) % 8
    lower = jnp.where(inner_place == 0, 0.1, 0.02).astype(jnp.float32)
    upper = jnp.where(inner_place == 7, 0.05, 0.2).astype(jnp.float32)
    unit = jax.random.uniform(jax.random.fold_in(key, 37), (NLAT,), jnp.float32, 0.0, 1.0)
    result = jnp.exp(jnp.log(lower) + (jnp.log(upper) - jnp.log(lower)) * unit)
    return jnp.clip(result, 0.02, 0.2).astype(jnp.float32)


def draw_source_patch(key, part):
    key_list = jax.random.split(jax.random.fold_in(key, 23), 5)
    per_rows = CLAT // 8
    per_cols = CLON // 8
    per_device = per_rows * per_cols
    lat_devs = NLAT // CLAT
    lon_devs = NLON // CLON
    dest_dev = jnp.arange(lat_devs)[None, None, :]
    jet_rows = jax.random.randint(key_list[0], (STEPS, lon_devs, 1), 0, lat_devs)
    reach_bands = jax.random.randint(key_list[4], (STEPS, lon_devs, lat_devs), 1, 3)
    edge_side = jnp.where(dest_dev < lat_devs - 1, 1, -1)
    toward = jnp.where(jet_rows > dest_dev, 1, jnp.where(jet_rows < dest_dev, -1, edge_side))
    first_pick = dest_dev + toward * reach_bands
    second_pick = dest_dev + toward
    third_pick = dest_dev - toward
    first_inside = (first_pick >= 0) & (first_pick < lat_devs)
    second_inside = (second_pick >= 0) & (second_pick < lat_devs)
    forced = jnp.where(first_inside, first_pick, jnp.where(second_inside, second_pick, third_pick))
    sources = jnp.arange(lat_devs)
    distance = jnp.abs(sources[None, :] - jnp.arange(lat_devs)[:, None])
    is_near = (distance >= 1) & (distance <= 2)
    counts = jax.random.randint(key_list[1], (STEPS, lon_devs, lat_devs, lat_devs), CAP // 2, CAP + 1)
    counts = jnp.where(is_near[None, None], counts, 0)
    counts = jnp.where(sources[None, None, None, :] == forced[..., None], CAP, counts)
    end_marks = jnp.cumsum(counts, axis=-1)
    places = jnp.arange(per_device)
    source_dev = jnp.sum((end_marks[..., None, :] <= places[:, None]).astype(jnp.int32), axis=-1)
    remote_total = end_marks[..., -1:]
    own_band = jnp.arange(lat_devs)[None, None, :, None]
    source_dev = jnp.where(places[None, None, None, :] < remote_total, source_dev, own_band)
    scores = jax.random.randint(key_list[2], (STEPS, lon_devs, lat_devs, per_device), 0, 1048576) * per_device + places
    shuffle = jnp.argsort(scores, axis=-1, stable=True)
    source_dev = jnp.take_along_axis(source_dev, shuffle, axis=-1)
    local_index = jax.random.randint(key_list[3], (STEPS, lon_devs, lat_devs, per_device), 0, per_device)
    tile_index = jnp.arange(lon_devs)[None, :, None, None]
    source_row = source_dev * per_rows + local_index // per_cols
    source_col = tile_index * per_cols + local_index % per_cols
    global_index = source_row * (NLON // 8) + source_col
    global_index = global_index.reshape(STEPS, lon_devs, lat_devs, per_rows, per_cols).transpose(0, 2, 3, 1, 4)
    return global_index.reshape(STEPS, NLAT // 8, NLON // 8).astype(jnp.int32)


def setup_inputs(seed: int = 0, part: int = 0) -> dict:
    arg_keys = jax.random.split(jax.random.key(seed), 5)
    part_keys = jax.random.split(jax.random.fold_in(arg_keys[4], part), 5)
    tracers = draw_tracers(jax.random.fold_in(jax.random.fold_in(arg_keys[4], part), 71), part)
    shifts = jnp.clip(jax.random.uniform(part_keys[1], (STEPS, 3, PLAT, PLON), jnp.float32, 0.0, 1.0), 0.0, 1.0)
    diffusivity = draw_diffusivity(jax.random.fold_in(arg_keys[4], 71), part)
    source_patch = draw_source_patch(jax.random.fold_in(jax.random.fold_in(arg_keys[4], part), 71), part)
    return {"tracers": tracers, "shifts": shifts, "diffusivity": diffusivity, "source_patch": source_patch}


def cubic_weights(fraction):
    first_term = -fraction * (fraction - 1.0) * (fraction - 2.0) / 6.0
    second_term = (fraction + 1.0) * (fraction - 1.0) * (fraction - 2.0) / 2.0
    third_term = -(fraction + 1.0) * fraction * (fraction - 2.0) / 2.0
    fourth_term = (fraction + 1.0) * fraction * (fraction - 1.0) / 6.0
    return (first_term, second_term, third_term, fourth_term)


def cubic_matrix(fraction, extent):
    places = jnp.arange(extent)
    running = jnp.zeros(fraction.shape + (extent, extent), jnp.float32)
    for offset, weight in zip(range(-1, 3), cubic_weights(fraction)):
        target_col = jnp.clip(places + offset, 0, extent - 1)
        indicator = (target_col[:, None] == places[None, :]).astype(jnp.float32)
        running = running + weight[..., None, None] * indicator
    return running


def interpolate(patches, fraction_y, fraction_x, fraction_z):
    patch_count = patches.shape[0]
    value_count = patches.shape[2]
    weight_y = cubic_matrix(fraction_y, 8)
    weight_x = cubic_matrix(fraction_x, 8)
    plane_weights = jnp.einsum("nac,nbd->nabcd", weight_y, weight_x, precision=lax.Precision.HIGHEST).reshape(patch_count, 64, 64)
    flat_result = jnp.einsum("nij,njv->niv", plane_weights, patches, precision=lax.Precision.HIGHEST)
    stacked = flat_result.reshape(patch_count, 64, LEV, value_count // LEV)
    weight_z = cubic_matrix(fraction_z, LEV)
    levelled = jnp.einsum("nlm,nimt->nilt", weight_z, stacked, precision=lax.Precision.HIGHEST)
    return levelled.reshape(patch_count, 64, value_count)


def to_patches(state_field):
    band_rows = state_field.shape[0] // 8
    band_cols = state_field.shape[1] // 8
    return state_field.reshape(band_rows, 8, band_cols, 8, -1).transpose(0, 2, 1, 3, 4).reshape(band_rows * band_cols, 64, -1)


def from_patches(patches, band_rows, band_cols):
    return patches.reshape(band_rows, band_cols, 8, 8, -1).transpose(0, 2, 1, 3, 4).reshape(band_rows * 8, band_cols * 8, -1)


def column_area(first_row, row_count, total_rows):
    latitude = ((first_row + jnp.arange(row_count)).astype(jnp.float32) + 0.5) * (math.pi / total_rows) - 0.5 * math.pi
    return jnp.cos(latitude)


def column_mass(state_field, weights):
    return jnp.sum(weights[:, None, None] * state_field, axis=(0, 1))


def diffuse(advected, diffusivity):
    padded = jnp.pad(advected, ((1, 1), (0, 0), (0, 0)))
    laplace = padded[2:] + padded[:-2] + jnp.roll(advected, -1, axis=1) + jnp.roll(advected, 1, axis=1) - 4.0 * advected
    return advected + diffusivity[:, None, None] * laplace


def reference(tracers, shifts, diffusivity, source_patch):
    weights = column_area(0, NLAT, NLAT)
    target = column_mass(tracers, weights)
    state_field = tracers
    for step_index in range(STEPS):
        departed = to_patches(state_field)[source_patch[step_index].reshape(-1)]
        fractions = shifts[step_index].reshape(3, -1)
        finished = interpolate(departed, fractions[0], fractions[1], fractions[2])
        advected = from_patches(finished, NLAT // 8, NLON // 8)
        diffused = diffuse(advected, diffusivity)
        state_field = diffused * (target / column_mass(diffused, weights))[None, None, :]
    return state_field
```

```python
import math

import jax
import jax.numpy as jnp
from jax import lax
from jax.sharding import PartitionSpec as P

LEV = 4
STEPS = 2
CAP = 4


def from_behind(block, axis, distance):
    devices = range(lax.axis_size(axis))
    route = [(i - distance, i) for i in devices if i - distance in devices]
    return lax.ppermute(block, axis, route)


def all_sum(value, axes):
    for axis in axes:
        count = lax.axis_size(axis)
        if count & (count - 1):
            value = lax.psum(value, axis)
            continue
        distance = 1
        while distance < count:
            value = value + lax.ppermute(
                value, axis, [(i, i ^ distance) for i in range(count)]
            )
            distance *= 2
    return value


def extended(cells, sides, width, closed):
    for axis, dim in sides:
        count = lax.axis_size(axis)
        ends = count if closed else count - 1
        head = lax.slice_in_dim(cells, 0, width, axis=dim)
        tail = lax.slice_in_dim(cells, cells.shape[dim] - width, cells.shape[dim], axis=dim)
        cells = jnp.concatenate(
            [
                lax.ppermute(tail, axis, [(i, (i + 1) % count) for i in range(ends)]),
                cells,
                lax.ppermute(head, axis, [((i + 1) % count, i) for i in range(ends)]),
            ],
            axis=dim,
        )
    return cells


def cubic_weights(fraction):
    first_term = -fraction * (fraction - 1.0) * (fraction - 2.0) / 6.0
    second_term = (fraction + 1.0) * (fraction - 1.0) * (fraction - 2.0) / 2.0
    third_term = -(fraction + 1.0) * fraction * (fraction - 2.0) / 2.0
    fourth_term = (fraction + 1.0) * fraction * (fraction - 1.0) / 6.0
    return (first_term, second_term, third_term, fourth_term)


def cubic_matrix(fraction, extent):
    places = jnp.arange(extent)
    running = jnp.zeros(fraction.shape + (extent, extent), jnp.float32)
    for offset, weight in zip(range(-1, 3), cubic_weights(fraction)):
        target_col = jnp.clip(places + offset, 0, extent - 1)
        indicator = (target_col[:, None] == places[None, :]).astype(jnp.float32)
        running = running + weight[..., None, None] * indicator
    return running


def interpolate(patches, fraction_y, fraction_x, fraction_z):
    patch_count = patches.shape[0]
    value_count = patches.shape[2]
    weight_y = cubic_matrix(fraction_y, 8)
    weight_x = cubic_matrix(fraction_x, 8)
    plane_weights = jnp.einsum(
        "nac,nbd->nabcd", weight_y, weight_x, precision=lax.Precision.HIGHEST
    ).reshape(patch_count, 64, 64)
    flat_result = jnp.einsum(
        "nij,njv->niv", plane_weights, patches, precision=lax.Precision.HIGHEST
    )
    stacked = flat_result.reshape(patch_count, 64, LEV, value_count // LEV)
    weight_z = cubic_matrix(fraction_z, LEV)
    levelled = jnp.einsum("nlm,nimt->nilt", weight_z, stacked, precision=lax.Precision.HIGHEST)
    return levelled.reshape(patch_count, 64, value_count)


def to_patches(state_field):
    band_rows = state_field.shape[0] // 8
    band_cols = state_field.shape[1] // 8
    return (
        state_field.reshape(band_rows, 8, band_cols, 8, -1)
        .transpose(0, 2, 1, 3, 4)
        .reshape(band_rows * band_cols, 64, -1)
    )


def from_patches(patches, band_rows, band_cols):
    return (
        patches.reshape(band_rows, band_cols, 8, 8, -1)
        .transpose(0, 2, 1, 3, 4)
        .reshape(band_rows * 8, band_cols * 8, -1)
    )


def column_area(first_row, row_count, total_rows):
    latitude = ((first_row + jnp.arange(row_count)).astype(jnp.float32) + 0.5) * (
        math.pi / total_rows
    ) - 0.5 * math.pi
    return jnp.cos(latitude)


def column_mass(state_field, weights):
    return jnp.sum(weights[:, None, None] * state_field, axis=(0, 1))


def local(tracers, shifts, diffusivity, source_patch):
    lat_count = lax.axis_size("lat")
    lat_index = lax.axis_index("lat")
    lon_index = lax.axis_index("lon")
    row_count, col_count, value_count = tracers.shape
    band_rows = row_count // 8
    band_cols = col_count // 8
    per_device = band_rows * band_cols
    total_cols = source_patch.shape[2]
    band_offsets = (-2, -1, 1, 2)
    weights = column_area(lat_index * row_count, row_count, row_count * lat_count)
    devices = jnp.arange(lat_count)
    slot_range = jnp.arange(CAP)
    state_field = tracers
    target_part = column_mass(tracers, weights)
    target = None
    for step_index in range(STEPS):
        column_ids = lax.dynamic_slice_in_dim(
            source_patch[step_index], lon_index * band_cols, band_cols, 1
        ).reshape(lat_count, per_device)
        fractions = lax.dynamic_slice_in_dim(
            shifts[step_index], lon_index * band_cols, band_cols, 2
        ).reshape(3, lat_count, per_device)
        source_row = column_ids // total_cols
        source_dev = source_row // band_rows
        source_local = (
            source_row % band_rows * band_cols + column_ids % total_cols - lon_index * band_cols
        )
        remote = source_dev != devices[:, None]
        matches = (source_dev[:, :, None] == devices[None, None, :]) & remote[:, :, None]
        slot_ranks = jnp.cumsum(matches.astype(jnp.int32), axis=1) - 1
        slot_of = jnp.sum(jnp.where(matches, slot_ranks, 0), axis=2)
        owned_here = remote & (source_dev == lat_index)
        sending = owned_here[:, :, None] & (slot_of[:, :, None] == slot_range[None, None, :])
        send_local = jnp.sum(jnp.where(sending, source_local[:, :, None], 0), axis=1)
        near_local = jnp.stack(
            [
                lax.dynamic_index_in_dim(send_local, lat_index + offset, 0, keepdims=False)
                for offset in band_offsets
            ]
        )
        own_patches = to_patches(state_field)
        send_patches = own_patches[near_local.reshape(-1)]
        my_dev = lax.dynamic_index_in_dim(source_dev, lat_index, 0, keepdims=False)
        my_slot = lax.dynamic_index_in_dim(slot_of, lat_index, 0, keepdims=False)
        my_local = lax.dynamic_index_in_dim(source_local, lat_index, 0, keepdims=False)
        my_remote = lax.dynamic_index_in_dim(remote, lat_index, 0, keepdims=False)
        my_frac = lax.dynamic_index_in_dim(fractions, lat_index, 1, keepdims=False)
        my_offset = lat_index - my_dev
        pick_index = jnp.where(my_offset < 0, my_offset + 2, my_offset + 1) * CAP + my_slot
        send_frac = jnp.sum(jnp.where(sending[None], fractions[:, :, :, None], 0.0), axis=2)
        near_frac = jnp.stack(
            [
                lax.dynamic_index_in_dim(send_frac, lat_index + offset, 1, keepdims=False)
                for offset in band_offsets
            ],
            axis=1,
        ).reshape(3, -1)
        outgoing = interpolate(send_patches, near_frac[0], near_frac[1], near_frac[2])
        outgoing = outgoing.reshape(4, CAP, 64, value_count)
        arrived = jnp.stack(
            [
                from_behind(outgoing[slot_place], "lat", offset)
                for slot_place, offset in enumerate(band_offsets)
            ]
        )
        arrived = arrived.reshape(4 * CAP, 64, value_count)
        local_done = interpolate(own_patches[my_local], my_frac[0], my_frac[1], my_frac[2])
        finished = jnp.where(my_remote[:, None, None], arrived[pick_index], local_done)
        advected = from_patches(finished, band_rows, band_cols)
        lon_wide = extended(advected, (("lon", 1),), 1, True)
        lat_wide = extended(advected, (("lat", 0),), 1, False)
        laplace = lat_wide[2:] + lat_wide[:-2] + lon_wide[:, 2:] + lon_wide[:, :-2] - 4.0 * advected
        diffused = advected + diffusivity[:, None, None] * laplace
        if target is None:
            both = all_sum(
                jnp.concatenate([target_part, column_mass(diffused, weights)]), ("lon", "lat")
            )
            target, step_total = both[:value_count], both[value_count:]
        else:
            step_total = all_sum(column_mass(diffused, weights), ("lon", "lat"))
        state_field = diffused * (target / step_total)[None, None, :]
    return state_field


def solution(mesh):
    return jax.shard_map(
        local,
        mesh=mesh,
        in_specs=(
            P(("groups", "lat"), "lon", None),
            P("groups", None, None, None),
            P("lat"),
            P("groups", None, None),
        ),
        out_specs=P(("groups", "lat"), "lon", None),
        check_vma=False,
    )
```

```python
import math

import jax
import jax.numpy as jnp
from jax import lax
from jax.sharding import PartitionSpec as P

LEV = 4
STEPS = 2
CAP = 4


def from_behind(block, axis, distance):
    devices = range(lax.axis_size(axis))
    route = [(i - distance, i) for i in devices if i - distance in devices]
    return lax.ppermute(block, axis, route)


def all_sum(value, axes):
    for axis in axes:
        count = lax.axis_size(axis)
        if count & (count - 1):
            value = lax.psum(value, axis)
            continue
        distance = 1
        while distance < count:
            value = value + lax.ppermute(
                value, axis, [(i, i ^ distance) for i in range(count)]
            )
            distance *= 2
    return value


def extended(cells, sides, width, closed):
    for axis, dim in sides:
        count = lax.axis_size(axis)
        ends = count if closed else count - 1
        head = lax.slice_in_dim(cells, 0, width, axis=dim)
        tail = lax.slice_in_dim(cells, cells.shape[dim] - width, cells.shape[dim], axis=dim)
        cells = jnp.concatenate(
            [
                lax.ppermute(tail, axis, [(i, (i + 1) % count) for i in range(ends)]),
                cells,
                lax.ppermute(head, axis, [((i + 1) % count, i) for i in range(ends)]),
            ],
            axis=dim,
        )
    return cells


def cubic_weights(fraction):
    first_term = -fraction * (fraction - 1.0) * (fraction - 2.0) / 6.0
    second_term = (fraction + 1.0) * (fraction - 1.0) * (fraction - 2.0) / 2.0
    third_term = -(fraction + 1.0) * fraction * (fraction - 2.0) / 2.0
    fourth_term = (fraction + 1.0) * fraction * (fraction - 1.0) / 6.0
    return (first_term, second_term, third_term, fourth_term)


def cubic_matrix(fraction, extent):
    places = jnp.arange(extent)
    running = jnp.zeros(fraction.shape + (extent, extent), jnp.float32)
    for offset, weight in zip(range(-1, 3), cubic_weights(fraction)):
        target_col = jnp.clip(places + offset, 0, extent - 1)
        indicator = (target_col[:, None] == places[None, :]).astype(jnp.float32)
        running = running + weight[..., None, None] * indicator
    return running


def spatial(patches, fraction_y, fraction_x):
    patch_count = patches.shape[0]
    weight_y = cubic_matrix(fraction_y, 8)
    weight_x = cubic_matrix(fraction_x, 8)
    plane_weights = jnp.einsum(
        "nac,nbd->nabcd", weight_y, weight_x, precision=lax.Precision.HIGHEST
    ).reshape(patch_count, 64, 64)
    return jnp.einsum("nij,njv->niv", plane_weights, patches, precision=lax.Precision.HIGHEST)


def levels(flat, fraction_z):
    patch_count, cols, value_count = flat.shape
    stacked = flat.reshape(patch_count, cols, LEV, value_count // LEV)
    weight_z = cubic_matrix(fraction_z, LEV)
    levelled = jnp.einsum("nlm,nimt->nilt", weight_z, stacked, precision=lax.Precision.HIGHEST)
    return levelled.reshape(patch_count, cols, value_count)


def to_patches(state_field):
    band_rows = state_field.shape[0] // 8
    band_cols = state_field.shape[1] // 8
    return (
        state_field.reshape(band_rows, 8, band_cols, 8, -1)
        .transpose(0, 2, 1, 3, 4)
        .reshape(band_rows * band_cols, 64, -1)
    )


def from_patches(patches, band_rows, band_cols):
    return (
        patches.reshape(band_rows, band_cols, 8, 8, -1)
        .transpose(0, 2, 1, 3, 4)
        .reshape(band_rows * 8, band_cols * 8, -1)
    )


def column_area(first_row, row_count, total_rows):
    latitude = ((first_row + jnp.arange(row_count)).astype(jnp.float32) + 0.5) * (
        math.pi / total_rows
    ) - 0.5 * math.pi
    return jnp.cos(latitude)


def column_mass(state_field, weights):
    return jnp.sum(weights[:, None, None] * state_field, axis=(0, 1))


def diffuse(advected, diffusivity, row_dim):
    col_dim = row_dim + 1
    rows = advected.shape[row_dim]
    cols = advected.shape[col_dim]
    lon_wide = extended(advected, (("lon", col_dim),), 1, True)
    lat_wide = extended(advected, (("lat", row_dim),), 1, False)
    laplace = (
        lax.slice_in_dim(lat_wide, 2, rows + 2, axis=row_dim)
        + lax.slice_in_dim(lat_wide, 0, rows, axis=row_dim)
        + lax.slice_in_dim(lon_wide, 2, cols + 2, axis=col_dim)
        + lax.slice_in_dim(lon_wide, 0, cols, axis=col_dim)
        - 4.0 * advected
    )
    k_shape = [1] * advected.ndim
    k_shape[row_dim] = rows
    return advected + diffusivity.reshape(k_shape) * laplace


def departed(state_field, source_ids, shifts_now):
    lat_count = lax.axis_size("lat")
    lat_index = lax.axis_index("lat")
    lon_index = lax.axis_index("lon")
    row_count, col_count, value_count = state_field.shape
    band_rows = row_count // 8
    band_cols = col_count // 8
    per_device = band_rows * band_cols
    total_cols = source_ids.shape[1]
    band_offsets = (-2, -1, 1, 2)
    devices = jnp.arange(lat_count)
    slot_range = jnp.arange(CAP)
    column_ids = lax.dynamic_slice_in_dim(
        source_ids, lon_index * band_cols, band_cols, 1
    ).reshape(lat_count, per_device)
    fractions = lax.dynamic_slice_in_dim(
        shifts_now, lon_index * band_cols, band_cols, 2
    ).reshape(3, lat_count, per_device)
    source_row = column_ids // total_cols
    source_dev = source_row // band_rows
    source_local = (
        source_row % band_rows * band_cols + column_ids % total_cols - lon_index * band_cols
    )
    remote = source_dev != devices[:, None]
    matches = (source_dev[:, :, None] == devices[None, None, :]) & remote[:, :, None]
    slot_ranks = jnp.cumsum(matches.astype(jnp.int32), axis=1) - 1
    slot_of = jnp.sum(jnp.where(matches, slot_ranks, 0), axis=2)
    owned_here = remote & (source_dev == lat_index)
    sending = owned_here[:, :, None] & (slot_of[:, :, None] == slot_range[None, None, :])
    send_local = jnp.sum(jnp.where(sending, source_local[:, :, None], 0), axis=1)
    near_local = jnp.stack(
        [
            lax.dynamic_index_in_dim(send_local, lat_index + offset, 0, keepdims=False)
            for offset in band_offsets
        ]
    )
    own_patches = to_patches(state_field)
    outgoing = own_patches[near_local.reshape(-1)].reshape(4, CAP, 64, value_count)
    my_dev = lax.dynamic_index_in_dim(source_dev, lat_index, 0, keepdims=False)
    my_slot = lax.dynamic_index_in_dim(slot_of, lat_index, 0, keepdims=False)
    my_local = lax.dynamic_index_in_dim(source_local, lat_index, 0, keepdims=False)
    my_remote = lax.dynamic_index_in_dim(remote, lat_index, 0, keepdims=False)
    my_frac = lax.dynamic_index_in_dim(fractions, lat_index, 1, keepdims=False)
    my_offset = lat_index - my_dev
    pick_index = jnp.where(my_offset < 0, my_offset + 2, my_offset + 1) * CAP + my_slot
    arrived = jnp.stack(
        [
            from_behind(outgoing[slot_place], "lat", offset)
            for slot_place, offset in enumerate(band_offsets)
        ]
    ).reshape(4 * CAP, 64, value_count)
    patches = jnp.where(my_remote[:, None, None], arrived[pick_index], own_patches[my_local])
    return patches, my_frac


def local(tracers, shifts, diffusivity, source_patch):
    lat_count = lax.axis_size("lat")
    lat_index = lax.axis_index("lat")
    row_count, col_count, value_count = tracers.shape
    band_rows = row_count // 8
    band_cols = col_count // 8
    per_device = band_rows * band_cols
    per_level = value_count // LEV
    total_rows = row_count * lat_count
    weights = column_area(lat_index * row_count, row_count, total_rows)
    target_part = column_mass(tracers, weights)

    patches, frac = departed(tracers, source_patch[0], shifts[0])
    advected = from_patches(levels(spatial(patches, frac[0], frac[1]), frac[2]), band_rows, band_cols)
    first = diffuse(advected, diffusivity, 0)
    first_part = column_mass(first, weights)

    patches, frac = departed(first, source_patch[1], shifts[1])
    planar = spatial(patches, frac[0], frac[1])
    weight_z = cubic_matrix(frac[2], LEV)

    k_wide = extended(diffusivity, (("lat", 0),), 1, False)
    area_wide = column_area(lat_index * row_count - 1, row_count + 2, total_rows)
    flux = area_wide * k_wide
    g = weights - 2.0 * flux[1:-1] + flux[:-2] + flux[2:]
    g_cols = jnp.broadcast_to(g.reshape(band_rows, 1, 8, 1), (band_rows, band_cols, 8, 8))
    weighted = jnp.einsum(
        "pi,piv->pv", g_cols.reshape(per_device, 64), planar, precision=lax.Precision.HIGHEST
    ).reshape(per_device, LEV, per_level)
    mix_part = jnp.einsum(
        "plm,pmt->lmt", weight_z, weighted, precision=lax.Precision.HIGHEST
    )
    totals = all_sum(
        jnp.concatenate([target_part, first_part, mix_part.reshape(-1)]), ("lon", "lat")
    )
    target = totals[:value_count]
    first_mass = totals[value_count : 2 * value_count]
    mix = totals[2 * value_count :].reshape(LEV, LEV, per_level)
    first_ratio = (target / first_mass).reshape(LEV, per_level)
    second_mass = jnp.sum(first_ratio[None] * mix, axis=1).reshape(value_count)
    second_ratio = target / second_mass

    parts = []
    for source_level in range(LEV):
        block = planar[:, :, source_level * per_level : (source_level + 1) * per_level]
        spread = jnp.concatenate(
            [weight_z[:, level, source_level][:, None, None] * block for level in range(LEV)],
            axis=2,
        )
        parts.append(from_patches(spread, band_rows, band_cols))
    spread_diffused = diffuse(jnp.stack(parts), diffusivity, 1)
    factor = jnp.tile(first_ratio, (1, LEV))
    combined = jnp.sum(factor[:, None, None, :] * spread_diffused, axis=0)
    return combined * second_ratio[None, None, :]


def solution(mesh):
    return jax.shard_map(
        local,
        mesh=mesh,
        in_specs=(
            P(("groups", "lat"), "lon", None),
            P("groups", None, None, None),
            P("lat"),
            P("groups", None, None),
        ),
        out_specs=P(("groups", "lat"), "lon", None),
        check_vma=False,
    )
```

```python
import math

import jax
import jax.numpy as jnp
from jax import lax
from jax.sharding import PartitionSpec as P

LEV = 4
STEPS = 2
CAP = 4


def from_behind(block, axis, distance):
    devices = range(lax.axis_size(axis))
    route = [(i - distance, i) for i in devices if i - distance in devices]
    return lax.ppermute(block, axis, route)


def all_sum(value, axes):
    for axis in axes:
        count = lax.axis_size(axis)
        if count & (count - 1):
            value = lax.psum(value, axis)
            continue
        distance = 1
        while distance < count:
            value = value + lax.ppermute(
                value, axis, [(i, i ^ distance) for i in range(count)]
            )
            distance *= 2
    return value


def extended(cells, sides, width, closed):
    for axis, dim in sides:
        count = lax.axis_size(axis)
        ends = count if closed else count - 1
        head = lax.slice_in_dim(cells, 0, width, axis=dim)
        tail = lax.slice_in_dim(cells, cells.shape[dim] - width, cells.shape[dim], axis=dim)
        cells = jnp.concatenate(
            [
                lax.ppermute(tail, axis, [(i, (i + 1) % count) for i in range(ends)]),
                cells,
                lax.ppermute(head, axis, [((i + 1) % count, i) for i in range(ends)]),
            ],
            axis=dim,
        )
    return cells


def cubic_weights(fraction):
    first_term = -fraction * (fraction - 1.0) * (fraction - 2.0) / 6.0
    second_term = (fraction + 1.0) * (fraction - 1.0) * (fraction - 2.0) / 2.0
    third_term = -(fraction + 1.0) * fraction * (fraction - 2.0) / 2.0
    fourth_term = (fraction + 1.0) * fraction * (fraction - 1.0) / 6.0
    return (first_term, second_term, third_term, fourth_term)


def cubic_matrix(fraction, extent):
    places = jnp.arange(extent)
    running = jnp.zeros(fraction.shape + (extent, extent), jnp.float32)
    for offset, weight in zip(range(-1, 3), cubic_weights(fraction)):
        target_col = jnp.clip(places + offset, 0, extent - 1)
        indicator = (target_col[:, None] == places[None, :]).astype(jnp.float32)
        running = running + weight[..., None, None] * indicator
    return running


def tap_sources(target, extent):
    return sorted({min(max(target + offset, 0), extent - 1) for offset in range(-1, 3)})


def plane_weights(fraction_y, fraction_x):
    rows = lax.broadcasted_iota(jnp.int32, (1, 64, 64), 1)
    cols = lax.broadcasted_iota(jnp.int32, (1, 64, 64), 2)

    def along(fraction, source, target):
        running = jnp.zeros((fraction.shape[0], 64, 64), jnp.float32)
        for offset, weight in zip(range(-1, 3), cubic_weights(fraction)):
            indicator = (jnp.clip(source + offset, 0, 7) == target).astype(jnp.float32)
            running = running + weight[:, None, None] * indicator
        return running

    return along(fraction_y, rows // 8, cols // 8) * along(fraction_x, rows % 8, cols % 8)


def spatial(patches, fraction_y, fraction_x):
    return jnp.einsum(
        "nij,njv->niv",
        plane_weights(fraction_y, fraction_x),
        patches,
        precision=lax.Precision.HIGHEST,
    )


def levels(flat, fraction_z):
    value_count = flat.shape[2]
    per_level = value_count // LEV
    weight_z = cubic_matrix(fraction_z, LEV)
    blocks = [flat[:, :, m * per_level : (m + 1) * per_level] for m in range(LEV)]
    out = []
    for level in range(LEV):
        acc = None
        for m in tap_sources(level, LEV):
            term = weight_z[:, level, m][:, None, None] * blocks[m]
            acc = term if acc is None else acc + term
        out.append(acc)
    return jnp.concatenate(out, axis=2)


def to_patches(state_field):
    band_rows = state_field.shape[0] // 8
    band_cols = state_field.shape[1] // 8
    return (
        state_field.reshape(band_rows, 8, band_cols, 8, -1)
        .transpose(0, 2, 1, 3, 4)
        .reshape(band_rows * band_cols, 64, -1)
    )


def from_patches(patches, band_rows, band_cols):
    return (
        patches.reshape(band_rows, band_cols, 8, 8, -1)
        .transpose(0, 2, 1, 3, 4)
        .reshape(band_rows * 8, band_cols * 8, -1)
    )


def column_area(first_row, row_count, total_rows):
    latitude = ((first_row + jnp.arange(row_count)).astype(jnp.float32) + 0.5) * (
        math.pi / total_rows
    ) - 0.5 * math.pi
    return jnp.cos(latitude)


def column_mass(state_field, weights):
    return jnp.sum(weights[:, None, None] * state_field, axis=(0, 1))


def diffuse(advected, diffusivity, row_dim):
    col_dim = row_dim + 1
    rows = advected.shape[row_dim]
    cols = advected.shape[col_dim]
    lon_wide = extended(advected, (("lon", col_dim),), 1, True)
    lat_wide = extended(advected, (("lat", row_dim),), 1, False)
    laplace = (
        lax.slice_in_dim(lat_wide, 2, rows + 2, axis=row_dim)
        + lax.slice_in_dim(lat_wide, 0, rows, axis=row_dim)
        + lax.slice_in_dim(lon_wide, 2, cols + 2, axis=col_dim)
        + lax.slice_in_dim(lon_wide, 0, cols, axis=col_dim)
        - 4.0 * advected
    )
    k_shape = [1] * advected.ndim
    k_shape[row_dim] = rows
    return advected + diffusivity.reshape(k_shape) * laplace


def diffuse_first(advected, diffusivity):
    rows, cols, value_count = advected.shape
    count = lax.axis_size("lat")

    def pack(row, number):
        return jnp.concatenate(
            [row, jnp.broadcast_to(number, (1, 1, value_count))], axis=1
        )

    from_above = lax.ppermute(
        pack(advected[rows - 1 :], diffusivity[rows - 1]),
        "lat",
        [(i, i + 1) for i in range(count - 1)],
    )
    from_below = lax.ppermute(
        pack(advected[:1], diffusivity[0]), "lat", [(i + 1, i) for i in range(count - 1)]
    )
    lat_wide = jnp.concatenate([from_above[:, :cols], advected, from_below[:, :cols]], axis=0)
    k_wide = jnp.concatenate([from_above[0, cols, :1], diffusivity, from_below[0, cols, :1]])
    lon_wide = extended(advected, (("lon", 1),), 1, True)
    laplace = (
        lat_wide[2:] + lat_wide[:-2] + lon_wide[:, 2:] + lon_wide[:, :-2] - 4.0 * advected
    )
    return advected + diffusivity[:, None, None] * laplace, k_wide


def departed(state_field, source_ids, shifts_now):
    lat_count = lax.axis_size("lat")
    lat_index = lax.axis_index("lat")
    lon_index = lax.axis_index("lon")
    row_count, col_count, value_count = state_field.shape
    band_rows = row_count // 8
    band_cols = col_count // 8
    per_device = band_rows * band_cols
    total_cols = source_ids.shape[1]
    band_offsets = (-2, -1, 1, 2)
    devices = jnp.arange(lat_count)
    slot_range = jnp.arange(CAP)
    column_ids = lax.dynamic_slice_in_dim(
        source_ids, lon_index * band_cols, band_cols, 1
    ).reshape(lat_count, per_device)
    fractions = lax.dynamic_slice_in_dim(
        shifts_now, lon_index * band_cols, band_cols, 2
    ).reshape(3, lat_count, per_device)
    source_row = column_ids // total_cols
    source_dev = source_row // band_rows
    source_local = (
        source_row % band_rows * band_cols + column_ids % total_cols - lon_index * band_cols
    )
    remote = source_dev != devices[:, None]
    matches = (source_dev[:, :, None] == devices[None, None, :]) & remote[:, :, None]
    slot_ranks = jnp.cumsum(matches.astype(jnp.int32), axis=1) - 1
    slot_of = jnp.sum(jnp.where(matches, slot_ranks, 0), axis=2)
    owned_here = remote & (source_dev == lat_index)
    sending = owned_here[:, :, None] & (slot_of[:, :, None] == slot_range[None, None, :])
    send_local = jnp.sum(jnp.where(sending, source_local[:, :, None], 0), axis=1)
    near_local = jnp.stack(
        [
            lax.dynamic_index_in_dim(send_local, lat_index + offset, 0, keepdims=False)
            for offset in band_offsets
        ]
    )
    own_patches = to_patches(state_field)
    outgoing = own_patches[near_local.reshape(-1)].reshape(4, CAP, 64, value_count)
    my_dev = lax.dynamic_index_in_dim(source_dev, lat_index, 0, keepdims=False)
    my_slot = lax.dynamic_index_in_dim(slot_of, lat_index, 0, keepdims=False)
    my_local = lax.dynamic_index_in_dim(source_local, lat_index, 0, keepdims=False)
    my_remote = lax.dynamic_index_in_dim(remote, lat_index, 0, keepdims=False)
    my_frac = lax.dynamic_index_in_dim(fractions, lat_index, 1, keepdims=False)
    my_offset = lat_index - my_dev
    pick_index = jnp.where(my_offset < 0, my_offset + 2, my_offset + 1) * CAP + my_slot
    arrived = jnp.stack(
        [
            from_behind(outgoing[slot_place], "lat", offset)
            for slot_place, offset in enumerate(band_offsets)
        ]
    ).reshape(4 * CAP, 64, value_count)
    patches = jnp.where(my_remote[:, None, None], arrived[pick_index], own_patches[my_local])
    return patches, my_frac


def local(tracers, shifts, diffusivity, source_patch):
    lat_count = lax.axis_size("lat")
    lat_index = lax.axis_index("lat")
    row_count, col_count, value_count = tracers.shape
    band_rows = row_count // 8
    band_cols = col_count // 8
    per_device = band_rows * band_cols
    per_level = value_count // LEV
    total_rows = row_count * lat_count
    weights = column_area(lat_index * row_count, row_count, total_rows)
    target_part = column_mass(tracers, weights)

    patches, frac = departed(tracers, source_patch[0], shifts[0])
    advected = from_patches(levels(spatial(patches, frac[0], frac[1]), frac[2]), band_rows, band_cols)
    first, k_wide = diffuse_first(advected, diffusivity)
    first_part = column_mass(first, weights)

    patches, frac = departed(first, source_patch[1], shifts[1])
    planar = spatial(patches, frac[0], frac[1])
    weight_z = cubic_matrix(frac[2], LEV)

    area_wide = column_area(lat_index * row_count - 1, row_count + 2, total_rows)
    flux = area_wide * k_wide
    g = weights - 2.0 * flux[1:-1] + flux[:-2] + flux[2:]
    g_cols = jnp.broadcast_to(g.reshape(band_rows, 1, 8, 1), (band_rows, band_cols, 8, 8))
    weighted = jnp.einsum(
        "pi,piv->pv", g_cols.reshape(per_device, 64), planar, precision=lax.Precision.HIGHEST
    ).reshape(per_device, LEV, per_level)
    mix_part = jnp.einsum(
        "plm,pmt->lmt", weight_z, weighted, precision=lax.Precision.HIGHEST
    )
    totals = all_sum(
        jnp.concatenate([target_part, first_part, mix_part.reshape(-1)]), ("lon", "lat")
    )
    parts = []
    for source_level in range(LEV):
        block = planar[:, :, source_level * per_level : (source_level + 1) * per_level]
        spread = jnp.concatenate(
            [weight_z[:, level, source_level][:, None, None] * block for level in range(LEV)],
            axis=2,
        )
        parts.append(from_patches(spread, band_rows, band_cols))
    spread_diffused = diffuse(jnp.stack(parts), diffusivity, 1)
    spread_diffused, totals = lax.optimization_barrier((spread_diffused, totals))
    target = totals[:value_count]
    first_mass = totals[value_count : 2 * value_count]
    mix = totals[2 * value_count :].reshape(LEV, LEV, per_level)
    first_ratio = (target / first_mass).reshape(LEV, per_level)
    second_mass = jnp.sum(first_ratio[None] * mix, axis=1).reshape(value_count)
    second_ratio = target / second_mass

    factor = jnp.tile(first_ratio, (1, LEV))
    combined = jnp.sum(factor[:, None, None, :] * spread_diffused, axis=0)
    return combined * second_ratio[None, None, :]


def solution(mesh):
    return jax.shard_map(
        local,
        mesh=mesh,
        in_specs=(
            P(("groups", "lat"), "lon", None),
            P("groups", None, None, None),
            P("lat"),
            P("groups", None, None),
        ),
        out_specs=P(("groups", "lat"), "lon", None),
        check_vma=False,
    )
```

```python
import math

import jax
import jax.numpy as jnp
from jax import lax
from jax.sharding import PartitionSpec as P

LEV = 4
STEPS = 2
CAP = 4


def all_sum(value, axes, rider=None):
    rider_done = None
    for axis in axes:
        count = lax.axis_size(axis)
        if count & (count - 1):
            value = lax.psum(value, axis)
            continue
        distance = 1
        while distance < count:
            value = value + lax.ppermute(
                value, axis, [(i, i ^ distance) for i in range(count)]
            )
            if rider is not None:
                value, rider = lax.optimization_barrier((value, rider))
                rider_done, rider = rider, None
            distance *= 2
    if rider_done is None and rider is None:
        return value
    return value, rider if rider_done is None else rider_done


def extended(cells, sides, width, closed):
    for axis, dim in sides:
        count = lax.axis_size(axis)
        ends = count if closed else count - 1
        head = lax.slice_in_dim(cells, 0, width, axis=dim)
        tail = lax.slice_in_dim(cells, cells.shape[dim] - width, cells.shape[dim], axis=dim)
        cells = jnp.concatenate(
            [
                lax.ppermute(tail, axis, [(i, (i + 1) % count) for i in range(ends)]),
                cells,
                lax.ppermute(head, axis, [((i + 1) % count, i) for i in range(ends)]),
            ],
            axis=dim,
        )
    return cells


def cubic_weights(fraction):
    first_term = -fraction * (fraction - 1.0) * (fraction - 2.0) / 6.0
    second_term = (fraction + 1.0) * (fraction - 1.0) * (fraction - 2.0) / 2.0
    third_term = -(fraction + 1.0) * fraction * (fraction - 2.0) / 2.0
    fourth_term = (fraction + 1.0) * fraction * (fraction - 1.0) / 6.0
    return (first_term, second_term, third_term, fourth_term)


def cubic_matrix(fraction, extent):
    places = jnp.arange(extent)
    running = jnp.zeros(fraction.shape + (extent, extent), jnp.float32)
    for offset, weight in zip(range(-1, 3), cubic_weights(fraction)):
        target_col = jnp.clip(places + offset, 0, extent - 1)
        indicator = (target_col[:, None] == places[None, :]).astype(jnp.float32)
        running = running + weight[..., None, None] * indicator
    return running


def tap_sources(target, extent):
    return sorted({min(max(target + offset, 0), extent - 1) for offset in range(-1, 3)})


def plane_weights(fraction_y, fraction_x):
    rows = lax.broadcasted_iota(jnp.int32, (1, 64, 64), 1)
    cols = lax.broadcasted_iota(jnp.int32, (1, 64, 64), 2)

    def along(fraction, source, target):
        running = jnp.zeros((fraction.shape[0], 64, 64), jnp.float32)
        for offset, weight in zip(range(-1, 3), cubic_weights(fraction)):
            indicator = (jnp.clip(source + offset, 0, 7) == target).astype(jnp.float32)
            running = running + weight[:, None, None] * indicator
        return running

    return along(fraction_y, rows // 8, cols // 8) * along(fraction_x, rows % 8, cols % 8)


def spatial(patches, fraction_y, fraction_x):
    return jnp.einsum(
        "nij,njv->niv",
        plane_weights(fraction_y, fraction_x),
        patches,
        precision=lax.Precision.HIGHEST,
    )


def levels(flat, fraction_z):
    value_count = flat.shape[2]
    per_level = value_count // LEV
    weight_z = cubic_matrix(fraction_z, LEV)
    blocks = [flat[:, :, m * per_level : (m + 1) * per_level] for m in range(LEV)]
    out = []
    for level in range(LEV):
        acc = None
        for m in tap_sources(level, LEV):
            term = weight_z[:, level, m][:, None, None] * blocks[m]
            acc = term if acc is None else acc + term
        out.append(acc)
    return jnp.concatenate(out, axis=2)


def to_patches(state_field):
    band_rows = state_field.shape[0] // 8
    band_cols = state_field.shape[1] // 8
    return (
        state_field.reshape(band_rows, 8, band_cols, 8, -1)
        .transpose(0, 2, 1, 3, 4)
        .reshape(band_rows * band_cols, 64, -1)
    )


def from_patches(patches, band_rows, band_cols):
    return (
        patches.reshape(band_rows, band_cols, 8, 8, -1)
        .transpose(0, 2, 1, 3, 4)
        .reshape(band_rows * 8, band_cols * 8, -1)
    )


def column_area(first_row, row_count, total_rows):
    latitude = ((first_row + jnp.arange(row_count)).astype(jnp.float32) + 0.5) * (
        math.pi / total_rows
    ) - 0.5 * math.pi
    return jnp.cos(latitude)


def column_mass(state_field, weights):
    return jnp.sum(weights[:, None, None] * state_field, axis=(0, 1))


def diffuse(advected, diffusivity, row_dim):
    col_dim = row_dim + 1
    rows = advected.shape[row_dim]
    cols = advected.shape[col_dim]
    lon_wide = extended(advected, (("lon", col_dim),), 1, True)
    lat_wide = extended(advected, (("lat", row_dim),), 1, False)
    laplace = (
        lax.slice_in_dim(lat_wide, 2, rows + 2, axis=row_dim)
        + lax.slice_in_dim(lat_wide, 0, rows, axis=row_dim)
        + lax.slice_in_dim(lon_wide, 2, cols + 2, axis=col_dim)
        + lax.slice_in_dim(lon_wide, 0, cols, axis=col_dim)
        - 4.0 * advected
    )
    k_shape = [1] * advected.ndim
    k_shape[row_dim] = rows
    return advected + diffusivity.reshape(k_shape) * laplace


def diffuse_first(advected, diffusivity):
    rows, cols, value_count = advected.shape
    count = lax.axis_size("lat")

    def pack(row, number):
        return jnp.concatenate(
            [row, jnp.broadcast_to(number, (1, 1, value_count))], axis=1
        )

    from_above = lax.ppermute(
        pack(advected[rows - 1 :], diffusivity[rows - 1]),
        "lat",
        [(i, i + 1) for i in range(count - 1)],
    )
    from_below = lax.ppermute(
        pack(advected[:1], diffusivity[0]), "lat", [(i + 1, i) for i in range(count - 1)]
    )
    lat_wide = jnp.concatenate([from_above[:, :cols], advected, from_below[:, :cols]], axis=0)
    k_wide = jnp.concatenate([from_above[0, cols, :1], diffusivity, from_below[0, cols, :1]])
    lon_wide = extended(advected, (("lon", 1),), 1, True)
    laplace = (
        lat_wide[2:] + lat_wide[:-2] + lon_wide[:, 2:] + lon_wide[:, :-2] - 4.0 * advected
    )
    return advected + diffusivity[:, None, None] * laplace, k_wide


def departed(state_field, source_ids, shifts_now):
    lat_count = lax.axis_size("lat")
    lat_index = lax.axis_index("lat")
    lon_index = lax.axis_index("lon")
    row_count, col_count, value_count = state_field.shape
    band_rows = row_count // 8
    band_cols = col_count // 8
    per_device = band_rows * band_cols
    total_cols = source_ids.shape[1]
    devices = jnp.arange(lat_count)
    slot_range = jnp.arange(CAP)
    column_ids = lax.dynamic_slice_in_dim(
        source_ids, lon_index * band_cols, band_cols, 1
    ).reshape(lat_count, per_device)
    fractions = lax.dynamic_slice_in_dim(
        shifts_now, lon_index * band_cols, band_cols, 2
    ).reshape(3, lat_count, per_device)
    source_row = column_ids // total_cols
    source_dev = source_row // band_rows
    source_local = (
        source_row % band_rows * band_cols + column_ids % total_cols - lon_index * band_cols
    )
    remote = source_dev != devices[:, None]
    matches = (source_dev[:, :, None] == devices[None, None, :]) & remote[:, :, None]
    slot_ranks = jnp.cumsum(matches.astype(jnp.int32), axis=1) - 1
    slot_of = jnp.sum(jnp.where(matches, slot_ranks, 0), axis=2)
    owned_here = remote & (source_dev == lat_index)
    sending = owned_here[:, :, None] & (slot_of[:, :, None] == slot_range[None, None, :])
    send_local = jnp.sum(jnp.where(sending, source_local[:, :, None], 0), axis=1)
    own_patches = to_patches(state_field)
    outgoing = own_patches[send_local.reshape(-1)].reshape(lat_count, CAP, 64, value_count)
    my_dev = lax.dynamic_index_in_dim(source_dev, lat_index, 0, keepdims=False)
    my_slot = lax.dynamic_index_in_dim(slot_of, lat_index, 0, keepdims=False)
    my_local = lax.dynamic_index_in_dim(source_local, lat_index, 0, keepdims=False)
    my_remote = lax.dynamic_index_in_dim(remote, lat_index, 0, keepdims=False)
    my_frac = lax.dynamic_index_in_dim(fractions, lat_index, 1, keepdims=False)
    arrived = lax.all_to_all(outgoing, "lat", 0, 0, tiled=True).reshape(
        lat_count * CAP, 64, value_count
    )
    pick_index = my_dev * CAP + my_slot
    patches = jnp.where(my_remote[:, None, None], arrived[pick_index], own_patches[my_local])
    return patches, my_frac


def local(tracers, shifts, diffusivity, source_patch):
    lat_count = lax.axis_size("lat")
    lat_index = lax.axis_index("lat")
    row_count, col_count, value_count = tracers.shape
    band_rows = row_count // 8
    band_cols = col_count // 8
    per_device = band_rows * band_cols
    per_level = value_count // LEV
    total_rows = row_count * lat_count
    weights = column_area(lat_index * row_count, row_count, total_rows)
    target_part = column_mass(tracers, weights)

    patches, frac = departed(tracers, source_patch[0], shifts[0])
    advected = from_patches(levels(spatial(patches, frac[0], frac[1]), frac[2]), band_rows, band_cols)
    first, k_wide = diffuse_first(advected, diffusivity)
    first_part = column_mass(first, weights)

    patches, frac = departed(first, source_patch[1], shifts[1])
    planar = spatial(patches, frac[0], frac[1])
    weight_z = cubic_matrix(frac[2], LEV)

    area_wide = column_area(lat_index * row_count - 1, row_count + 2, total_rows)
    flux = area_wide * k_wide
    g = weights - 2.0 * flux[1:-1] + flux[:-2] + flux[2:]
    g_cols = jnp.broadcast_to(g.reshape(band_rows, 1, 8, 1), (band_rows, band_cols, 8, 8))
    weighted = jnp.einsum(
        "pi,piv->pv", g_cols.reshape(per_device, 64), planar, precision=lax.Precision.HIGHEST
    ).reshape(per_device, LEV, per_level)
    mix_part = jnp.einsum(
        "plm,pmt->lmt", weight_z, weighted, precision=lax.Precision.HIGHEST
    )
    parts = []
    for source_level in range(LEV):
        block = planar[:, :, source_level * per_level : (source_level + 1) * per_level]
        spread = jnp.concatenate(
            [weight_z[:, level, source_level][:, None, None] * block for level in range(LEV)],
            axis=2,
        )
        parts.append(from_patches(spread, band_rows, band_cols))
    spread_diffused = diffuse(jnp.stack(parts), diffusivity, 1)
    totals, spread_diffused = all_sum(
        jnp.concatenate([target_part, first_part, mix_part.reshape(-1)]), ("lon", "lat"),
        spread_diffused,
    )
    target = totals[:value_count]
    first_mass = totals[value_count : 2 * value_count]
    mix = totals[2 * value_count :].reshape(LEV, LEV, per_level)
    first_ratio = (target / first_mass).reshape(LEV, per_level)
    second_mass = jnp.sum(first_ratio[None] * mix, axis=1).reshape(value_count)
    second_ratio = target / second_mass

    factor = jnp.tile(first_ratio, (1, LEV))
    combined = jnp.sum(factor[:, None, None, :] * spread_diffused, axis=0)
    return combined * second_ratio[None, None, :]


def solution(mesh):
    return jax.shard_map(
        local,
        mesh=mesh,
        in_specs=(
            P(("groups", "lat"), "lon", None),
            P("groups", None, None, None),
            P("lat"),
            P("groups", None, None),
        ),
        out_specs=P(("groups", "lat"), "lon", None),
        check_vma=False,
    )
```

```python
import math

import jax
import jax.numpy as jnp
from jax import lax
from jax.sharding import PartitionSpec as P

LEV = 4
STEPS = 2
CAP = 4


def all_sum(value, axes, rider=None):
    rider_done = None
    for axis in axes:
        count = lax.axis_size(axis)
        if count & (count - 1):
            value = lax.psum(value, axis)
            continue
        distance = 1
        while distance < count:
            value = value + lax.ppermute(
                value, axis, [(i, i ^ distance) for i in range(count)]
            )
            if rider is not None:
                value, rider = lax.optimization_barrier((value, rider))
                rider_done, rider = rider, None
            distance *= 2
    if rider_done is None and rider is None:
        return value
    return value, rider if rider_done is None else rider_done


def extended(cells, sides, width, closed):
    for axis, dim in sides:
        count = lax.axis_size(axis)
        ends = count if closed else count - 1
        head = lax.slice_in_dim(cells, 0, width, axis=dim)
        tail = lax.slice_in_dim(cells, cells.shape[dim] - width, cells.shape[dim], axis=dim)
        cells = jnp.concatenate(
            [
                lax.ppermute(tail, axis, [(i, (i + 1) % count) for i in range(ends)]),
                cells,
                lax.ppermute(head, axis, [((i + 1) % count, i) for i in range(ends)]),
            ],
            axis=dim,
        )
    return cells


def cubic_weights(fraction):
    first_term = -fraction * (fraction - 1.0) * (fraction - 2.0) / 6.0
    second_term = (fraction + 1.0) * (fraction - 1.0) * (fraction - 2.0) / 2.0
    third_term = -(fraction + 1.0) * fraction * (fraction - 2.0) / 2.0
    fourth_term = (fraction + 1.0) * fraction * (fraction - 1.0) / 6.0
    return (first_term, second_term, third_term, fourth_term)


def cubic_matrix(fraction, extent):
    places = jnp.arange(extent)
    running = jnp.zeros(fraction.shape + (extent, extent), jnp.float32)
    for offset, weight in zip(range(-1, 3), cubic_weights(fraction)):
        target_col = jnp.clip(places + offset, 0, extent - 1)
        indicator = (target_col[:, None] == places[None, :]).astype(jnp.float32)
        running = running + weight[..., None, None] * indicator
    return running


def tap_sources(target, extent):
    return sorted({min(max(target + offset, 0), extent - 1) for offset in range(-1, 3)})


def plane_weights(fraction_y, fraction_x):
    rows = lax.broadcasted_iota(jnp.int32, (1, 64, 64), 1)
    cols = lax.broadcasted_iota(jnp.int32, (1, 64, 64), 2)

    def along(fraction, source, target):
        running = jnp.zeros((fraction.shape[0], 64, 64), jnp.float32)
        for offset, weight in zip(range(-1, 3), cubic_weights(fraction)):
            indicator = (jnp.clip(source + offset, 0, 7) == target).astype(jnp.float32)
            running = running + weight[:, None, None] * indicator
        return running

    return along(fraction_y, rows // 8, cols // 8) * along(fraction_x, rows % 8, cols % 8)


def spatial(patches, fraction_y, fraction_x):
    return jnp.einsum(
        "nij,njv->niv",
        plane_weights(fraction_y, fraction_x),
        patches,
        precision=lax.Precision.HIGHEST,
    )


def levels(flat, fraction_z):
    value_count = flat.shape[2]
    per_level = value_count // LEV
    weight_z = cubic_matrix(fraction_z, LEV)
    blocks = [flat[:, :, m * per_level : (m + 1) * per_level] for m in range(LEV)]
    out = []
    for level in range(LEV):
        acc = None
        for m in tap_sources(level, LEV):
            term = weight_z[:, level, m][:, None, None] * blocks[m]
            acc = term if acc is None else acc + term
        out.append(acc)
    return jnp.concatenate(out, axis=2)


def to_patches(state_field):
    band_rows = state_field.shape[0] // 8
    band_cols = state_field.shape[1] // 8
    return (
        state_field.reshape(band_rows, 8, band_cols, 8, -1)
        .transpose(0, 2, 1, 3, 4)
        .reshape(band_rows * band_cols, 64, -1)
    )


def from_patches(patches, band_rows, band_cols):
    return (
        patches.reshape(band_rows, band_cols, 8, 8, -1)
        .transpose(0, 2, 1, 3, 4)
        .reshape(band_rows * 8, band_cols * 8, -1)
    )


def column_area(first_row, row_count, total_rows):
    latitude = ((first_row + jnp.arange(row_count)).astype(jnp.float32) + 0.5) * (
        math.pi / total_rows
    ) - 0.5 * math.pi
    return jnp.cos(latitude)


def column_mass(state_field, weights):
    return jnp.sum(weights[:, None, None] * state_field, axis=(0, 1))


def diffuse(advected, diffusivity, row_dim):
    col_dim = row_dim + 1
    rows = advected.shape[row_dim]
    cols = advected.shape[col_dim]
    lon_wide = extended(advected, (("lon", col_dim),), 1, True)
    lat_wide = extended(advected, (("lat", row_dim),), 1, False)
    laplace = (
        lax.slice_in_dim(lat_wide, 2, rows + 2, axis=row_dim)
        + lax.slice_in_dim(lat_wide, 0, rows, axis=row_dim)
        + lax.slice_in_dim(lon_wide, 2, cols + 2, axis=col_dim)
        + lax.slice_in_dim(lon_wide, 0, cols, axis=col_dim)
        - 4.0 * advected
    )
    k_shape = [1] * advected.ndim
    k_shape[row_dim] = rows
    return advected + diffusivity.reshape(k_shape) * laplace


def diffuse_first(advected, diffusivity):
    rows, cols, value_count = advected.shape
    count = lax.axis_size("lat")

    def pack(row, number):
        return jnp.concatenate(
            [row, jnp.broadcast_to(number, (1, 1, value_count))], axis=1
        )

    from_above = lax.ppermute(
        pack(advected[rows - 1 :], diffusivity[rows - 1]),
        "lat",
        [(i, i + 1) for i in range(count - 1)],
    )
    from_below = lax.ppermute(
        pack(advected[:1], diffusivity[0]), "lat", [(i + 1, i) for i in range(count - 1)]
    )
    lat_wide = jnp.concatenate([from_above[:, :cols], advected, from_below[:, :cols]], axis=0)
    k_wide = jnp.concatenate([from_above[0, cols, :1], diffusivity, from_below[0, cols, :1]])
    lon_wide = extended(advected, (("lon", 1),), 1, True)
    laplace = (
        lat_wide[2:] + lat_wide[:-2] + lon_wide[:, 2:] + lon_wide[:, :-2] - 4.0 * advected
    )
    return advected + diffusivity[:, None, None] * laplace, k_wide


def departed(state_field, source_ids, shifts_now):
    lat_count = lax.axis_size("lat")
    lat_index = lax.axis_index("lat")
    lon_index = lax.axis_index("lon")
    row_count, col_count, value_count = state_field.shape
    band_rows = row_count // 8
    band_cols = col_count // 8
    per_device = band_rows * band_cols
    total_cols = source_ids.shape[1]
    devices = jnp.arange(lat_count)
    slot_range = jnp.arange(CAP)
    column_ids = lax.dynamic_slice_in_dim(
        source_ids, lon_index * band_cols, band_cols, 1
    ).reshape(lat_count, per_device)
    fractions = lax.dynamic_slice_in_dim(
        shifts_now, lon_index * band_cols, band_cols, 2
    ).reshape(3, lat_count, per_device)
    source_row = column_ids // total_cols
    source_dev = source_row // band_rows
    source_local = (
        source_row % band_rows * band_cols + column_ids % total_cols - lon_index * band_cols
    )
    remote = source_dev != devices[:, None]
    matches = (source_dev[:, :, None] == devices[None, None, :]) & remote[:, :, None]
    slot_ranks = jnp.cumsum(matches.astype(jnp.int32), axis=1) - 1
    slot_of = jnp.sum(jnp.where(matches, slot_ranks, 0), axis=2)
    owned_here = remote & (source_dev == lat_index)
    sending = owned_here[:, :, None] & (slot_of[:, :, None] == slot_range[None, None, :])
    send_local = jnp.sum(jnp.where(sending, source_local[:, :, None], 0), axis=1)
    own_patches = to_patches(state_field)
    outgoing = own_patches[send_local.reshape(-1)].reshape(lat_count, CAP, 64, value_count)
    my_dev = lax.dynamic_index_in_dim(source_dev, lat_index, 0, keepdims=False)
    my_slot = lax.dynamic_index_in_dim(slot_of, lat_index, 0, keepdims=False)
    my_local = lax.dynamic_index_in_dim(source_local, lat_index, 0, keepdims=False)
    my_remote = lax.dynamic_index_in_dim(remote, lat_index, 0, keepdims=False)
    my_frac = lax.dynamic_index_in_dim(fractions, lat_index, 1, keepdims=False)
    arrived = lax.all_to_all(outgoing, "lat", 0, 0, tiled=True).reshape(
        lat_count * CAP, 64, value_count
    )
    pick_index = my_dev * CAP + my_slot
    patches = jnp.where(my_remote[:, None, None], arrived[pick_index], own_patches[my_local])
    return patches, my_frac


def local(tracers, shifts, diffusivity, source_patch):
    lat_count = lax.axis_size("lat")
    lat_index = lax.axis_index("lat")
    row_count, col_count, value_count = tracers.shape
    band_rows = row_count // 8
    band_cols = col_count // 8
    per_device = band_rows * band_cols
    per_level = value_count // LEV
    total_rows = row_count * lat_count
    weights = column_area(lat_index * row_count, row_count, total_rows)
    target_part = column_mass(tracers, weights)

    patches, frac = departed(tracers, source_patch[0], shifts[0])
    advected = from_patches(levels(spatial(patches, frac[0], frac[1]), frac[2]), band_rows, band_cols)
    first, k_wide = diffuse_first(advected, diffusivity)
    first_part = column_mass(first, weights)

    patches, frac = departed(first, source_patch[1], shifts[1])
    planar = spatial(patches, frac[0], frac[1])
    weight_z = cubic_matrix(frac[2], LEV)

    area_wide = column_area(lat_index * row_count - 1, row_count + 2, total_rows)
    flux = area_wide * k_wide
    g = weights - 2.0 * flux[1:-1] + flux[:-2] + flux[2:]
    g_cols = jnp.broadcast_to(g.reshape(band_rows, 1, 8, 1), (band_rows, band_cols, 8, 8))
    weighted = jnp.einsum(
        "pi,piv->pv", g_cols.reshape(per_device, 64), planar, precision=lax.Precision.HIGHEST
    ).reshape(per_device, LEV, per_level)
    mix_part = jnp.einsum(
        "plm,pmt->lmt", weight_z, weighted, precision=lax.Precision.HIGHEST
    )
    totals = all_sum(
        jnp.concatenate([target_part, first_part, mix_part.reshape(-1)]), ("lon", "lat")
    )
    target = totals[:value_count]
    first_mass = totals[value_count : 2 * value_count]
    mix = totals[2 * value_count :].reshape(LEV, LEV, per_level)
    first_ratio = target / first_mass
    second_mass = jnp.sum(first_ratio.reshape(LEV, per_level)[None] * mix, axis=1).reshape(
        value_count
    )
    second_ratio = target / second_mass
    advected = from_patches(
        levels(planar * first_ratio[None, None, :], frac[2]), band_rows, band_cols
    )
    return diffuse(advected, diffusivity, 0) * second_ratio[None, None, :]


def solution(mesh):
    return jax.shard_map(
        local,
        mesh=mesh,
        in_specs=(
            P(("groups", "lat"), "lon", None),
            P("groups", None, None, None),
            P("lat"),
            P("groups", None, None),
        ),
        out_specs=P(("groups", "lat"), "lon", None),
        check_vma=False,
    )
```

```python
import math

import jax
import jax.numpy as jnp
from jax import lax
from jax.sharding import PartitionSpec as P

LEV = 4
STEPS = 2
CAP = 4


def all_sum(value, axes, rider=None):
    rider_done = None
    for axis in axes:
        count = lax.axis_size(axis)
        if count & (count - 1):
            value = lax.psum(value, axis)
            continue
        distance = 1
        while distance < count:
            value = value + lax.ppermute(
                value, axis, [(i, i ^ distance) for i in range(count)]
            )
            if rider is not None:
                value, rider = lax.optimization_barrier((value, rider))
                rider_done, rider = rider, None
            distance *= 2
    if rider_done is None and rider is None:
        return value
    return value, rider if rider_done is None else rider_done


def extended(cells, sides, width, closed):
    for axis, dim in sides:
        count = lax.axis_size(axis)
        ends = count if closed else count - 1
        head = lax.slice_in_dim(cells, 0, width, axis=dim)
        tail = lax.slice_in_dim(cells, cells.shape[dim] - width, cells.shape[dim], axis=dim)
        cells = jnp.concatenate(
            [
                lax.ppermute(tail, axis, [(i, (i + 1) % count) for i in range(ends)]),
                cells,
                lax.ppermute(head, axis, [((i + 1) % count, i) for i in range(ends)]),
            ],
            axis=dim,
        )
    return cells


def cubic_weights(fraction):
    first_term = -fraction * (fraction - 1.0) * (fraction - 2.0) / 6.0
    second_term = (fraction + 1.0) * (fraction - 1.0) * (fraction - 2.0) / 2.0
    third_term = -(fraction + 1.0) * fraction * (fraction - 2.0) / 2.0
    fourth_term = (fraction + 1.0) * fraction * (fraction - 1.0) / 6.0
    return (first_term, second_term, third_term, fourth_term)


def cubic_matrix(fraction, extent):
    places = jnp.arange(extent)
    running = jnp.zeros(fraction.shape + (extent, extent), jnp.float32)
    for offset, weight in zip(range(-1, 3), cubic_weights(fraction)):
        target_col = jnp.clip(places + offset, 0, extent - 1)
        indicator = (target_col[:, None] == places[None, :]).astype(jnp.float32)
        running = running + weight[..., None, None] * indicator
    return running


def tap_sources(target, extent):
    return sorted({min(max(target + offset, 0), extent - 1) for offset in range(-1, 3)})


def plane_weights(fraction_y, fraction_x):
    rows = lax.broadcasted_iota(jnp.int32, (1, 64, 64), 1)
    cols = lax.broadcasted_iota(jnp.int32, (1, 64, 64), 2)

    def along(fraction, source, target):
        running = jnp.zeros((fraction.shape[0], 64, 64), jnp.float32)
        for offset, weight in zip(range(-1, 3), cubic_weights(fraction)):
            indicator = (jnp.clip(source + offset, 0, 7) == target).astype(jnp.float32)
            running = running + weight[:, None, None] * indicator
        return running

    return along(fraction_y, rows // 8, cols // 8) * along(fraction_x, rows % 8, cols % 8)


def spatial(patches, fraction_y, fraction_x):
    return jnp.einsum(
        "nij,njv->niv",
        plane_weights(fraction_y, fraction_x),
        patches,
        precision=lax.Precision.HIGHEST,
    )


def levels(flat, fraction_z):
    value_count = flat.shape[2]
    per_level = value_count // LEV
    weight_z = cubic_matrix(fraction_z, LEV)
    blocks = [flat[:, :, m * per_level : (m + 1) * per_level] for m in range(LEV)]
    out = []
    for level in range(LEV):
        acc = None
        for m in tap_sources(level, LEV):
            term = weight_z[:, level, m][:, None, None] * blocks[m]
            acc = term if acc is None else acc + term
        out.append(acc)
    return jnp.concatenate(out, axis=2)


def to_patches(state_field):
    band_rows = state_field.shape[0] // 8
    band_cols = state_field.shape[1] // 8
    return (
        state_field.reshape(band_rows, 8, band_cols, 8, -1)
        .transpose(0, 2, 1, 3, 4)
        .reshape(band_rows * band_cols, 64, -1)
    )


def from_patches(patches, band_rows, band_cols):
    return (
        patches.reshape(band_rows, band_cols, 8, 8, -1)
        .transpose(0, 2, 1, 3, 4)
        .reshape(band_rows * 8, band_cols * 8, -1)
    )


def column_area(first_row, row_count, total_rows):
    latitude = ((first_row + jnp.arange(row_count)).astype(jnp.float32) + 0.5) * (
        math.pi / total_rows
    ) - 0.5 * math.pi
    return jnp.cos(latitude)


def column_mass(state_field, weights):
    return jnp.sum(weights[:, None, None] * state_field, axis=(0, 1))


def diffuse(advected, diffusivity, row_dim):
    col_dim = row_dim + 1
    rows = advected.shape[row_dim]
    cols = advected.shape[col_dim]
    lon_wide = extended(advected, (("lon", col_dim),), 1, True)
    lat_wide = extended(advected, (("lat", row_dim),), 1, False)
    laplace = (
        lax.slice_in_dim(lat_wide, 2, rows + 2, axis=row_dim)
        + lax.slice_in_dim(lat_wide, 0, rows, axis=row_dim)
        + lax.slice_in_dim(lon_wide, 2, cols + 2, axis=col_dim)
        + lax.slice_in_dim(lon_wide, 0, cols, axis=col_dim)
        - 4.0 * advected
    )
    k_shape = [1] * advected.ndim
    k_shape[row_dim] = rows
    return advected + diffusivity.reshape(k_shape) * laplace


def diffuse_first(advected, diffusivity):
    rows, cols, value_count = advected.shape
    count = lax.axis_size("lat")

    def pack(row, number):
        return jnp.concatenate(
            [row, jnp.broadcast_to(number, (1, 1, value_count))], axis=1
        )

    from_above = lax.ppermute(
        pack(advected[rows - 1 :], diffusivity[rows - 1]),
        "lat",
        [(i, i + 1) for i in range(count - 1)],
    )
    from_below = lax.ppermute(
        pack(advected[:1], diffusivity[0]), "lat", [(i + 1, i) for i in range(count - 1)]
    )
    lat_wide = jnp.concatenate([from_above[:, :cols], advected, from_below[:, :cols]], axis=0)
    k_wide = jnp.concatenate([from_above[0, cols, :1], diffusivity, from_below[0, cols, :1]])
    lon_wide = extended(advected, (("lon", 1),), 1, True)
    laplace = (
        lat_wide[2:] + lat_wide[:-2] + lon_wide[:, 2:] + lon_wide[:, :-2] - 4.0 * advected
    )
    return advected + diffusivity[:, None, None] * laplace, k_wide


def departed(state_field, source_ids, shifts_now):
    lat_count = lax.axis_size("lat")
    lat_index = lax.axis_index("lat")
    lon_index = lax.axis_index("lon")
    row_count, col_count, value_count = state_field.shape
    band_rows = row_count // 8
    band_cols = col_count // 8
    per_device = band_rows * band_cols
    total_cols = source_ids.shape[1]
    devices = jnp.arange(lat_count)
    slot_range = jnp.arange(CAP)
    column_ids = lax.dynamic_slice_in_dim(
        source_ids, lon_index * band_cols, band_cols, 1
    ).reshape(lat_count, per_device)
    fractions = lax.dynamic_slice_in_dim(
        shifts_now, lon_index * band_cols, band_cols, 2
    ).reshape(3, lat_count, per_device)
    source_row = column_ids // total_cols
    source_dev = source_row // band_rows
    source_local = (
        source_row % band_rows * band_cols + column_ids % total_cols - lon_index * band_cols
    )
    remote = source_dev != devices[:, None]
    matches = (source_dev[:, :, None] == devices[None, None, :]) & remote[:, :, None]
    slot_ranks = jnp.cumsum(matches.astype(jnp.int32), axis=1) - 1
    slot_of = jnp.sum(jnp.where(matches, slot_ranks, 0), axis=2)
    owned_here = remote & (source_dev == lat_index)
    sending = owned_here[:, :, None] & (slot_of[:, :, None] == slot_range[None, None, :])
    send_local = jnp.sum(jnp.where(sending, source_local[:, :, None], 0), axis=1)
    own_patches = to_patches(state_field)
    outgoing = own_patches[send_local.reshape(-1)].reshape(lat_count, CAP, 64, value_count)
    my_dev = lax.dynamic_index_in_dim(source_dev, lat_index, 0, keepdims=False)
    my_slot = lax.dynamic_index_in_dim(slot_of, lat_index, 0, keepdims=False)
    my_local = lax.dynamic_index_in_dim(source_local, lat_index, 0, keepdims=False)
    my_remote = lax.dynamic_index_in_dim(remote, lat_index, 0, keepdims=False)
    my_frac = lax.dynamic_index_in_dim(fractions, lat_index, 1, keepdims=False)
    arrived = lax.all_to_all(outgoing, "lat", 0, 0, tiled=True).reshape(
        lat_count * CAP, 64, value_count
    )
    pick_index = my_dev * CAP + my_slot
    slot_owner = (pick_index[None, :] == jnp.arange(lat_count * CAP)[:, None]) & my_remote[None, :]
    slot_frac = jnp.sum(jnp.where(slot_owner[None], my_frac[:, None, :], 0.0), axis=2)
    return own_patches[my_local], my_frac, arrived, slot_frac, pick_index, my_remote


def gathered_spatial(state_field, source_ids, shifts_now):
    near, frac, arrived, slot_frac, pick_index, remote = departed(
        state_field, source_ids, shifts_now
    )
    near_done = spatial(near, frac[0], frac[1])
    arrived_done = spatial(arrived, slot_frac[0], slot_frac[1])
    return near_done, frac, arrived_done, slot_frac, pick_index, remote


def local(tracers, shifts, diffusivity, source_patch):
    lat_count = lax.axis_size("lat")
    lat_index = lax.axis_index("lat")
    row_count, col_count, value_count = tracers.shape
    band_rows = row_count // 8
    band_cols = col_count // 8
    per_device = band_rows * band_cols
    per_level = value_count // LEV
    total_rows = row_count * lat_count
    weights = column_area(lat_index * row_count, row_count, total_rows)
    target_part = column_mass(tracers, weights)

    near, frac, arrived, slot_frac, pick_index, remote = gathered_spatial(
        tracers, source_patch[0], shifts[0]
    )
    finished = jnp.where(
        remote[:, None, None],
        levels(arrived, slot_frac[2])[pick_index],
        levels(near, frac[2]),
    )
    advected = from_patches(finished, band_rows, band_cols)
    first, k_wide = diffuse_first(advected, diffusivity)
    first_part = column_mass(first, weights)

    near, frac, arrived, _, pick_index, remote = gathered_spatial(
        first, source_patch[1], shifts[1]
    )
    planar = jnp.where(remote[:, None, None], arrived[pick_index], near)
    weight_z = cubic_matrix(frac[2], LEV)

    area_wide = column_area(lat_index * row_count - 1, row_count + 2, total_rows)
    flux = area_wide * k_wide
    g = weights - 2.0 * flux[1:-1] + flux[:-2] + flux[2:]
    g_cols = jnp.broadcast_to(g.reshape(band_rows, 1, 8, 1), (band_rows, band_cols, 8, 8))
    weighted = jnp.einsum(
        "pi,piv->pv", g_cols.reshape(per_device, 64), planar, precision=lax.Precision.HIGHEST
    ).reshape(per_device, LEV, per_level)
    mix_part = jnp.einsum(
        "plm,pmt->lmt", weight_z, weighted, precision=lax.Precision.HIGHEST
    )
    totals = all_sum(
        jnp.concatenate([target_part, first_part, mix_part.reshape(-1)]), ("lon", "lat")
    )
    target = totals[:value_count]
    first_mass = totals[value_count : 2 * value_count]
    mix = totals[2 * value_count :].reshape(LEV, LEV, per_level)
    first_ratio = target / first_mass
    second_mass = jnp.sum(first_ratio.reshape(LEV, per_level)[None] * mix, axis=1).reshape(
        value_count
    )
    second_ratio = target / second_mass
    advected = from_patches(
        levels(planar * first_ratio[None, None, :], frac[2]), band_rows, band_cols
    )
    return diffuse(advected, diffusivity, 0) * second_ratio[None, None, :]


def solution(mesh):
    return jax.shard_map(
        local,
        mesh=mesh,
        in_specs=(
            P(("groups", "lat"), "lon", None),
            P("groups", None, None, None),
            P("lat"),
            P("groups", None, None),
        ),
        out_specs=P(("groups", "lat"), "lon", None),
        check_vma=False,
    )
```

```python
import math

import jax
import jax.numpy as jnp
from jax import lax
from jax.sharding import PartitionSpec as P

LEV = 4
STEPS = 2
CAP = 4


def all_sum(value, axes, rider=None):
    rider_done = None
    for axis in axes:
        count = lax.axis_size(axis)
        if count & (count - 1):
            value = lax.psum(value, axis)
            continue
        distance = 1
        while distance < count:
            value = value + lax.ppermute(
                value, axis, [(i, i ^ distance) for i in range(count)]
            )
            if rider is not None:
                value, rider = lax.optimization_barrier((value, rider))
                rider_done, rider = rider, None
            distance *= 2
    if rider_done is None and rider is None:
        return value
    return value, rider if rider_done is None else rider_done


def extended(cells, sides, width, closed):
    for axis, dim in sides:
        count = lax.axis_size(axis)
        ends = count if closed else count - 1
        head = lax.slice_in_dim(cells, 0, width, axis=dim)
        tail = lax.slice_in_dim(cells, cells.shape[dim] - width, cells.shape[dim], axis=dim)
        cells = jnp.concatenate(
            [
                lax.ppermute(tail, axis, [(i, (i + 1) % count) for i in range(ends)]),
                cells,
                lax.ppermute(head, axis, [((i + 1) % count, i) for i in range(ends)]),
            ],
            axis=dim,
        )
    return cells


def cubic_weights(fraction):
    first_term = -fraction * (fraction - 1.0) * (fraction - 2.0) / 6.0
    second_term = (fraction + 1.0) * (fraction - 1.0) * (fraction - 2.0) / 2.0
    third_term = -(fraction + 1.0) * fraction * (fraction - 2.0) / 2.0
    fourth_term = (fraction + 1.0) * fraction * (fraction - 1.0) / 6.0
    return (first_term, second_term, third_term, fourth_term)


def cubic_matrix(fraction, extent):
    places = jnp.arange(extent)
    running = jnp.zeros(fraction.shape + (extent, extent), jnp.float32)
    for offset, weight in zip(range(-1, 3), cubic_weights(fraction)):
        target_col = jnp.clip(places + offset, 0, extent - 1)
        indicator = (target_col[:, None] == places[None, :]).astype(jnp.float32)
        running = running + weight[..., None, None] * indicator
    return running


def tap_sources(target, extent):
    return sorted({min(max(target + offset, 0), extent - 1) for offset in range(-1, 3)})


def plane_weights(fraction_y, fraction_x):
    rows = lax.broadcasted_iota(jnp.int32, (1, 64, 64), 1)
    cols = lax.broadcasted_iota(jnp.int32, (1, 64, 64), 2)

    def along(fraction, source, target):
        running = jnp.zeros((fraction.shape[0], 64, 64), jnp.float32)
        for offset, weight in zip(range(-1, 3), cubic_weights(fraction)):
            indicator = (jnp.clip(source + offset, 0, 7) == target).astype(jnp.float32)
            running = running + weight[:, None, None] * indicator
        return running

    return along(fraction_y, rows // 8, cols // 8) * along(fraction_x, rows % 8, cols % 8)


def spatial(patches, fraction_y, fraction_x):
    return jnp.einsum(
        "nij,njv->niv",
        plane_weights(fraction_y, fraction_x),
        patches,
        precision=lax.Precision.HIGHEST,
    )


def levels(flat, fraction_z):
    value_count = flat.shape[2]
    per_level = value_count // LEV
    weight_z = cubic_matrix(fraction_z, LEV)
    blocks = [flat[:, :, m * per_level : (m + 1) * per_level] for m in range(LEV)]
    out = []
    for level in range(LEV):
        acc = None
        for m in tap_sources(level, LEV):
            term = weight_z[:, level, m][:, None, None] * blocks[m]
            acc = term if acc is None else acc + term
        out.append(acc)
    return jnp.concatenate(out, axis=2)


def to_patches(state_field):
    band_rows = state_field.shape[0] // 8
    band_cols = state_field.shape[1] // 8
    return (
        state_field.reshape(band_rows, 8, band_cols, 8, -1)
        .transpose(0, 2, 1, 3, 4)
        .reshape(band_rows * band_cols, 64, -1)
    )


def from_patches(patches, band_rows, band_cols):
    return (
        patches.reshape(band_rows, band_cols, 8, 8, -1)
        .transpose(0, 2, 1, 3, 4)
        .reshape(band_rows * 8, band_cols * 8, -1)
    )


def column_area(first_row, row_count, total_rows):
    latitude = ((first_row + jnp.arange(row_count)).astype(jnp.float32) + 0.5) * (
        math.pi / total_rows
    ) - 0.5 * math.pi
    return jnp.cos(latitude)


def column_mass(state_field, weights):
    return jnp.sum(weights[:, None, None] * state_field, axis=(0, 1))


def diffuse(advected, diffusivity, row_dim):
    col_dim = row_dim + 1
    rows = advected.shape[row_dim]
    cols = advected.shape[col_dim]
    lon_wide = extended(advected, (("lon", col_dim),), 1, True)
    lat_wide = extended(advected, (("lat", row_dim),), 1, False)
    laplace = (
        lax.slice_in_dim(lat_wide, 2, rows + 2, axis=row_dim)
        + lax.slice_in_dim(lat_wide, 0, rows, axis=row_dim)
        + lax.slice_in_dim(lon_wide, 2, cols + 2, axis=col_dim)
        + lax.slice_in_dim(lon_wide, 0, cols, axis=col_dim)
        - 4.0 * advected
    )
    k_shape = [1] * advected.ndim
    k_shape[row_dim] = rows
    return advected + diffusivity.reshape(k_shape) * laplace


def levels_cols(values, weight_z):
    value_count = values.shape[-1]
    per_level = value_count // LEV
    blocks = [values[..., m * per_level : (m + 1) * per_level] for m in range(LEV)]
    out = []
    for level in range(LEV):
        acc = None
        for m in tap_sources(level, LEV):
            term = weight_z[..., level, m][..., None] * blocks[m]
            acc = term if acc is None else acc + term
        out.append(acc)
    return jnp.concatenate(out, axis=-1)


def halos(field):
    lat_count = lax.axis_size("lat")
    lon_count = lax.axis_size("lon")
    rows, cols = field.shape[0], field.shape[1]
    above = lax.ppermute(field[rows - 1 :], "lat", [(i, i + 1) for i in range(lat_count - 1)])
    below = lax.ppermute(field[:1], "lat", [(i + 1, i) for i in range(lat_count - 1)])
    left = lax.ppermute(
        field[:, cols - 1 :], "lon", [(i, (i + 1) % lon_count) for i in range(lon_count)]
    )
    right = lax.ppermute(
        field[:, :1], "lon", [((i + 1) % lon_count, i) for i in range(lon_count)]
    )
    return above, below, left, right


def diffuse_first(advected, diffusivity):
    rows, cols, value_count = advected.shape
    count = lax.axis_size("lat")

    def pack(row, number):
        return jnp.concatenate(
            [row, jnp.broadcast_to(number, (1, 1, value_count))], axis=1
        )

    from_above = lax.ppermute(
        pack(advected[rows - 1 :], diffusivity[rows - 1]),
        "lat",
        [(i, i + 1) for i in range(count - 1)],
    )
    from_below = lax.ppermute(
        pack(advected[:1], diffusivity[0]), "lat", [(i + 1, i) for i in range(count - 1)]
    )
    lat_wide = jnp.concatenate([from_above[:, :cols], advected, from_below[:, :cols]], axis=0)
    k_wide = jnp.concatenate([from_above[0, cols, :1], diffusivity, from_below[0, cols, :1]])
    lon_wide = extended(advected, (("lon", 1),), 1, True)
    laplace = (
        lat_wide[2:] + lat_wide[:-2] + lon_wide[:, 2:] + lon_wide[:, :-2] - 4.0 * advected
    )
    return advected + diffusivity[:, None, None] * laplace, k_wide


def departed(state_field, source_ids, shifts_now):
    lat_count = lax.axis_size("lat")
    lat_index = lax.axis_index("lat")
    lon_index = lax.axis_index("lon")
    row_count, col_count, value_count = state_field.shape
    band_rows = row_count // 8
    band_cols = col_count // 8
    per_device = band_rows * band_cols
    total_cols = source_ids.shape[1]
    devices = jnp.arange(lat_count)
    slot_range = jnp.arange(CAP)
    column_ids = lax.dynamic_slice_in_dim(
        source_ids, lon_index * band_cols, band_cols, 1
    ).reshape(lat_count, per_device)
    fractions = lax.dynamic_slice_in_dim(
        shifts_now, lon_index * band_cols, band_cols, 2
    ).reshape(3, lat_count, per_device)
    source_row = column_ids // total_cols
    source_dev = source_row // band_rows
    source_local = (
        source_row % band_rows * band_cols + column_ids % total_cols - lon_index * band_cols
    )
    remote = source_dev != devices[:, None]
    matches = (source_dev[:, :, None] == devices[None, None, :]) & remote[:, :, None]
    slot_ranks = jnp.cumsum(matches.astype(jnp.int32), axis=1) - 1
    slot_of = jnp.sum(jnp.where(matches, slot_ranks, 0), axis=2)
    owned_here = remote & (source_dev == lat_index)
    sending = owned_here[:, :, None] & (slot_of[:, :, None] == slot_range[None, None, :])
    send_local = jnp.sum(jnp.where(sending, source_local[:, :, None], 0), axis=1)
    own_patches = to_patches(state_field)
    outgoing = own_patches[send_local.reshape(-1)].reshape(lat_count, CAP, 64, value_count)
    my_dev = lax.dynamic_index_in_dim(source_dev, lat_index, 0, keepdims=False)
    my_slot = lax.dynamic_index_in_dim(slot_of, lat_index, 0, keepdims=False)
    my_local = lax.dynamic_index_in_dim(source_local, lat_index, 0, keepdims=False)
    my_remote = lax.dynamic_index_in_dim(remote, lat_index, 0, keepdims=False)
    my_frac = lax.dynamic_index_in_dim(fractions, lat_index, 1, keepdims=False)
    arrived = lax.all_to_all(outgoing, "lat", 0, 0, tiled=True).reshape(
        lat_count * CAP, 64, value_count
    )
    pick_index = my_dev * CAP + my_slot
    patches = jnp.where(my_remote[:, None, None], arrived[pick_index], own_patches[my_local])
    return patches, my_frac


def local(tracers, shifts, diffusivity, source_patch):
    lat_count = lax.axis_size("lat")
    lat_index = lax.axis_index("lat")
    row_count, col_count, value_count = tracers.shape
    band_rows = row_count // 8
    band_cols = col_count // 8
    per_device = band_rows * band_cols
    per_level = value_count // LEV
    total_rows = row_count * lat_count
    weights = column_area(lat_index * row_count, row_count, total_rows)
    target_part = column_mass(tracers, weights)

    patches, frac = departed(tracers, source_patch[0], shifts[0])
    advected = from_patches(levels(spatial(patches, frac[0], frac[1]), frac[2]), band_rows, band_cols)
    first, k_wide = diffuse_first(advected, diffusivity)
    first_part = column_mass(first, weights)

    patches, frac = departed(first, source_patch[1], shifts[1])
    planar = spatial(patches, frac[0], frac[1])
    weight_z = cubic_matrix(frac[2], LEV)

    area_wide = column_area(lat_index * row_count - 1, row_count + 2, total_rows)
    flux = area_wide * k_wide
    g = weights - 2.0 * flux[1:-1] + flux[:-2] + flux[2:]
    g_cols = jnp.broadcast_to(g.reshape(band_rows, 1, 8, 1), (band_rows, band_cols, 8, 8))
    weighted = jnp.einsum(
        "pi,piv->pv", g_cols.reshape(per_device, 64), planar, precision=lax.Precision.HIGHEST
    ).reshape(per_device, LEV, per_level)
    mix_part = jnp.einsum(
        "plm,pmt->lmt", weight_z, weighted, precision=lax.Precision.HIGHEST
    )
    field_planar = from_patches(planar, band_rows, band_cols)
    above, below, left, right = halos(field_planar)
    lon_index = lax.axis_index("lon")
    fraction_z = shifts[1, 2]
    patch_rows, patch_cols = fraction_z.shape
    first_row = lat_index * band_rows
    first_col = lon_index * band_cols
    tile_cols = (first_col + jnp.arange(band_cols)) % patch_cols
    band_patch_rows = first_row + jnp.arange(band_rows)
    row_above = jnp.clip(first_row - 1, 0, patch_rows - 1)
    row_below = jnp.clip(first_row + band_rows, 0, patch_rows - 1)
    col_left = (first_col - 1) % patch_cols
    col_right = (first_col + band_cols) % patch_cols
    cz_own = cubic_matrix(fraction_z[band_patch_rows][:, tile_cols], LEV)
    cz_above = jnp.repeat(cubic_matrix(fraction_z[row_above, tile_cols], LEV), 8, axis=0)[None]
    cz_below = jnp.repeat(cubic_matrix(fraction_z[row_below, tile_cols], LEV), 8, axis=0)[None]
    cz_left = jnp.repeat(cubic_matrix(fraction_z[band_patch_rows, col_left], LEV), 8, axis=0)[
        :, None
    ]
    cz_right = jnp.repeat(cubic_matrix(fraction_z[band_patch_rows, col_right], LEV), 8, axis=0)[
        :, None
    ]
    totals = all_sum(
        jnp.concatenate([target_part, first_part, mix_part.reshape(-1)]), ("lon", "lat")
    )
    target = totals[:value_count]
    first_mass = totals[value_count : 2 * value_count]
    mix = totals[2 * value_count :].reshape(LEV, LEV, per_level)
    first_ratio = target / first_mass
    second_mass = jnp.sum(first_ratio.reshape(LEV, per_level)[None] * mix, axis=1).reshape(
        value_count
    )
    second_ratio = target / second_mass
    mixed = levels_cols(
        (field_planar * first_ratio).reshape(band_rows, 8, band_cols, 8, value_count),
        cz_own[:, None, :, None],
    ).reshape(row_count, col_count, value_count)
    above = levels_cols(above * first_ratio, cz_above)
    below = levels_cols(below * first_ratio, cz_below)
    left = levels_cols(left * first_ratio, cz_left)
    right = levels_cols(right * first_ratio, cz_right)
    lat_wide = jnp.concatenate([above, mixed, below], axis=0)
    lon_wide = jnp.concatenate([left, mixed, right], axis=1)
    laplace = lat_wide[2:] + lat_wide[:-2] + lon_wide[:, 2:] + lon_wide[:, :-2] - 4.0 * mixed
    second = mixed + diffusivity[:, None, None] * laplace
    return second * second_ratio[None, None, :]


def solution(mesh):
    return jax.shard_map(
        local,
        mesh=mesh,
        in_specs=(
            P(("groups", "lat"), "lon", None),
            P("groups", None, None, None),
            P("lat"),
            P("groups", None, None),
        ),
        out_specs=P(("groups", "lat"), "lon", None),
        check_vma=False,
    )
```

```python
import functools
import math

import jax
import jax.numpy as jnp
from jax import lax
from jax.experimental import pallas as pl
from jax.experimental.pallas import tpu as pltpu
from jax.sharding import PartitionSpec as P

LEV = 4
STEPS = 2
CAP = 4


def all_sum(value, axes, rider=None):
    rider_done = None
    for axis in axes:
        count = lax.axis_size(axis)
        if count & (count - 1):
            value = lax.psum(value, axis)
            continue
        distance = 1
        while distance < count:
            value = value + lax.ppermute(
                value, axis, [(i, i ^ distance) for i in range(count)]
            )
            if rider is not None:
                value, rider = lax.optimization_barrier((value, rider))
                rider_done, rider = rider, None
            distance *= 2
    if rider_done is None and rider is None:
        return value
    return value, rider if rider_done is None else rider_done


def extended(cells, sides, width, closed):
    for axis, dim in sides:
        count = lax.axis_size(axis)
        ends = count if closed else count - 1
        head = lax.slice_in_dim(cells, 0, width, axis=dim)
        tail = lax.slice_in_dim(cells, cells.shape[dim] - width, cells.shape[dim], axis=dim)
        cells = jnp.concatenate(
            [
                lax.ppermute(tail, axis, [(i, (i + 1) % count) for i in range(ends)]),
                cells,
                lax.ppermute(head, axis, [((i + 1) % count, i) for i in range(ends)]),
            ],
            axis=dim,
        )
    return cells


def cubic_weights(fraction):
    first_term = -fraction * (fraction - 1.0) * (fraction - 2.0) / 6.0
    second_term = (fraction + 1.0) * (fraction - 1.0) * (fraction - 2.0) / 2.0
    third_term = -(fraction + 1.0) * fraction * (fraction - 2.0) / 2.0
    fourth_term = (fraction + 1.0) * fraction * (fraction - 1.0) / 6.0
    return (first_term, second_term, third_term, fourth_term)


def cubic_matrix(fraction, extent):
    places = jnp.arange(extent)
    running = jnp.zeros(fraction.shape + (extent, extent), jnp.float32)
    for offset, weight in zip(range(-1, 3), cubic_weights(fraction)):
        target_col = jnp.clip(places + offset, 0, extent - 1)
        indicator = (target_col[:, None] == places[None, :]).astype(jnp.float32)
        running = running + weight[..., None, None] * indicator
    return running


def tap_sources(target, extent):
    return sorted({min(max(target + offset, 0), extent - 1) for offset in range(-1, 3)})


def plane_weights(fraction_y, fraction_x):
    rows = lax.broadcasted_iota(jnp.int32, (1, 64, 64), 1)
    cols = lax.broadcasted_iota(jnp.int32, (1, 64, 64), 2)

    def along(fraction, source, target):
        running = jnp.zeros((fraction.shape[0], 64, 64), jnp.float32)
        for offset, weight in zip(range(-1, 3), cubic_weights(fraction)):
            indicator = (jnp.clip(source + offset, 0, 7) == target).astype(jnp.float32)
            running = running + weight[:, None, None] * indicator
        return running

    return along(fraction_y, rows // 8, cols // 8) * along(fraction_x, rows % 8, cols % 8)


def spatial(patches, fraction_y, fraction_x):
    return jnp.einsum(
        "nij,njv->niv",
        plane_weights(fraction_y, fraction_x),
        patches,
        precision=lax.Precision.HIGHEST,
    )


def levels(flat, fraction_z):
    value_count = flat.shape[2]
    per_level = value_count // LEV
    weight_z = cubic_matrix(fraction_z, LEV)
    blocks = [flat[:, :, m * per_level : (m + 1) * per_level] for m in range(LEV)]
    out = []
    for level in range(LEV):
        acc = None
        for m in tap_sources(level, LEV):
            term = weight_z[:, level, m][:, None, None] * blocks[m]
            acc = term if acc is None else acc + term
        out.append(acc)
    return jnp.concatenate(out, axis=2)


def level_rolls(fraction_z, value_count):
    weight_z = cubic_matrix(fraction_z, LEV)
    per_level = value_count // LEV
    rows = []
    for d in (-1, 0, 1, 2):
        picked = [
            weight_z[:, level, level + d] if 0 <= level + d < LEV else jnp.zeros_like(fraction_z)
            for level in range(LEV)
        ]
        rows.append(jnp.repeat(jnp.stack(picked, axis=1), per_level, axis=1))
    return jnp.stack(rows, axis=1)


def _interp_kernel(local_ref, pick_ref, remote_ref, field_ref, arr_ref, pw_ref, *rest, band_cols):
    out_ref = rest[-1]
    coef_ref = rest[0] if len(rest) == 2 else None
    value_count = field_ref.shape[2]
    per_level = value_count // LEV

    def body(q, carry):
        source = local_ref[q]
        src_row = pl.multiple_of((source // band_cols) * 8, 8)
        src_col = pl.multiple_of((source % band_cols) * 8, 8)
        own = field_ref[pl.ds(src_row, 8), pl.ds(src_col, 8), :].reshape(64, value_count)
        got = arr_ref[pick_ref[q]]
        patch = jnp.where(remote_ref[q] != 0, got, own)
        out = jnp.dot(
            pw_ref[q], patch, precision=lax.Precision.HIGHEST, preferred_element_type=jnp.float32
        )
        if coef_ref is not None:
            coef = coef_ref[q]
            mixed = coef[1:2, :] * out
            for row, d in ((0, -1), (2, 1), (3, 2)):
                rolled = pltpu.roll(out, (-d * per_level) % value_count, 1)
                mixed = mixed + coef[row : row + 1, :] * rolled
            out = mixed
        dst_row = pl.multiple_of((q // band_cols) * 8, 8)
        dst_col = pl.multiple_of((q % band_cols) * 8, 8)
        out_ref[pl.ds(dst_row, 8), pl.ds(dst_col, 8), :] = out.reshape(8, 8, value_count)
        return carry

    lax.fori_loop(0, local_ref.shape[0], body, 0)


def interpolate_into_field(local, pick, remote, field, arrived, plane, coef=None):
    rows, cols, value_count = field.shape
    smem = pl.BlockSpec(memory_space=pltpu.SMEM)
    vmem = pl.BlockSpec(memory_space=pltpu.VMEM)
    operands = [local, pick, remote, field, arrived, plane] + ([] if coef is None else [coef])
    patch_count = local.shape[0]
    return pl.pallas_call(
        functools.partial(_interp_kernel, band_cols=cols // 8),
        out_shape=jax.ShapeDtypeStruct(field.shape, jnp.float32),
        in_specs=[smem] * 3 + [vmem] * (len(operands) - 3),
        out_specs=vmem,
        cost_estimate=pl.CostEstimate(
            flops=patch_count * 2 * 64 * 64 * value_count * 6,
            bytes_accessed=4 * (2 * field.size + arrived.size + plane.size),
            transcendentals=0,
        ),
    )(*operands)


def _gather_kernel(index_ref, field_ref, out_ref, *, band_cols):
    value_count = field_ref.shape[2]

    def body(s, carry):
        source = index_ref[s]
        src_row = pl.multiple_of((source // band_cols) * 8, 8)
        src_col = pl.multiple_of((source % band_cols) * 8, 8)
        out_ref[s] = field_ref[pl.ds(src_row, 8), pl.ds(src_col, 8), :].reshape(64, value_count)
        return carry

    lax.fori_loop(0, index_ref.shape[0], body, 0)


def gather_patches(index, field):
    rows, cols, value_count = field.shape
    return pl.pallas_call(
        functools.partial(_gather_kernel, band_cols=cols // 8),
        out_shape=jax.ShapeDtypeStruct((index.shape[0], 64, value_count), jnp.float32),
        in_specs=[pl.BlockSpec(memory_space=pltpu.SMEM), pl.BlockSpec(memory_space=pltpu.VMEM)],
        out_specs=pl.BlockSpec(memory_space=pltpu.VMEM),
        cost_estimate=pl.CostEstimate(
            flops=0, bytes_accessed=8 * index.shape[0] * 64 * value_count, transcendentals=0
        ),
    )(index, field)


def to_patches(state_field):
    band_rows = state_field.shape[0] // 8
    band_cols = state_field.shape[1] // 8
    return (
        state_field.reshape(band_rows, 8, band_cols, 8, -1)
        .transpose(0, 2, 1, 3, 4)
        .reshape(band_rows * band_cols, 64, -1)
    )


def from_patches(patches, band_rows, band_cols):
    return (
        patches.reshape(band_rows, band_cols, 8, 8, -1)
        .transpose(0, 2, 1, 3, 4)
        .reshape(band_rows * 8, band_cols * 8, -1)
    )


def column_area(first_row, row_count, total_rows):
    latitude = ((first_row + jnp.arange(row_count)).astype(jnp.float32) + 0.5) * (
        math.pi / total_rows
    ) - 0.5 * math.pi
    return jnp.cos(latitude)


def column_mass(state_field, weights):
    return jnp.sum(weights[:, None, None] * state_field, axis=(0, 1))


def diffuse(advected, diffusivity, row_dim):
    col_dim = row_dim + 1
    rows = advected.shape[row_dim]
    cols = advected.shape[col_dim]
    lon_wide = extended(advected, (("lon", col_dim),), 1, True)
    lat_wide = extended(advected, (("lat", row_dim),), 1, False)
    laplace = (
        lax.slice_in_dim(lat_wide, 2, rows + 2, axis=row_dim)
        + lax.slice_in_dim(lat_wide, 0, rows, axis=row_dim)
        + lax.slice_in_dim(lon_wide, 2, cols + 2, axis=col_dim)
        + lax.slice_in_dim(lon_wide, 0, cols, axis=col_dim)
        - 4.0 * advected
    )
    k_shape = [1] * advected.ndim
    k_shape[row_dim] = rows
    return advected + diffusivity.reshape(k_shape) * laplace


def levels_field(values, weight_z):
    value_count = values.shape[-1]
    per_level = value_count // LEV
    blocks = [values[..., m * per_level : (m + 1) * per_level] for m in range(LEV)]
    out = []
    for level in range(LEV):
        acc = None
        for m in tap_sources(level, LEV):
            term = weight_z[..., level, m][..., None] * blocks[m]
            acc = term if acc is None else acc + term
        out.append(acc)
    return jnp.concatenate(out, axis=-1)


def diffuse_first(advected, diffusivity):
    rows, cols, value_count = advected.shape
    count = lax.axis_size("lat")

    def pack(row, number):
        return jnp.concatenate(
            [row, jnp.broadcast_to(number, (1, 1, value_count))], axis=1
        )

    from_above = lax.ppermute(
        pack(advected[rows - 1 :], diffusivity[rows - 1]),
        "lat",
        [(i, i + 1) for i in range(count - 1)],
    )
    from_below = lax.ppermute(
        pack(advected[:1], diffusivity[0]), "lat", [(i + 1, i) for i in range(count - 1)]
    )
    lat_wide = jnp.concatenate([from_above[:, :cols], advected, from_below[:, :cols]], axis=0)
    k_wide = jnp.concatenate([from_above[0, cols, :1], diffusivity, from_below[0, cols, :1]])
    lon_wide = extended(advected, (("lon", 1),), 1, True)
    laplace = (
        lat_wide[2:] + lat_wide[:-2] + lon_wide[:, 2:] + lon_wide[:, :-2] - 4.0 * advected
    )
    return advected + diffusivity[:, None, None] * laplace, k_wide


def departed(state_field, source_ids, shifts_now):
    lat_count = lax.axis_size("lat")
    lat_index = lax.axis_index("lat")
    lon_index = lax.axis_index("lon")
    row_count, col_count, value_count = state_field.shape
    band_rows = row_count // 8
    band_cols = col_count // 8
    per_device = band_rows * band_cols
    total_cols = source_ids.shape[1]
    devices = jnp.arange(lat_count)
    slot_range = jnp.arange(CAP)
    column_ids = lax.dynamic_slice_in_dim(
        source_ids, lon_index * band_cols, band_cols, 1
    ).reshape(lat_count, per_device)
    fractions = lax.dynamic_slice_in_dim(
        shifts_now, lon_index * band_cols, band_cols, 2
    ).reshape(3, lat_count, per_device)
    source_row = column_ids // total_cols
    source_dev = source_row // band_rows
    source_local = (
        source_row % band_rows * band_cols + column_ids % total_cols - lon_index * band_cols
    )
    remote = source_dev != devices[:, None]
    matches = (source_dev[:, :, None] == devices[None, None, :]) & remote[:, :, None]
    slot_ranks = jnp.cumsum(matches.astype(jnp.int32), axis=1) - 1
    slot_of = jnp.sum(jnp.where(matches, slot_ranks, 0), axis=2)
    owned_here = remote & (source_dev == lat_index)
    sending = owned_here[:, :, None] & (slot_of[:, :, None] == slot_range[None, None, :])
    send_local = jnp.sum(jnp.where(sending, source_local[:, :, None], 0), axis=1)
    outgoing = gather_patches(
        jnp.clip(send_local.reshape(-1), 0, per_device - 1), state_field
    ).reshape(
        lat_count, CAP, 64, value_count
    )
    my_dev = lax.dynamic_index_in_dim(source_dev, lat_index, 0, keepdims=False)
    my_slot = lax.dynamic_index_in_dim(slot_of, lat_index, 0, keepdims=False)
    my_local = lax.dynamic_index_in_dim(source_local, lat_index, 0, keepdims=False)
    my_remote = lax.dynamic_index_in_dim(remote, lat_index, 0, keepdims=False)
    my_frac = lax.dynamic_index_in_dim(fractions, lat_index, 1, keepdims=False)
    arrived = lax.all_to_all(outgoing, "lat", 0, 0, tiled=True).reshape(
        lat_count * CAP, 64, value_count
    )
    pick_index = jnp.clip(my_dev * CAP + my_slot, 0, lat_count * CAP - 1)
    my_local = jnp.clip(my_local, 0, per_device - 1)
    return my_local, pick_index, my_remote.astype(jnp.int32), arrived, my_frac


def local(tracers, shifts, diffusivity, source_patch):
    lat_count = lax.axis_size("lat")
    lat_index = lax.axis_index("lat")
    row_count, col_count, value_count = tracers.shape
    band_rows = row_count // 8
    band_cols = col_count // 8
    per_device = band_rows * band_cols
    per_level = value_count // LEV
    total_rows = row_count * lat_count
    weights = column_area(lat_index * row_count, row_count, total_rows)
    target_part = column_mass(tracers, weights)

    near, pick, remote, arrived, frac = departed(tracers, source_patch[0], shifts[0])
    advected = interpolate_into_field(
        near,
        pick,
        remote,
        tracers,
        arrived,
        plane_weights(frac[0], frac[1]),
        level_rolls(frac[2], value_count),
    )
    first, k_wide = diffuse_first(advected, diffusivity)
    first_part = column_mass(first, weights)

    near, pick, remote, arrived, frac = departed(first, source_patch[1], shifts[1])
    planar = interpolate_into_field(
        near, pick, remote, first, arrived, plane_weights(frac[0], frac[1])
    )
    weight_z = cubic_matrix(frac[2], LEV)

    area_wide = column_area(lat_index * row_count - 1, row_count + 2, total_rows)
    flux = area_wide * k_wide
    g = weights - 2.0 * flux[1:-1] + flux[:-2] + flux[2:]
    weighted = jnp.sum(
        (g[:, None, None] * planar).reshape(band_rows, 8, band_cols, 8, value_count), axis=(1, 3)
    ).reshape(per_device, LEV, per_level)
    mix_part = jnp.einsum(
        "plm,pmt->lmt", weight_z, weighted, precision=lax.Precision.HIGHEST
    )
    totals = all_sum(
        jnp.concatenate([target_part, first_part, mix_part.reshape(-1)]), ("lon", "lat")
    )
    target = totals[:value_count]
    first_mass = totals[value_count : 2 * value_count]
    mix = totals[2 * value_count :].reshape(LEV, LEV, per_level)
    first_ratio = target / first_mass
    second_mass = jnp.sum(first_ratio.reshape(LEV, per_level)[None] * mix, axis=1).reshape(
        value_count
    )
    second_ratio = target / second_mass
    advected = levels_field(
        (planar * first_ratio).reshape(band_rows, 8, band_cols, 8, value_count),
        weight_z.reshape(band_rows, 1, band_cols, 1, LEV, LEV),
    ).reshape(row_count, col_count, value_count)
    return diffuse(advected, diffusivity, 0) * second_ratio[None, None, :]


def solution(mesh):
    return jax.shard_map(
        local,
        mesh=mesh,
        in_specs=(
            P(("groups", "lat"), "lon", None),
            P("groups", None, None, None),
            P("lat"),
            P("groups", None, None),
        ),
        out_specs=P(("groups", "lat"), "lon", None),
        check_vma=False,
    )
```

```python
import math

import jax
import jax.numpy as jnp
from jax import lax
from jax.sharding import PartitionSpec as P

LEV = 4
STEPS = 2
CAP = 4


def all_sum(value, axes, rider=None):
    rider_done = None
    for axis in axes:
        count = lax.axis_size(axis)
        if count & (count - 1):
            value = lax.psum(value, axis)
            continue
        distance = 1
        while distance < count:
            value = value + lax.ppermute(
                value, axis, [(i, i ^ distance) for i in range(count)]
            )
            if rider is not None:
                value, rider = lax.optimization_barrier((value, rider))
                rider_done, rider = rider, None
            distance *= 2
    if rider_done is None and rider is None:
        return value
    return value, rider if rider_done is None else rider_done


def extended(cells, sides, width, closed):
    for axis, dim in sides:
        count = lax.axis_size(axis)
        ends = count if closed else count - 1
        head = lax.slice_in_dim(cells, 0, width, axis=dim)
        tail = lax.slice_in_dim(cells, cells.shape[dim] - width, cells.shape[dim], axis=dim)
        cells = jnp.concatenate(
            [
                lax.ppermute(tail, axis, [(i, (i + 1) % count) for i in range(ends)]),
                cells,
                lax.ppermute(head, axis, [((i + 1) % count, i) for i in range(ends)]),
            ],
            axis=dim,
        )
    return cells


def cubic_weights(fraction):
    first_term = -fraction * (fraction - 1.0) * (fraction - 2.0) / 6.0
    second_term = (fraction + 1.0) * (fraction - 1.0) * (fraction - 2.0) / 2.0
    third_term = -(fraction + 1.0) * fraction * (fraction - 2.0) / 2.0
    fourth_term = (fraction + 1.0) * fraction * (fraction - 1.0) / 6.0
    return (first_term, second_term, third_term, fourth_term)


def cubic_matrix(fraction, extent):
    places = jnp.arange(extent)
    running = jnp.zeros(fraction.shape + (extent, extent), jnp.float32)
    for offset, weight in zip(range(-1, 3), cubic_weights(fraction)):
        target_col = jnp.clip(places + offset, 0, extent - 1)
        indicator = (target_col[:, None] == places[None, :]).astype(jnp.float32)
        running = running + weight[..., None, None] * indicator
    return running


def tap_sources(target, extent):
    return sorted({min(max(target + offset, 0), extent - 1) for offset in range(-1, 3)})


def plane_weights(fraction_y, fraction_x):
    rows = lax.broadcasted_iota(jnp.int32, (1, 64, 64), 1)
    cols = lax.broadcasted_iota(jnp.int32, (1, 64, 64), 2)

    def along(fraction, source, target):
        running = jnp.zeros((fraction.shape[0], 64, 64), jnp.float32)
        for offset, weight in zip(range(-1, 3), cubic_weights(fraction)):
            indicator = (jnp.clip(source + offset, 0, 7) == target).astype(jnp.float32)
            running = running + weight[:, None, None] * indicator
        return running

    return along(fraction_y, rows // 8, cols // 8) * along(fraction_x, rows % 8, cols % 8)


def spatial(patches, fraction_y, fraction_x):
    return jnp.einsum(
        "nij,njv->niv",
        plane_weights(fraction_y, fraction_x),
        patches,
        precision=lax.Precision.HIGHEST,
    )


def levels(flat, fraction_z):
    value_count = flat.shape[2]
    per_level = value_count // LEV
    weight_z = cubic_matrix(fraction_z, LEV)
    blocks = [flat[:, :, m * per_level : (m + 1) * per_level] for m in range(LEV)]
    out = []
    for level in range(LEV):
        acc = None
        for m in tap_sources(level, LEV):
            term = weight_z[:, level, m][:, None, None] * blocks[m]
            acc = term if acc is None else acc + term
        out.append(acc)
    return jnp.concatenate(out, axis=2)


def to_patches(state_field):
    band_rows = state_field.shape[0] // 8
    band_cols = state_field.shape[1] // 8
    return (
        state_field.reshape(band_rows, 8, band_cols, 8, -1)
        .transpose(0, 2, 1, 3, 4)
        .reshape(band_rows * band_cols, 64, -1)
    )


def from_patches(patches, band_rows, band_cols):
    return (
        patches.reshape(band_rows, band_cols, 8, 8, -1)
        .transpose(0, 2, 1, 3, 4)
        .reshape(band_rows * 8, band_cols * 8, -1)
    )


def column_area(first_row, row_count, total_rows):
    latitude = ((first_row + jnp.arange(row_count)).astype(jnp.float32) + 0.5) * (
        math.pi / total_rows
    ) - 0.5 * math.pi
    return jnp.cos(latitude)


def column_mass(state_field, weights):
    return jnp.sum(weights[:, None, None] * state_field, axis=(0, 1))


def diffuse(advected, diffusivity, row_dim):
    col_dim = row_dim + 1
    rows = advected.shape[row_dim]
    cols = advected.shape[col_dim]
    lon_wide = extended(advected, (("lon", col_dim),), 1, True)
    lat_wide = extended(advected, (("lat", row_dim),), 1, False)
    laplace = (
        lax.slice_in_dim(lat_wide, 2, rows + 2, axis=row_dim)
        + lax.slice_in_dim(lat_wide, 0, rows, axis=row_dim)
        + lax.slice_in_dim(lon_wide, 2, cols + 2, axis=col_dim)
        + lax.slice_in_dim(lon_wide, 0, cols, axis=col_dim)
        - 4.0 * advected
    )
    k_shape = [1] * advected.ndim
    k_shape[row_dim] = rows
    return advected + diffusivity.reshape(k_shape) * laplace


def diffuse_first(advected, diffusivity):
    rows, cols, value_count = advected.shape
    count = lax.axis_size("lat")

    def pack(row, number):
        return jnp.concatenate(
            [row, jnp.broadcast_to(number, (1, 1, value_count))], axis=1
        )

    from_above = lax.ppermute(
        pack(advected[rows - 1 :], diffusivity[rows - 1]),
        "lat",
        [(i, i + 1) for i in range(count - 1)],
    )
    from_below = lax.ppermute(
        pack(advected[:1], diffusivity[0]), "lat", [(i + 1, i) for i in range(count - 1)]
    )
    lat_wide = jnp.concatenate([from_above[:, :cols], advected, from_below[:, :cols]], axis=0)
    k_wide = jnp.concatenate([from_above[0, cols, :1], diffusivity, from_below[0, cols, :1]])
    lon_wide = extended(advected, (("lon", 1),), 1, True)
    laplace = (
        lat_wide[2:] + lat_wide[:-2] + lon_wide[:, 2:] + lon_wide[:, :-2] - 4.0 * advected
    )
    return advected + diffusivity[:, None, None] * laplace, k_wide


def departed(state_field, source_ids, shifts_now):
    lat_count = lax.axis_size("lat")
    lat_index = lax.axis_index("lat")
    lon_index = lax.axis_index("lon")
    row_count, col_count, value_count = state_field.shape
    band_rows = row_count // 8
    band_cols = col_count // 8
    per_device = band_rows * band_cols
    total_cols = source_ids.shape[1]
    devices = jnp.arange(lat_count)
    slot_range = jnp.arange(CAP)
    column_ids = lax.dynamic_slice_in_dim(
        source_ids, lon_index * band_cols, band_cols, 1
    ).reshape(lat_count, per_device)
    fractions = lax.dynamic_slice_in_dim(
        shifts_now, lon_index * band_cols, band_cols, 2
    ).reshape(3, lat_count, per_device)
    source_row = column_ids // total_cols
    source_dev = source_row // band_rows
    source_local = (
        source_row % band_rows * band_cols + column_ids % total_cols - lon_index * band_cols
    )
    remote = source_dev != devices[:, None]
    matches = (source_dev[:, :, None] == devices[None, None, :]) & remote[:, :, None]
    slot_ranks = jnp.cumsum(matches.astype(jnp.int32), axis=1) - 1
    slot_of = jnp.sum(jnp.where(matches, slot_ranks, 0), axis=2)
    owned_here = remote & (source_dev == lat_index)
    sending = owned_here[:, :, None] & (slot_of[:, :, None] == slot_range[None, None, :])
    send_local = jnp.sum(jnp.where(sending, source_local[:, :, None], 0), axis=1)
    own_patches = to_patches(state_field)
    outgoing = own_patches[send_local.reshape(-1)].reshape(lat_count, CAP, 64, value_count)
    my_dev = lax.dynamic_index_in_dim(source_dev, lat_index, 0, keepdims=False)
    my_slot = lax.dynamic_index_in_dim(slot_of, lat_index, 0, keepdims=False)
    my_local = lax.dynamic_index_in_dim(source_local, lat_index, 0, keepdims=False)
    my_remote = lax.dynamic_index_in_dim(remote, lat_index, 0, keepdims=False)
    my_frac = lax.dynamic_index_in_dim(fractions, lat_index, 1, keepdims=False)
    arrived = lax.all_to_all(outgoing, "lat", 0, 0, tiled=True).reshape(
        lat_count * CAP, 64, value_count
    )
    pick_index = my_dev * CAP + my_slot
    patches = jnp.where(my_remote[:, None, None], arrived[pick_index], own_patches[my_local])
    return patches, my_frac


def local(tracers, shifts, diffusivity, source_patch):
    lat_count = lax.axis_size("lat")
    lat_index = lax.axis_index("lat")
    row_count, col_count, value_count = tracers.shape
    band_rows = row_count // 8
    band_cols = col_count // 8
    per_device = band_rows * band_cols
    per_level = value_count // LEV
    total_rows = row_count * lat_count
    weights = column_area(lat_index * row_count, row_count, total_rows)
    target_part = column_mass(tracers, weights)

    patches, frac = departed(tracers, source_patch[0], shifts[0])
    advected = from_patches(spatial(levels(patches, frac[2]), frac[0], frac[1]), band_rows, band_cols)
    first, k_wide = diffuse_first(advected, diffusivity)
    first_part = column_mass(first, weights)

    patches, frac = departed(first, source_patch[1], shifts[1])
    planar = spatial(patches, frac[0], frac[1])
    weight_z = cubic_matrix(frac[2], LEV)

    area_wide = column_area(lat_index * row_count - 1, row_count + 2, total_rows)
    flux = area_wide * k_wide
    g = weights - 2.0 * flux[1:-1] + flux[:-2] + flux[2:]
    g_cols = jnp.broadcast_to(g.reshape(band_rows, 1, 8, 1), (band_rows, band_cols, 8, 8))
    weighted = jnp.einsum(
        "pi,piv->pv", g_cols.reshape(per_device, 64), planar, precision=lax.Precision.HIGHEST
    ).reshape(per_device, LEV, per_level)
    mix_part = jnp.einsum(
        "plm,pmt->lmt", weight_z, weighted, precision=lax.Precision.HIGHEST
    )
    totals = all_sum(
        jnp.concatenate([target_part, first_part, mix_part.reshape(-1)]), ("lon", "lat")
    )
    target = totals[:value_count]
    first_mass = totals[value_count : 2 * value_count]
    mix = totals[2 * value_count :].reshape(LEV, LEV, per_level)
    first_ratio = target / first_mass
    second_mass = jnp.sum(first_ratio.reshape(LEV, per_level)[None] * mix, axis=1).reshape(
        value_count
    )
    second_ratio = target / second_mass
    advected = from_patches(
        levels(planar * first_ratio[None, None, :], frac[2]), band_rows, band_cols
    )
    return diffuse(advected, diffusivity, 0) * second_ratio[None, None, :]


def solution(mesh):
    return jax.shard_map(
        local,
        mesh=mesh,
        in_specs=(
            P(("groups", "lat"), "lon", None),
            P("groups", None, None, None),
            P("lat"),
            P("groups", None, None),
        ),
        out_specs=P(("groups", "lat"), "lon", None),
        check_vma=False,
    )
```

```python
import math

import jax
import jax.numpy as jnp
from jax import lax
from jax.sharding import PartitionSpec as P

LEV = 4
STEPS = 2
CAP = 4


def all_sum(value, axes, rider=None):
    rider_done = None
    for axis in axes:
        count = lax.axis_size(axis)
        if count & (count - 1):
            value = lax.psum(value, axis)
            continue
        distance = 1
        while distance < count:
            value = value + lax.ppermute(
                value, axis, [(i, i ^ distance) for i in range(count)]
            )
            if rider is not None:
                value, rider = lax.optimization_barrier((value, rider))
                rider_done, rider = rider, None
            distance *= 2
    if rider_done is None and rider is None:
        return value
    return value, rider if rider_done is None else rider_done


def extended(cells, sides, width, closed):
    for axis, dim in sides:
        count = lax.axis_size(axis)
        ends = count if closed else count - 1
        head = lax.slice_in_dim(cells, 0, width, axis=dim)
        tail = lax.slice_in_dim(cells, cells.shape[dim] - width, cells.shape[dim], axis=dim)
        cells = jnp.concatenate(
            [
                lax.ppermute(tail, axis, [(i, (i + 1) % count) for i in range(ends)]),
                cells,
                lax.ppermute(head, axis, [((i + 1) % count, i) for i in range(ends)]),
            ],
            axis=dim,
        )
    return cells


def cubic_weights(fraction):
    first_term = -fraction * (fraction - 1.0) * (fraction - 2.0) / 6.0
    second_term = (fraction + 1.0) * (fraction - 1.0) * (fraction - 2.0) / 2.0
    third_term = -(fraction + 1.0) * fraction * (fraction - 2.0) / 2.0
    fourth_term = (fraction + 1.0) * fraction * (fraction - 1.0) / 6.0
    return (first_term, second_term, third_term, fourth_term)


def cubic_matrix(fraction, extent):
    places = jnp.arange(extent)
    running = jnp.zeros(fraction.shape + (extent, extent), jnp.float32)
    for offset, weight in zip(range(-1, 3), cubic_weights(fraction)):
        target_col = jnp.clip(places + offset, 0, extent - 1)
        indicator = (target_col[:, None] == places[None, :]).astype(jnp.float32)
        running = running + weight[..., None, None] * indicator
    return running


def tap_sources(target, extent):
    return sorted({min(max(target + offset, 0), extent - 1) for offset in range(-1, 3)})


def plane_weights(fraction_y, fraction_x):
    rows = lax.broadcasted_iota(jnp.int32, (1, 64, 64), 1)
    cols = lax.broadcasted_iota(jnp.int32, (1, 64, 64), 2)

    def along(fraction, source, target):
        running = jnp.zeros((fraction.shape[0], 64, 64), jnp.float32)
        for offset, weight in zip(range(-1, 3), cubic_weights(fraction)):
            indicator = (jnp.clip(source + offset, 0, 7) == target).astype(jnp.float32)
            running = running + weight[:, None, None] * indicator
        return running

    return along(fraction_y, rows // 8, cols // 8) * along(fraction_x, rows % 8, cols % 8)


def spatial(patches, fraction_y, fraction_x):
    return jnp.einsum(
        "nij,njv->niv",
        plane_weights(fraction_y, fraction_x),
        patches,
        precision=lax.Precision.HIGHEST,
    )


def levels(flat, fraction_z):
    value_count = flat.shape[2]
    per_level = value_count // LEV
    weight_z = cubic_matrix(fraction_z, LEV)
    blocks = [flat[:, :, m * per_level : (m + 1) * per_level] for m in range(LEV)]
    out = []
    for level in range(LEV):
        acc = None
        for m in tap_sources(level, LEV):
            term = weight_z[:, level, m][:, None, None] * blocks[m]
            acc = term if acc is None else acc + term
        out.append(acc)
    return jnp.concatenate(out, axis=2)


def to_patches(state_field):
    band_rows = state_field.shape[0] // 8
    band_cols = state_field.shape[1] // 8
    return (
        state_field.reshape(band_rows, 8, band_cols, 8, -1)
        .transpose(0, 2, 1, 3, 4)
        .reshape(band_rows * band_cols, 64, -1)
    )


def from_patches(patches, band_rows, band_cols):
    return (
        patches.reshape(band_rows, band_cols, 8, 8, -1)
        .transpose(0, 2, 1, 3, 4)
        .reshape(band_rows * 8, band_cols * 8, -1)
    )


def column_area(first_row, row_count, total_rows):
    latitude = ((first_row + jnp.arange(row_count)).astype(jnp.float32) + 0.5) * (
        math.pi / total_rows
    ) - 0.5 * math.pi
    return jnp.cos(latitude)


def column_mass(state_field, weights):
    return jnp.sum(weights[:, None, None] * state_field, axis=(0, 1))


def diffuse(advected, diffusivity, row_dim):
    col_dim = row_dim + 1
    rows = advected.shape[row_dim]
    cols = advected.shape[col_dim]
    lon_wide = extended(advected, (("lon", col_dim),), 1, True)
    lat_wide = extended(advected, (("lat", row_dim),), 1, False)
    laplace = (
        lax.slice_in_dim(lat_wide, 2, rows + 2, axis=row_dim)
        + lax.slice_in_dim(lat_wide, 0, rows, axis=row_dim)
        + lax.slice_in_dim(lon_wide, 2, cols + 2, axis=col_dim)
        + lax.slice_in_dim(lon_wide, 0, cols, axis=col_dim)
        - 4.0 * advected
    )
    k_shape = [1] * advected.ndim
    k_shape[row_dim] = rows
    return advected + diffusivity.reshape(k_shape) * laplace


def diffuse_first(advected, diffusivity):
    rows, cols, value_count = advected.shape
    count = lax.axis_size("lat")

    def pack(row, number):
        return jnp.concatenate(
            [row, jnp.broadcast_to(number, (1, 1, value_count))], axis=1
        )

    from_above = lax.ppermute(
        pack(advected[rows - 1 :], diffusivity[rows - 1]),
        "lat",
        [(i, i + 1) for i in range(count - 1)],
    )
    from_below = lax.ppermute(
        pack(advected[:1], diffusivity[0]), "lat", [(i + 1, i) for i in range(count - 1)]
    )
    lat_wide = jnp.concatenate([from_above[:, :cols], advected, from_below[:, :cols]], axis=0)
    k_wide = jnp.concatenate([from_above[0, cols, :1], diffusivity, from_below[0, cols, :1]])
    lon_wide = extended(advected, (("lon", 1),), 1, True)
    laplace = (
        lat_wide[2:] + lat_wide[:-2] + lon_wide[:, 2:] + lon_wide[:, :-2] - 4.0 * advected
    )
    return advected + diffusivity[:, None, None] * laplace, k_wide


def departed(state_field, source_ids, shifts_now):
    lat_count = lax.axis_size("lat")
    lat_index = lax.axis_index("lat")
    lon_index = lax.axis_index("lon")
    row_count, col_count, value_count = state_field.shape
    band_rows = row_count // 8
    band_cols = col_count // 8
    per_device = band_rows * band_cols
    total_cols = source_ids.shape[1]
    devices = jnp.arange(lat_count)
    slot_range = jnp.arange(CAP)
    column_ids = lax.dynamic_slice_in_dim(
        source_ids, lon_index * band_cols, band_cols, 1
    ).reshape(lat_count, per_device)
    fractions = lax.dynamic_slice_in_dim(
        shifts_now, lon_index * band_cols, band_cols, 2
    ).reshape(3, lat_count, per_device)
    source_row = column_ids // total_cols
    source_dev = source_row // band_rows
    source_local = (
        source_row % band_rows * band_cols + column_ids % total_cols - lon_index * band_cols
    )
    remote = source_dev != devices[:, None]
    matches = (source_dev[:, :, None] == devices[None, None, :]) & remote[:, :, None]
    slot_ranks = jnp.cumsum(matches.astype(jnp.int32), axis=1) - 1
    slot_of = jnp.sum(jnp.where(matches, slot_ranks, 0), axis=2)
    owned_here = remote & (source_dev == lat_index)
    sending = owned_here[:, :, None] & (slot_of[:, :, None] == slot_range[None, None, :])
    send_local = jnp.sum(jnp.where(sending, source_local[:, :, None], 0), axis=1)
    own_patches = to_patches(state_field)
    outgoing = own_patches[send_local.reshape(-1)].reshape(lat_count, CAP, 64, value_count)
    my_dev = lax.dynamic_index_in_dim(source_dev, lat_index, 0, keepdims=False)
    my_slot = lax.dynamic_index_in_dim(slot_of, lat_index, 0, keepdims=False)
    my_local = lax.dynamic_index_in_dim(source_local, lat_index, 0, keepdims=False)
    my_remote = lax.dynamic_index_in_dim(remote, lat_index, 0, keepdims=False)
    my_frac = lax.dynamic_index_in_dim(fractions, lat_index, 1, keepdims=False)
    arrived = lax.all_to_all(outgoing, "lat", 0, 0, tiled=True).reshape(
        lat_count * CAP, 64, value_count
    )
    pick_index = my_dev * CAP + my_slot
    patches = jnp.where(my_remote[:, None, None], arrived[pick_index], own_patches[my_local])
    return patches, my_frac


def local(tracers, shifts, diffusivity, source_patch):
    lat_count = lax.axis_size("lat")
    lat_index = lax.axis_index("lat")
    row_count, col_count, value_count = tracers.shape
    band_rows = row_count // 8
    band_cols = col_count // 8
    per_device = band_rows * band_cols
    per_level = value_count // LEV
    total_rows = row_count * lat_count
    weights = column_area(lat_index * row_count, row_count, total_rows)
    target_part = column_mass(tracers, weights)

    patches, frac = departed(tracers, source_patch[0], shifts[0])
    advected = from_patches(levels(spatial(patches, frac[0], frac[1]), frac[2]), band_rows, band_cols)
    first, k_wide = diffuse_first(advected, diffusivity)
    first_part = column_mass(first, weights)

    patches, frac = departed(first, source_patch[1], shifts[1])
    planar = spatial(patches, frac[0], frac[1])
    weight_z = cubic_matrix(frac[2], LEV)

    area_wide = column_area(lat_index * row_count - 1, row_count + 2, total_rows)
    flux = area_wide * k_wide
    g = weights - 2.0 * flux[1:-1] + flux[:-2] + flux[2:]
    g_cols = jnp.broadcast_to(g.reshape(band_rows, 1, 8, 1), (band_rows, band_cols, 8, 8))
    weighted = jnp.einsum(
        "pi,piv->pv", g_cols.reshape(per_device, 64), planar, precision=lax.Precision.HIGHEST
    ).reshape(per_device, LEV, per_level)
    mix_part = jnp.einsum(
        "plm,pmt->lmt", weight_z, weighted, precision=lax.Precision.HIGHEST
    )
    totals = all_sum(
        jnp.concatenate([target_part, first_part, mix_part.reshape(-1)]), ("lat", "lon")
    )
    target = totals[:value_count]
    first_mass = totals[value_count : 2 * value_count]
    mix = totals[2 * value_count :].reshape(LEV, LEV, per_level)
    first_ratio = target / first_mass
    second_mass = jnp.sum(first_ratio.reshape(LEV, per_level)[None] * mix, axis=1).reshape(
        value_count
    )
    second_ratio = target / second_mass
    advected = from_patches(
        levels(planar * first_ratio[None, None, :], frac[2]), band_rows, band_cols
    )
    return diffuse(advected, diffusivity, 0) * second_ratio[None, None, :]


def solution(mesh):
    return jax.shard_map(
        local,
        mesh=mesh,
        in_specs=(
            P(("groups", "lat"), "lon", None),
            P("groups", None, None, None),
            P("lat"),
            P("groups", None, None),
        ),
        out_specs=P(("groups", "lat"), "lon", None),
        check_vma=False,
    )
```

```python
import math

import jax
import jax.numpy as jnp
from jax import lax
from jax.sharding import PartitionSpec as P

LEV = 4
STEPS = 2
CAP = 4


def all_sum(value, axes, rider=None):
    rider_done = None
    for axis in axes:
        count = lax.axis_size(axis)
        if count & (count - 1):
            value = lax.psum(value, axis)
            continue
        distance = 1
        while distance < count:
            value = value + lax.ppermute(
                value, axis, [(i, i ^ distance) for i in range(count)]
            )
            if rider is not None:
                value, rider = lax.optimization_barrier((value, rider))
                rider_done, rider = rider, None
            distance *= 2
    if rider_done is None and rider is None:
        return value
    return value, rider if rider_done is None else rider_done


def extended(cells, sides, width, closed):
    for axis, dim in sides:
        count = lax.axis_size(axis)
        ends = count if closed else count - 1
        head = lax.slice_in_dim(cells, 0, width, axis=dim)
        tail = lax.slice_in_dim(cells, cells.shape[dim] - width, cells.shape[dim], axis=dim)
        cells = jnp.concatenate(
            [
                lax.ppermute(tail, axis, [(i, (i + 1) % count) for i in range(ends)]),
                cells,
                lax.ppermute(head, axis, [((i + 1) % count, i) for i in range(ends)]),
            ],
            axis=dim,
        )
    return cells


def cubic_weights(fraction):
    first_term = -fraction * (fraction - 1.0) * (fraction - 2.0) / 6.0
    second_term = (fraction + 1.0) * (fraction - 1.0) * (fraction - 2.0) / 2.0
    third_term = -(fraction + 1.0) * fraction * (fraction - 2.0) / 2.0
    fourth_term = (fraction + 1.0) * fraction * (fraction - 1.0) / 6.0
    return (first_term, second_term, third_term, fourth_term)


def cubic_matrix(fraction, extent):
    places = jnp.arange(extent)
    running = jnp.zeros(fraction.shape + (extent, extent), jnp.float32)
    for offset, weight in zip(range(-1, 3), cubic_weights(fraction)):
        target_col = jnp.clip(places + offset, 0, extent - 1)
        indicator = (target_col[:, None] == places[None, :]).astype(jnp.float32)
        running = running + weight[..., None, None] * indicator
    return running


def tap_sources(target, extent):
    return sorted({min(max(target + offset, 0), extent - 1) for offset in range(-1, 3)})


def plane_weights(fraction_y, fraction_x):
    rows = lax.broadcasted_iota(jnp.int32, (1, 64, 64), 1)
    cols = lax.broadcasted_iota(jnp.int32, (1, 64, 64), 2)

    def along(fraction, source, target):
        running = jnp.zeros((fraction.shape[0], 64, 64), jnp.float32)
        for offset, weight in zip(range(-1, 3), cubic_weights(fraction)):
            indicator = (jnp.clip(source + offset, 0, 7) == target).astype(jnp.float32)
            running = running + weight[:, None, None] * indicator
        return running

    return along(fraction_y, rows // 8, cols // 8) * along(fraction_x, rows % 8, cols % 8)


def spatial(patches, fraction_y, fraction_x):
    return jnp.einsum(
        "nij,njv->niv",
        plane_weights(fraction_y, fraction_x),
        patches,
        precision=lax.Precision.HIGHEST,
    )


def levels(flat, fraction_z):
    value_count = flat.shape[2]
    per_level = value_count // LEV
    weight_z = cubic_matrix(fraction_z, LEV)
    blocks = [flat[:, :, m * per_level : (m + 1) * per_level] for m in range(LEV)]
    out = []
    for level in range(LEV):
        acc = None
        for m in tap_sources(level, LEV):
            term = weight_z[:, level, m][:, None, None] * blocks[m]
            acc = term if acc is None else acc + term
        out.append(acc)
    return jnp.concatenate(out, axis=2)


def to_patches(state_field):
    band_rows = state_field.shape[0] // 8
    band_cols = state_field.shape[1] // 8
    return (
        state_field.reshape(band_rows, 8, band_cols, 8, -1)
        .transpose(0, 2, 1, 3, 4)
        .reshape(band_rows * band_cols, 64, -1)
    )


def from_patches(patches, band_rows, band_cols):
    return (
        patches.reshape(band_rows, band_cols, 8, 8, -1)
        .transpose(0, 2, 1, 3, 4)
        .reshape(band_rows * 8, band_cols * 8, -1)
    )


def column_area(first_row, row_count, total_rows):
    latitude = ((first_row + jnp.arange(row_count)).astype(jnp.float32) + 0.5) * (
        math.pi / total_rows
    ) - 0.5 * math.pi
    return jnp.cos(latitude)


def column_mass(state_field, weights):
    return jnp.sum(weights[:, None, None] * state_field, axis=(0, 1))


def diffuse(advected, diffusivity, row_dim):
    col_dim = row_dim + 1
    rows = advected.shape[row_dim]
    cols = advected.shape[col_dim]
    lon_wide = extended(advected, (("lon", col_dim),), 1, True)
    lat_wide = extended(advected, (("lat", row_dim),), 1, False)
    laplace = (
        lax.slice_in_dim(lat_wide, 2, rows + 2, axis=row_dim)
        + lax.slice_in_dim(lat_wide, 0, rows, axis=row_dim)
        + lax.slice_in_dim(lon_wide, 2, cols + 2, axis=col_dim)
        + lax.slice_in_dim(lon_wide, 0, cols, axis=col_dim)
        - 4.0 * advected
    )
    k_shape = [1] * advected.ndim
    k_shape[row_dim] = rows
    return advected + diffusivity.reshape(k_shape) * laplace


def diffuse_first(advected, diffusivity):
    rows, cols, value_count = advected.shape
    count = lax.axis_size("lat")

    def pack(row, number):
        return jnp.concatenate(
            [row, jnp.broadcast_to(number, (1, 1, value_count))], axis=1
        )

    from_above = lax.ppermute(
        pack(advected[rows - 1 :], diffusivity[rows - 1]),
        "lat",
        [(i, i + 1) for i in range(count - 1)],
    )
    from_below = lax.ppermute(
        pack(advected[:1], diffusivity[0]), "lat", [(i + 1, i) for i in range(count - 1)]
    )
    lat_wide = jnp.concatenate([from_above[:, :cols], advected, from_below[:, :cols]], axis=0)
    k_wide = jnp.concatenate([from_above[0, cols, :1], diffusivity, from_below[0, cols, :1]])
    lon_wide = extended(advected, (("lon", 1),), 1, True)
    laplace = (
        lat_wide[2:] + lat_wide[:-2] + lon_wide[:, 2:] + lon_wide[:, :-2] - 4.0 * advected
    )
    return advected + diffusivity[:, None, None] * laplace, k_wide


def departed(state_field, source_ids, shifts_now):
    lat_count = lax.axis_size("lat")
    lat_index = lax.axis_index("lat")
    lon_index = lax.axis_index("lon")
    row_count, col_count, value_count = state_field.shape
    band_rows = row_count // 8
    band_cols = col_count // 8
    per_device = band_rows * band_cols
    total_cols = source_ids.shape[1]
    devices = jnp.arange(lat_count)
    slot_range = jnp.arange(CAP)
    column_ids = lax.dynamic_slice_in_dim(
        source_ids, lon_index * band_cols, band_cols, 1
    ).reshape(lat_count, per_device)
    fractions = lax.dynamic_slice_in_dim(
        shifts_now, lon_index * band_cols, band_cols, 2
    ).reshape(3, lat_count, per_device)
    source_row = column_ids // total_cols
    source_dev = source_row // band_rows
    source_local = (
        source_row % band_rows * band_cols + column_ids % total_cols - lon_index * band_cols
    )
    remote = source_dev != devices[:, None]
    matches = (source_dev[:, :, None] == devices[None, None, :]) & remote[:, :, None]
    slot_ranks = jnp.cumsum(matches.astype(jnp.int32), axis=1) - 1
    slot_of = jnp.sum(jnp.where(matches, slot_ranks, 0), axis=2)
    owned_here = remote & (source_dev == lat_index)
    sending = owned_here[:, :, None] & (slot_of[:, :, None] == slot_range[None, None, :])
    send_local = jnp.sum(jnp.where(sending, source_local[:, :, None], 0), axis=1)
    field_view = state_field.reshape(band_rows, 8, band_cols, 8, value_count)

    def pick_patches(local_index):
        picked = field_view[local_index // band_cols, :, local_index % band_cols]
        return picked.reshape(local_index.shape[0], 64, value_count)

    outgoing = pick_patches(send_local.reshape(-1)).reshape(lat_count, CAP, 64, value_count)
    my_dev = lax.dynamic_index_in_dim(source_dev, lat_index, 0, keepdims=False)
    my_slot = lax.dynamic_index_in_dim(slot_of, lat_index, 0, keepdims=False)
    my_local = lax.dynamic_index_in_dim(source_local, lat_index, 0, keepdims=False)
    my_remote = lax.dynamic_index_in_dim(remote, lat_index, 0, keepdims=False)
    my_frac = lax.dynamic_index_in_dim(fractions, lat_index, 1, keepdims=False)
    arrived = lax.all_to_all(outgoing, "lat", 0, 0, tiled=True).reshape(
        lat_count * CAP, 64, value_count
    )
    pick_index = my_dev * CAP + my_slot
    patches = jnp.where(my_remote[:, None, None], arrived[pick_index], pick_patches(my_local))
    return patches, my_frac


def local(tracers, shifts, diffusivity, source_patch):
    lat_count = lax.axis_size("lat")
    lat_index = lax.axis_index("lat")
    row_count, col_count, value_count = tracers.shape
    band_rows = row_count // 8
    band_cols = col_count // 8
    per_device = band_rows * band_cols
    per_level = value_count // LEV
    total_rows = row_count * lat_count
    weights = column_area(lat_index * row_count, row_count, total_rows)
    target_part = column_mass(tracers, weights)

    patches, frac = departed(tracers, source_patch[0], shifts[0])
    advected = from_patches(levels(spatial(patches, frac[0], frac[1]), frac[2]), band_rows, band_cols)
    first, k_wide = diffuse_first(advected, diffusivity)
    first_part = column_mass(first, weights)

    patches, frac = departed(first, source_patch[1], shifts[1])
    planar = spatial(patches, frac[0], frac[1])
    weight_z = cubic_matrix(frac[2], LEV)

    area_wide = column_area(lat_index * row_count - 1, row_count + 2, total_rows)
    flux = area_wide * k_wide
    g = weights - 2.0 * flux[1:-1] + flux[:-2] + flux[2:]
    g_cols = jnp.broadcast_to(g.reshape(band_rows, 1, 8, 1), (band_rows, band_cols, 8, 8))
    weighted = jnp.einsum(
        "pi,piv->pv", g_cols.reshape(per_device, 64), planar, precision=lax.Precision.HIGHEST
    ).reshape(per_device, LEV, per_level)
    mix_part = jnp.einsum(
        "plm,pmt->lmt", weight_z, weighted, precision=lax.Precision.HIGHEST
    )
    totals = all_sum(
        jnp.concatenate([target_part, first_part, mix_part.reshape(-1)]), ("lon", "lat")
    )
    target = totals[:value_count]
    first_mass = totals[value_count : 2 * value_count]
    mix = totals[2 * value_count :].reshape(LEV, LEV, per_level)
    first_ratio = target / first_mass
    second_mass = jnp.sum(first_ratio.reshape(LEV, per_level)[None] * mix, axis=1).reshape(
        value_count
    )
    second_ratio = target / second_mass
    advected = from_patches(
        levels(planar * first_ratio[None, None, :], frac[2]), band_rows, band_cols
    )
    return diffuse(advected, diffusivity, 0) * second_ratio[None, None, :]


def solution(mesh):
    return jax.shard_map(
        local,
        mesh=mesh,
        in_specs=(
            P(("groups", "lat"), "lon", None),
            P("groups", None, None, None),
            P("lat"),
            P("groups", None, None),
        ),
        out_specs=P(("groups", "lat"), "lon", None),
        check_vma=False,
    )
```

```python
import math

import jax
import jax.numpy as jnp
from jax import lax
from jax.sharding import PartitionSpec as P

LEV = 4
STEPS = 2
CAP = 4


def all_sum(value, axes, rider=None):
    rider_done = None
    for axis in axes:
        count = lax.axis_size(axis)
        if count & (count - 1):
            value = lax.psum(value, axis)
            continue
        distance = 1
        while distance < count:
            value = value + lax.ppermute(
                value, axis, [(i, i ^ distance) for i in range(count)]
            )
            if rider is not None:
                value, rider = lax.optimization_barrier((value, rider))
                rider_done, rider = rider, None
            distance *= 2
    if rider_done is None and rider is None:
        return value
    return value, rider if rider_done is None else rider_done


def neighbour_halos(lo_edge, hi_edge, axis, closed):
    count = lax.axis_size(axis)
    if count % 2:
        ends = count if closed else count - 1
        from_lo = lax.ppermute(hi_edge, axis, [(i, (i + 1) % count) for i in range(ends)])
        from_hi = lax.ppermute(lo_edge, axis, [((i + 1) % count, i) for i in range(ends)])
        return from_lo, from_hi
    even = lax.axis_index(axis) % 2 == 0
    first = lax.ppermute(
        jnp.where(even, hi_edge, lo_edge), axis, [(i, i ^ 1) for i in range(count)]
    )
    pairs = []
    for i in range(1, count, 2):
        if i + 1 < count:
            pairs += [(i, i + 1), (i + 1, i)]
        elif closed:
            pairs += [(i, 0), (0, i)]
    second = lax.ppermute(jnp.where(even, lo_edge, hi_edge), axis, pairs)
    return jnp.where(even, second, first), jnp.where(even, first, second)


def extended(cells, sides, width, closed):
    for axis, dim in sides:
        count = lax.axis_size(axis)
        ends = count if closed else count - 1
        head = lax.slice_in_dim(cells, 0, width, axis=dim)
        tail = lax.slice_in_dim(cells, cells.shape[dim] - width, cells.shape[dim], axis=dim)
        from_lo, from_hi = neighbour_halos(head, tail, axis, closed)
        cells = jnp.concatenate([from_lo, cells, from_hi], axis=dim)
    return cells


def cubic_weights(fraction):
    first_term = -fraction * (fraction - 1.0) * (fraction - 2.0) / 6.0
    second_term = (fraction + 1.0) * (fraction - 1.0) * (fraction - 2.0) / 2.0
    third_term = -(fraction + 1.0) * fraction * (fraction - 2.0) / 2.0
    fourth_term = (fraction + 1.0) * fraction * (fraction - 1.0) / 6.0
    return (first_term, second_term, third_term, fourth_term)


def cubic_matrix(fraction, extent):
    places = jnp.arange(extent)
    running = jnp.zeros(fraction.shape + (extent, extent), jnp.float32)
    for offset, weight in zip(range(-1, 3), cubic_weights(fraction)):
        target_col = jnp.clip(places + offset, 0, extent - 1)
        indicator = (target_col[:, None] == places[None, :]).astype(jnp.float32)
        running = running + weight[..., None, None] * indicator
    return running


def tap_sources(target, extent):
    return sorted({min(max(target + offset, 0), extent - 1) for offset in range(-1, 3)})


def plane_weights(fraction_y, fraction_x):
    rows = lax.broadcasted_iota(jnp.int32, (1, 64, 64), 1)
    cols = lax.broadcasted_iota(jnp.int32, (1, 64, 64), 2)

    def along(fraction, source, target):
        running = jnp.zeros((fraction.shape[0], 64, 64), jnp.float32)
        for offset, weight in zip(range(-1, 3), cubic_weights(fraction)):
            indicator = (jnp.clip(source + offset, 0, 7) == target).astype(jnp.float32)
            running = running + weight[:, None, None] * indicator
        return running

    return along(fraction_y, rows // 8, cols // 8) * along(fraction_x, rows % 8, cols % 8)


def spatial(patches, fraction_y, fraction_x):
    return jnp.einsum(
        "nij,njv->niv",
        plane_weights(fraction_y, fraction_x),
        patches,
        precision=lax.Precision.HIGHEST,
    )


def levels(flat, fraction_z):
    value_count = flat.shape[2]
    per_level = value_count // LEV
    weight_z = cubic_matrix(fraction_z, LEV)
    blocks = [flat[:, :, m * per_level : (m + 1) * per_level] for m in range(LEV)]
    out = []
    for level in range(LEV):
        acc = None
        for m in tap_sources(level, LEV):
            term = weight_z[:, level, m][:, None, None] * blocks[m]
            acc = term if acc is None else acc + term
        out.append(acc)
    return jnp.concatenate(out, axis=2)


def to_patches(state_field):
    band_rows = state_field.shape[0] // 8
    band_cols = state_field.shape[1] // 8
    return (
        state_field.reshape(band_rows, 8, band_cols, 8, -1)
        .transpose(0, 2, 1, 3, 4)
        .reshape(band_rows * band_cols, 64, -1)
    )


def from_patches(patches, band_rows, band_cols):
    return (
        patches.reshape(band_rows, band_cols, 8, 8, -1)
        .transpose(0, 2, 1, 3, 4)
        .reshape(band_rows * 8, band_cols * 8, -1)
    )


def column_area(first_row, row_count, total_rows):
    latitude = ((first_row + jnp.arange(row_count)).astype(jnp.float32) + 0.5) * (
        math.pi / total_rows
    ) - 0.5 * math.pi
    return jnp.cos(latitude)


def column_mass(state_field, weights):
    return jnp.sum(weights[:, None, None] * state_field, axis=(0, 1))


def diffuse(advected, diffusivity, row_dim):
    col_dim = row_dim + 1
    rows = advected.shape[row_dim]
    cols = advected.shape[col_dim]
    lon_wide = extended(advected, (("lon", col_dim),), 1, True)
    lat_wide = extended(advected, (("lat", row_dim),), 1, False)
    laplace = (
        lax.slice_in_dim(lat_wide, 2, rows + 2, axis=row_dim)
        + lax.slice_in_dim(lat_wide, 0, rows, axis=row_dim)
        + lax.slice_in_dim(lon_wide, 2, cols + 2, axis=col_dim)
        + lax.slice_in_dim(lon_wide, 0, cols, axis=col_dim)
        - 4.0 * advected
    )
    k_shape = [1] * advected.ndim
    k_shape[row_dim] = rows
    return advected + diffusivity.reshape(k_shape) * laplace


def diffuse_first(advected, diffusivity):
    rows, cols, value_count = advected.shape
    count = lax.axis_size("lat")

    def pack(row, number):
        return jnp.concatenate(
            [row, jnp.broadcast_to(number, (1, 1, value_count))], axis=1
        )

    from_above, from_below = neighbour_halos(
        pack(advected[:1], diffusivity[0]),
        pack(advected[rows - 1 :], diffusivity[rows - 1]),
        "lat",
        False,
    )
    lat_wide = jnp.concatenate([from_above[:, :cols], advected, from_below[:, :cols]], axis=0)
    k_wide = jnp.concatenate([from_above[0, cols, :1], diffusivity, from_below[0, cols, :1]])
    lon_wide = extended(advected, (("lon", 1),), 1, True)
    laplace = (
        lat_wide[2:] + lat_wide[:-2] + lon_wide[:, 2:] + lon_wide[:, :-2] - 4.0 * advected
    )
    return advected + diffusivity[:, None, None] * laplace, k_wide


def departed(state_field, source_ids, shifts_now):
    lat_count = lax.axis_size("lat")
    lat_index = lax.axis_index("lat")
    lon_index = lax.axis_index("lon")
    row_count, col_count, value_count = state_field.shape
    band_rows = row_count // 8
    band_cols = col_count // 8
    per_device = band_rows * band_cols
    total_cols = source_ids.shape[1]
    devices = jnp.arange(lat_count)
    slot_range = jnp.arange(CAP)
    column_ids = lax.dynamic_slice_in_dim(
        source_ids, lon_index * band_cols, band_cols, 1
    ).reshape(lat_count, per_device)
    fractions = lax.dynamic_slice_in_dim(
        shifts_now, lon_index * band_cols, band_cols, 2
    ).reshape(3, lat_count, per_device)
    source_row = column_ids // total_cols
    source_dev = source_row // band_rows
    source_local = (
        source_row % band_rows * band_cols + column_ids % total_cols - lon_index * band_cols
    )
    remote = source_dev != devices[:, None]
    matches = (source_dev[:, :, None] == devices[None, None, :]) & remote[:, :, None]
    slot_ranks = jnp.cumsum(matches.astype(jnp.int32), axis=1) - 1
    slot_of = jnp.sum(jnp.where(matches, slot_ranks, 0), axis=2)
    owned_here = remote & (source_dev == lat_index)
    sending = owned_here[:, :, None] & (slot_of[:, :, None] == slot_range[None, None, :])
    send_local = jnp.sum(jnp.where(sending, source_local[:, :, None], 0), axis=1)
    own_patches = to_patches(state_field)
    outgoing = own_patches[send_local.reshape(-1)].reshape(lat_count, CAP, 64, value_count)
    my_dev = lax.dynamic_index_in_dim(source_dev, lat_index, 0, keepdims=False)
    my_slot = lax.dynamic_index_in_dim(slot_of, lat_index, 0, keepdims=False)
    my_local = lax.dynamic_index_in_dim(source_local, lat_index, 0, keepdims=False)
    my_remote = lax.dynamic_index_in_dim(remote, lat_index, 0, keepdims=False)
    my_frac = lax.dynamic_index_in_dim(fractions, lat_index, 1, keepdims=False)
    arrived = lax.all_to_all(outgoing, "lat", 0, 0, tiled=True).reshape(
        lat_count * CAP, 64, value_count
    )
    pick_index = my_dev * CAP + my_slot
    patches = jnp.where(my_remote[:, None, None], arrived[pick_index], own_patches[my_local])
    return patches, my_frac


def local(tracers, shifts, diffusivity, source_patch):
    lat_count = lax.axis_size("lat")
    lat_index = lax.axis_index("lat")
    row_count, col_count, value_count = tracers.shape
    band_rows = row_count // 8
    band_cols = col_count // 8
    per_device = band_rows * band_cols
    per_level = value_count // LEV
    total_rows = row_count * lat_count
    weights = column_area(lat_index * row_count, row_count, total_rows)
    target_part = column_mass(tracers, weights)

    patches, frac = departed(tracers, source_patch[0], shifts[0])
    advected = from_patches(levels(spatial(patches, frac[0], frac[1]), frac[2]), band_rows, band_cols)
    first, k_wide = diffuse_first(advected, diffusivity)
    first_part = column_mass(first, weights)

    patches, frac = departed(first, source_patch[1], shifts[1])
    planar = spatial(patches, frac[0], frac[1])
    weight_z = cubic_matrix(frac[2], LEV)

    area_wide = column_area(lat_index * row_count - 1, row_count + 2, total_rows)
    flux = area_wide * k_wide
    g = weights - 2.0 * flux[1:-1] + flux[:-2] + flux[2:]
    g_cols = jnp.broadcast_to(g.reshape(band_rows, 1, 8, 1), (band_rows, band_cols, 8, 8))
    weighted = jnp.einsum(
        "pi,piv->pv", g_cols.reshape(per_device, 64), planar, precision=lax.Precision.HIGHEST
    ).reshape(per_device, LEV, per_level)
    mix_part = jnp.einsum(
        "plm,pmt->lmt", weight_z, weighted, precision=lax.Precision.HIGHEST
    )
    totals = all_sum(
        jnp.concatenate([target_part, first_part, mix_part.reshape(-1)]), ("lon", "lat")
    )
    target = totals[:value_count]
    first_mass = totals[value_count : 2 * value_count]
    mix = totals[2 * value_count :].reshape(LEV, LEV, per_level)
    first_ratio = target / first_mass
    second_mass = jnp.sum(first_ratio.reshape(LEV, per_level)[None] * mix, axis=1).reshape(
        value_count
    )
    second_ratio = target / second_mass
    advected = from_patches(
        levels(planar * first_ratio[None, None, :], frac[2]), band_rows, band_cols
    )
    return diffuse(advected, diffusivity, 0) * second_ratio[None, None, :]


def solution(mesh):
    return jax.shard_map(
        local,
        mesh=mesh,
        in_specs=(
            P(("groups", "lat"), "lon", None),
            P("groups", None, None, None),
            P("lat"),
            P("groups", None, None),
        ),
        out_specs=P(("groups", "lat"), "lon", None),
        check_vma=False,
    )
```

```python
import math

import jax
import jax.numpy as jnp
from jax import lax
from jax.sharding import PartitionSpec as P

LEV = 4
STEPS = 2
CAP = 4


def all_sum(value, axes, rider=None):
    rider_done = None
    for axis in axes:
        count = lax.axis_size(axis)
        if count & (count - 1):
            value = lax.psum(value, axis)
            continue
        distance = 1
        while distance < count:
            value = value + lax.ppermute(
                value, axis, [(i, i ^ distance) for i in range(count)]
            )
            if rider is not None:
                value, rider = lax.optimization_barrier((value, rider))
                rider_done, rider = rider, None
            distance *= 2
    if rider_done is None and rider is None:
        return value
    return value, rider if rider_done is None else rider_done


def neighbour_halos(lo_edge, hi_edge, axis, closed):
    count = lax.axis_size(axis)
    if count % 2:
        ends = count if closed else count - 1
        from_lo = lax.ppermute(hi_edge, axis, [(i, (i + 1) % count) for i in range(ends)])
        from_hi = lax.ppermute(lo_edge, axis, [((i + 1) % count, i) for i in range(ends)])
        return from_lo, from_hi
    even = lax.axis_index(axis) % 2 == 0
    first = lax.ppermute(
        jnp.where(even, hi_edge, lo_edge), axis, [(i, i ^ 1) for i in range(count)]
    )
    pairs = []
    for i in range(1, count, 2):
        if i + 1 < count:
            pairs += [(i, i + 1), (i + 1, i)]
        elif closed:
            pairs += [(i, 0), (0, i)]
    second = lax.ppermute(jnp.where(even, lo_edge, hi_edge), axis, pairs)
    return jnp.where(even, second, first), jnp.where(even, first, second)


def extended(cells, sides, width, closed):
    for axis, dim in sides:
        count = lax.axis_size(axis)
        ends = count if closed else count - 1
        head = lax.slice_in_dim(cells, 0, width, axis=dim)
        tail = lax.slice_in_dim(cells, cells.shape[dim] - width, cells.shape[dim], axis=dim)
        from_lo, from_hi = neighbour_halos(head, tail, axis, closed)
        cells = jnp.concatenate([from_lo, cells, from_hi], axis=dim)
    return cells


def cubic_weights(fraction):
    first_term = -fraction * (fraction - 1.0) * (fraction - 2.0) / 6.0
    second_term = (fraction + 1.0) * (fraction - 1.0) * (fraction - 2.0) / 2.0
    third_term = -(fraction + 1.0) * fraction * (fraction - 2.0) / 2.0
    fourth_term = (fraction + 1.0) * fraction * (fraction - 1.0) / 6.0
    return (first_term, second_term, third_term, fourth_term)


def cubic_matrix(fraction, extent):
    places = jnp.arange(extent)
    running = jnp.zeros(fraction.shape + (extent, extent), jnp.float32)
    for offset, weight in zip(range(-1, 3), cubic_weights(fraction)):
        target_col = jnp.clip(places + offset, 0, extent - 1)
        indicator = (target_col[:, None] == places[None, :]).astype(jnp.float32)
        running = running + weight[..., None, None] * indicator
    return running


def tap_sources(target, extent):
    return sorted({min(max(target + offset, 0), extent - 1) for offset in range(-1, 3)})


def plane_weights(fraction_y, fraction_x):
    rows = lax.broadcasted_iota(jnp.int32, (1, 64, 64), 1)
    cols = lax.broadcasted_iota(jnp.int32, (1, 64, 64), 2)

    def along(fraction, source, target):
        running = jnp.zeros((fraction.shape[0], 64, 64), jnp.float32)
        for offset, weight in zip(range(-1, 3), cubic_weights(fraction)):
            indicator = (jnp.clip(source + offset, 0, 7) == target).astype(jnp.float32)
            running = running + weight[:, None, None] * indicator
        return running

    return along(fraction_y, rows // 8, cols // 8) * along(fraction_x, rows % 8, cols % 8)


def spatial(patches, fraction_y, fraction_x):
    return jnp.einsum(
        "nij,njv->niv",
        plane_weights(fraction_y, fraction_x),
        patches,
        precision=lax.Precision.HIGHEST,
    )


def levels(flat, fraction_z):
    value_count = flat.shape[2]
    per_level = value_count // LEV
    weight_z = cubic_matrix(fraction_z, LEV)
    blocks = [flat[:, :, m * per_level : (m + 1) * per_level] for m in range(LEV)]
    out = []
    for level in range(LEV):
        acc = None
        for m in tap_sources(level, LEV):
            term = weight_z[:, level, m][:, None, None] * blocks[m]
            acc = term if acc is None else acc + term
        out.append(acc)
    return jnp.concatenate(out, axis=2)


def to_patches(state_field):
    band_rows = state_field.shape[0] // 8
    band_cols = state_field.shape[1] // 8
    return (
        state_field.reshape(band_rows, 8, band_cols, 8, -1)
        .transpose(0, 2, 1, 3, 4)
        .reshape(band_rows * band_cols, 64, -1)
    )


def from_patches(patches, band_rows, band_cols):
    return (
        patches.reshape(band_rows, band_cols, 8, 8, -1)
        .transpose(0, 2, 1, 3, 4)
        .reshape(band_rows * 8, band_cols * 8, -1)
    )


def column_area(first_row, row_count, total_rows):
    latitude = ((first_row + jnp.arange(row_count)).astype(jnp.float32) + 0.5) * (
        math.pi / total_rows
    ) - 0.5 * math.pi
    return jnp.cos(latitude)


def column_mass(state_field, weights):
    return jnp.sum(weights[:, None, None] * state_field, axis=(0, 1))


def diffuse(advected, diffusivity, row_dim):
    col_dim = row_dim + 1
    rows = advected.shape[row_dim]
    cols = advected.shape[col_dim]
    lon_wide = extended(advected, (("lon", col_dim),), 1, True)
    lat_wide = extended(advected, (("lat", row_dim),), 1, False)
    laplace = (
        lax.slice_in_dim(lat_wide, 2, rows + 2, axis=row_dim)
        + lax.slice_in_dim(lat_wide, 0, rows, axis=row_dim)
        + lax.slice_in_dim(lon_wide, 2, cols + 2, axis=col_dim)
        + lax.slice_in_dim(lon_wide, 0, cols, axis=col_dim)
        - 4.0 * advected
    )
    k_shape = [1] * advected.ndim
    k_shape[row_dim] = rows
    return advected + diffusivity.reshape(k_shape) * laplace


def diffuse_first(advected, diffusivity):
    rows, cols, value_count = advected.shape
    count = lax.axis_size("lat")

    def pack(row, number):
        return jnp.concatenate(
            [row, jnp.broadcast_to(number, (1, 1, value_count))], axis=1
        )

    from_above, from_below = neighbour_halos(
        pack(advected[:1], diffusivity[0]),
        pack(advected[rows - 1 :], diffusivity[rows - 1]),
        "lat",
        False,
    )
    lat_wide = jnp.concatenate([from_above[:, :cols], advected, from_below[:, :cols]], axis=0)
    k_wide = jnp.concatenate([from_above[0, cols, :1], diffusivity, from_below[0, cols, :1]])
    lon_wide = extended(advected, (("lon", 1),), 1, True)
    laplace = (
        lat_wide[2:] + lat_wide[:-2] + lon_wide[:, 2:] + lon_wide[:, :-2] - 4.0 * advected
    )
    return advected + diffusivity[:, None, None] * laplace, k_wide


def departed(state_field, source_ids, shifts_now):
    lat_count = lax.axis_size("lat")
    lat_index = lax.axis_index("lat")
    lon_index = lax.axis_index("lon")
    row_count, col_count, value_count = state_field.shape
    band_rows = row_count // 8
    band_cols = col_count // 8
    per_device = band_rows * band_cols
    total_cols = source_ids.shape[1]
    devices = jnp.arange(lat_count)
    slot_range = jnp.arange(CAP)
    column_ids = lax.dynamic_slice_in_dim(
        source_ids, lon_index * band_cols, band_cols, 1
    ).reshape(lat_count, per_device)
    fractions = lax.dynamic_slice_in_dim(
        shifts_now, lon_index * band_cols, band_cols, 2
    ).reshape(3, lat_count, per_device)
    source_row = column_ids // total_cols
    source_dev = source_row // band_rows
    source_local = (
        source_row % band_rows * band_cols + column_ids % total_cols - lon_index * band_cols
    )
    remote = source_dev != devices[:, None]
    matches = (source_dev[:, :, None] == devices[None, None, :]) & remote[:, :, None]
    slot_ranks = jnp.cumsum(matches.astype(jnp.int32), axis=1) - 1
    slot_of = jnp.sum(jnp.where(matches, slot_ranks, 0), axis=2)
    owned_here = remote & (source_dev == lat_index)
    sending = owned_here[:, :, None] & (slot_of[:, :, None] == slot_range[None, None, :])
    send_local = jnp.sum(jnp.where(sending, source_local[:, :, None], 0), axis=1)
    own_patches = to_patches(state_field)
    outgoing = own_patches[send_local.reshape(-1)].reshape(lat_count, CAP, 64, value_count)
    my_dev = lax.dynamic_index_in_dim(source_dev, lat_index, 0, keepdims=False)
    my_slot = lax.dynamic_index_in_dim(slot_of, lat_index, 0, keepdims=False)
    my_local = lax.dynamic_index_in_dim(source_local, lat_index, 0, keepdims=False)
    my_remote = lax.dynamic_index_in_dim(remote, lat_index, 0, keepdims=False)
    my_frac = lax.dynamic_index_in_dim(fractions, lat_index, 1, keepdims=False)
    arrived = lax.all_to_all(outgoing, "lat", 0, 0, tiled=True).reshape(
        lat_count * CAP, 64, value_count
    )
    pick_index = my_dev * CAP + my_slot
    take_near = (my_local[:, None] == jnp.arange(per_device)[None, :]) & ~my_remote[:, None]
    take_far = (pick_index[:, None] == jnp.arange(lat_count * CAP)[None, :]) & my_remote[:, None]
    patches = (
        jnp.dot(
            take_near.astype(jnp.float32),
            own_patches.reshape(per_device, -1),
            precision=lax.Precision.HIGHEST,
        )
        + jnp.dot(
            take_far.astype(jnp.float32),
            arrived.reshape(lat_count * CAP, -1),
            precision=lax.Precision.HIGHEST,
        )
    ).reshape(per_device, 64, value_count)
    return patches, my_frac


def local(tracers, shifts, diffusivity, source_patch):
    lat_count = lax.axis_size("lat")
    lat_index = lax.axis_index("lat")
    row_count, col_count, value_count = tracers.shape
    band_rows = row_count // 8
    band_cols = col_count // 8
    per_device = band_rows * band_cols
    per_level = value_count // LEV
    total_rows = row_count * lat_count
    weights = column_area(lat_index * row_count, row_count, total_rows)
    target_part = column_mass(tracers, weights)

    patches, frac = departed(tracers, source_patch[0], shifts[0])
    advected = from_patches(levels(spatial(patches, frac[0], frac[1]), frac[2]), band_rows, band_cols)
    first, k_wide = diffuse_first(advected, diffusivity)
    first_part = column_mass(first, weights)

    patches, frac = departed(first, source_patch[1], shifts[1])
    planar = spatial(patches, frac[0], frac[1])
    weight_z = cubic_matrix(frac[2], LEV)

    area_wide = column_area(lat_index * row_count - 1, row_count + 2, total_rows)
    flux = area_wide * k_wide
    g = weights - 2.0 * flux[1:-1] + flux[:-2] + flux[2:]
    g_cols = jnp.broadcast_to(g.reshape(band_rows, 1, 8, 1), (band_rows, band_cols, 8, 8))
    weighted = jnp.einsum(
        "pi,piv->pv", g_cols.reshape(per_device, 64), planar, precision=lax.Precision.HIGHEST
    ).reshape(per_device, LEV, per_level)
    mix_part = jnp.einsum(
        "plm,pmt->lmt", weight_z, weighted, precision=lax.Precision.HIGHEST
    )
    totals = all_sum(
        jnp.concatenate([target_part, first_part, mix_part.reshape(-1)]), ("lon", "lat")
    )
    target = totals[:value_count]
    first_mass = totals[value_count : 2 * value_count]
    mix = totals[2 * value_count :].reshape(LEV, LEV, per_level)
    first_ratio = target / first_mass
    second_mass = jnp.sum(first_ratio.reshape(LEV, per_level)[None] * mix, axis=1).reshape(
        value_count
    )
    second_ratio = target / second_mass
    advected = from_patches(
        levels(planar * first_ratio[None, None, :], frac[2]), band_rows, band_cols
    )
    return diffuse(advected, diffusivity, 0) * second_ratio[None, None, :]


def solution(mesh):
    return jax.shard_map(
        local,
        mesh=mesh,
        in_specs=(
            P(("groups", "lat"), "lon", None),
            P("groups", None, None, None),
            P("lat"),
            P("groups", None, None),
        ),
        out_specs=P(("groups", "lat"), "lon", None),
        check_vma=False,
    )
```

```python
import math

import jax
import jax.numpy as jnp
from jax import lax
from jax.sharding import PartitionSpec as P

LEV = 4
STEPS = 2
CAP = 4


def all_sum(value, axes, rider=None):
    rider_done = None
    for axis in axes:
        count = lax.axis_size(axis)
        if count & (count - 1):
            value = lax.psum(value, axis)
            continue
        distance = 1
        while distance < count:
            value = value + lax.ppermute(
                value, axis, [(i, i ^ distance) for i in range(count)]
            )
            if rider is not None:
                value, rider = lax.optimization_barrier((value, rider))
                rider_done, rider = rider, None
            distance *= 2
    if rider_done is None and rider is None:
        return value
    return value, rider if rider_done is None else rider_done


def neighbour_halos(lo_edge, hi_edge, axis, closed):
    count = lax.axis_size(axis)
    if count % 2:
        ends = count if closed else count - 1
        from_lo = lax.ppermute(hi_edge, axis, [(i, (i + 1) % count) for i in range(ends)])
        from_hi = lax.ppermute(lo_edge, axis, [((i + 1) % count, i) for i in range(ends)])
        return from_lo, from_hi
    even = lax.axis_index(axis) % 2 == 0
    first = lax.ppermute(
        jnp.where(even, hi_edge, lo_edge), axis, [(i, i ^ 1) for i in range(count)]
    )
    pairs = []
    for i in range(1, count, 2):
        if i + 1 < count:
            pairs += [(i, i + 1), (i + 1, i)]
        elif closed:
            pairs += [(i, 0), (0, i)]
    second = lax.ppermute(jnp.where(even, lo_edge, hi_edge), axis, pairs)
    return jnp.where(even, second, first), jnp.where(even, first, second)


def extended(cells, sides, width, closed):
    for axis, dim in sides:
        count = lax.axis_size(axis)
        ends = count if closed else count - 1
        head = lax.slice_in_dim(cells, 0, width, axis=dim)
        tail = lax.slice_in_dim(cells, cells.shape[dim] - width, cells.shape[dim], axis=dim)
        from_lo, from_hi = neighbour_halos(head, tail, axis, closed)
        cells = jnp.concatenate([from_lo, cells, from_hi], axis=dim)
    return cells


def cubic_weights(fraction):
    first_term = -fraction * (fraction - 1.0) * (fraction - 2.0) / 6.0
    second_term = (fraction + 1.0) * (fraction - 1.0) * (fraction - 2.0) / 2.0
    third_term = -(fraction + 1.0) * fraction * (fraction - 2.0) / 2.0
    fourth_term = (fraction + 1.0) * fraction * (fraction - 1.0) / 6.0
    return (first_term, second_term, third_term, fourth_term)


def cubic_matrix(fraction, extent):
    places = jnp.arange(extent)
    running = jnp.zeros(fraction.shape + (extent, extent), jnp.float32)
    for offset, weight in zip(range(-1, 3), cubic_weights(fraction)):
        target_col = jnp.clip(places + offset, 0, extent - 1)
        indicator = (target_col[:, None] == places[None, :]).astype(jnp.float32)
        running = running + weight[..., None, None] * indicator
    return running


def tap_sources(target, extent):
    return sorted({min(max(target + offset, 0), extent - 1) for offset in range(-1, 3)})


def plane_weights(fraction_y, fraction_x):
    rows = lax.broadcasted_iota(jnp.int32, (1, 64, 64), 1)
    cols = lax.broadcasted_iota(jnp.int32, (1, 64, 64), 2)

    def along(fraction, source, target):
        running = jnp.zeros((fraction.shape[0], 64, 64), jnp.float32)
        for offset, weight in zip(range(-1, 3), cubic_weights(fraction)):
            indicator = (jnp.clip(source + offset, 0, 7) == target).astype(jnp.float32)
            running = running + weight[:, None, None] * indicator
        return running

    return along(fraction_y, rows // 8, cols // 8) * along(fraction_x, rows % 8, cols % 8)


def spatial(patches, fraction_y, fraction_x):
    return jnp.einsum(
        "nij,njv->niv",
        plane_weights(fraction_y, fraction_x),
        patches,
        precision=lax.Precision.HIGHEST,
    )


def levels(flat, fraction_z):
    value_count = flat.shape[2]
    per_level = value_count // LEV
    weight_z = cubic_matrix(fraction_z, LEV)
    blocks = [flat[:, :, m * per_level : (m + 1) * per_level] for m in range(LEV)]
    out = []
    for level in range(LEV):
        acc = None
        for m in tap_sources(level, LEV):
            term = weight_z[:, level, m][:, None, None] * blocks[m]
            acc = term if acc is None else acc + term
        out.append(acc)
    return jnp.concatenate(out, axis=2)


def to_patches(state_field):
    band_rows = state_field.shape[0] // 8
    band_cols = state_field.shape[1] // 8
    return (
        state_field.reshape(band_rows, 8, band_cols, 8, -1)
        .transpose(0, 2, 1, 3, 4)
        .reshape(band_rows * band_cols, 64, -1)
    )


def from_patches(patches, band_rows, band_cols):
    return (
        patches.reshape(band_rows, band_cols, 8, 8, -1)
        .transpose(0, 2, 1, 3, 4)
        .reshape(band_rows * 8, band_cols * 8, -1)
    )


def column_area(first_row, row_count, total_rows):
    latitude = ((first_row + jnp.arange(row_count)).astype(jnp.float32) + 0.5) * (
        math.pi / total_rows
    ) - 0.5 * math.pi
    return jnp.cos(latitude)


def column_mass(state_field, weights):
    return jnp.sum(weights[:, None, None] * state_field, axis=(0, 1))


def diffuse(advected, diffusivity, row_dim):
    col_dim = row_dim + 1
    rows = advected.shape[row_dim]
    cols = advected.shape[col_dim]
    lon_wide = extended(advected, (("lon", col_dim),), 1, True)
    lat_wide = extended(advected, (("lat", row_dim),), 1, False)
    laplace = (
        lax.slice_in_dim(lat_wide, 2, rows + 2, axis=row_dim)
        + lax.slice_in_dim(lat_wide, 0, rows, axis=row_dim)
        + lax.slice_in_dim(lon_wide, 2, cols + 2, axis=col_dim)
        + lax.slice_in_dim(lon_wide, 0, cols, axis=col_dim)
        - 4.0 * advected
    )
    k_shape = [1] * advected.ndim
    k_shape[row_dim] = rows
    return advected + diffusivity.reshape(k_shape) * laplace


def diffuse_first(advected, diffusivity):
    rows, cols, value_count = advected.shape
    count = lax.axis_size("lat")

    def pack(row, number):
        return jnp.concatenate(
            [row, jnp.broadcast_to(number, (1, 1, value_count))], axis=1
        )

    from_above, from_below = neighbour_halos(
        pack(advected[:1], diffusivity[0]),
        pack(advected[rows - 1 :], diffusivity[rows - 1]),
        "lat",
        False,
    )
    lat_wide = jnp.concatenate([from_above[:, :cols], advected, from_below[:, :cols]], axis=0)
    k_wide = jnp.concatenate([from_above[0, cols, :1], diffusivity, from_below[0, cols, :1]])
    lon_wide = extended(advected, (("lon", 1),), 1, True)
    laplace = (
        lat_wide[2:] + lat_wide[:-2] + lon_wide[:, 2:] + lon_wide[:, :-2] - 4.0 * advected
    )
    return advected + diffusivity[:, None, None] * laplace, k_wide


def departed(state_field, source_ids, shifts_now):
    lat_count = lax.axis_size("lat")
    lat_index = lax.axis_index("lat")
    lon_index = lax.axis_index("lon")
    row_count, col_count, value_count = state_field.shape
    band_rows = row_count // 8
    band_cols = col_count // 8
    per_device = band_rows * band_cols
    total_cols = source_ids.shape[1]
    devices = jnp.arange(lat_count)
    slot_range = jnp.arange(CAP)
    column_ids = lax.dynamic_slice_in_dim(
        source_ids, lon_index * band_cols, band_cols, 1
    ).reshape(lat_count, per_device)
    fractions = lax.dynamic_slice_in_dim(
        shifts_now, lon_index * band_cols, band_cols, 2
    ).reshape(3, lat_count, per_device)
    source_row = column_ids // total_cols
    source_dev = source_row // band_rows
    source_local = (
        source_row % band_rows * band_cols + column_ids % total_cols - lon_index * band_cols
    )
    remote = source_dev != devices[:, None]
    matches = (source_dev[:, :, None] == devices[None, None, :]) & remote[:, :, None]
    slot_ranks = jnp.cumsum(matches.astype(jnp.int32), axis=1) - 1
    slot_of = jnp.sum(jnp.where(matches, slot_ranks, 0), axis=2)
    owned_here = remote & (source_dev == lat_index)
    sending = owned_here[:, :, None] & (slot_of[:, :, None] == slot_range[None, None, :])
    send_local = jnp.sum(jnp.where(sending, source_local[:, :, None], 0), axis=1)
    own_patches = to_patches(state_field)
    send_flat = send_local.reshape(-1)
    outgoing = jnp.dot(
        (send_flat[:, None] == jnp.arange(per_device)[None, :]).astype(jnp.float32),
        own_patches.reshape(per_device, -1),
        precision=lax.Precision.HIGHEST,
    ).reshape(lat_count, CAP, 64, value_count)
    my_dev = lax.dynamic_index_in_dim(source_dev, lat_index, 0, keepdims=False)
    my_slot = lax.dynamic_index_in_dim(slot_of, lat_index, 0, keepdims=False)
    my_local = lax.dynamic_index_in_dim(source_local, lat_index, 0, keepdims=False)
    my_remote = lax.dynamic_index_in_dim(remote, lat_index, 0, keepdims=False)
    my_frac = lax.dynamic_index_in_dim(fractions, lat_index, 1, keepdims=False)
    arrived = lax.all_to_all(outgoing, "lat", 0, 0, tiled=True).reshape(
        lat_count * CAP, 64, value_count
    )
    pick_index = my_dev * CAP + my_slot
    take_near = (my_local[:, None] == jnp.arange(per_device)[None, :]) & ~my_remote[:, None]
    take_far = (pick_index[:, None] == jnp.arange(lat_count * CAP)[None, :]) & my_remote[:, None]
    patches = (
        jnp.dot(
            take_near.astype(jnp.float32),
            own_patches.reshape(per_device, -1),
            precision=lax.Precision.HIGHEST,
        )
        + jnp.dot(
            take_far.astype(jnp.float32),
            arrived.reshape(lat_count * CAP, -1),
            precision=lax.Precision.HIGHEST,
        )
    ).reshape(per_device, 64, value_count)
    return patches, my_frac


def local(tracers, shifts, diffusivity, source_patch):
    lat_count = lax.axis_size("lat")
    lat_index = lax.axis_index("lat")
    row_count, col_count, value_count = tracers.shape
    band_rows = row_count // 8
    band_cols = col_count // 8
    per_device = band_rows * band_cols
    per_level = value_count // LEV
    total_rows = row_count * lat_count
    weights = column_area(lat_index * row_count, row_count, total_rows)
    target_part = column_mass(tracers, weights)

    patches, frac = departed(tracers, source_patch[0], shifts[0])
    advected = from_patches(levels(spatial(patches, frac[0], frac[1]), frac[2]), band_rows, band_cols)
    first, k_wide = diffuse_first(advected, diffusivity)
    first_part = column_mass(first, weights)

    patches, frac = departed(first, source_patch[1], shifts[1])
    planar = spatial(patches, frac[0], frac[1])
    weight_z = cubic_matrix(frac[2], LEV)

    area_wide = column_area(lat_index * row_count - 1, row_count + 2, total_rows)
    flux = area_wide * k_wide
    g = weights - 2.0 * flux[1:-1] + flux[:-2] + flux[2:]
    g_cols = jnp.broadcast_to(g.reshape(band_rows, 1, 8, 1), (band_rows, band_cols, 8, 8))
    weighted = jnp.einsum(
        "pi,piv->pv", g_cols.reshape(per_device, 64), planar, precision=lax.Precision.HIGHEST
    ).reshape(per_device, LEV, per_level)
    mix_part = jnp.einsum(
        "plm,pmt->lmt", weight_z, weighted, precision=lax.Precision.HIGHEST
    )
    totals = all_sum(
        jnp.concatenate([target_part, first_part, mix_part.reshape(-1)]), ("lon", "lat")
    )
    target = totals[:value_count]
    first_mass = totals[value_count : 2 * value_count]
    mix = totals[2 * value_count :].reshape(LEV, LEV, per_level)
    first_ratio = target / first_mass
    second_mass = jnp.sum(first_ratio.reshape(LEV, per_level)[None] * mix, axis=1).reshape(
        value_count
    )
    second_ratio = target / second_mass
    advected = from_patches(
        levels(planar * first_ratio[None, None, :], frac[2]), band_rows, band_cols
    )
    return diffuse(advected, diffusivity, 0) * second_ratio[None, None, :]


def solution(mesh):
    return jax.shard_map(
        local,
        mesh=mesh,
        in_specs=(
            P(("groups", "lat"), "lon", None),
            P("groups", None, None, None),
            P("lat"),
            P("groups", None, None),
        ),
        out_specs=P(("groups", "lat"), "lon", None),
        check_vma=False,
    )
```

```python
import math

import jax
import jax.numpy as jnp
from jax import lax
from jax.sharding import PartitionSpec as P

LEV = 4
STEPS = 2
CAP = 4


def all_sum(value, axes, rider=None):
    rider_done = None
    for axis in axes:
        count = lax.axis_size(axis)
        if count & (count - 1):
            value = lax.psum(value, axis)
            continue
        distance = 1
        while distance < count:
            value = value + lax.ppermute(
                value, axis, [(i, i ^ distance) for i in range(count)]
            )
            if rider is not None:
                value, rider = lax.optimization_barrier((value, rider))
                rider_done, rider = rider, None
            distance *= 2
    if rider_done is None and rider is None:
        return value
    return value, rider if rider_done is None else rider_done


def neighbour_halos(lo_edge, hi_edge, axis, closed):
    count = lax.axis_size(axis)
    if count % 2:
        ends = count if closed else count - 1
        from_lo = lax.ppermute(hi_edge, axis, [(i, (i + 1) % count) for i in range(ends)])
        from_hi = lax.ppermute(lo_edge, axis, [((i + 1) % count, i) for i in range(ends)])
        return from_lo, from_hi
    even = lax.axis_index(axis) % 2 == 0
    first = lax.ppermute(
        jnp.where(even, hi_edge, lo_edge), axis, [(i, i ^ 1) for i in range(count)]
    )
    pairs = []
    for i in range(1, count, 2):
        if i + 1 < count:
            pairs += [(i, i + 1), (i + 1, i)]
        elif closed:
            pairs += [(i, 0), (0, i)]
    second = lax.ppermute(jnp.where(even, lo_edge, hi_edge), axis, pairs)
    return jnp.where(even, second, first), jnp.where(even, first, second)


def extended(cells, sides, width, closed):
    for axis, dim in sides:
        count = lax.axis_size(axis)
        ends = count if closed else count - 1
        head = lax.slice_in_dim(cells, 0, width, axis=dim)
        tail = lax.slice_in_dim(cells, cells.shape[dim] - width, cells.shape[dim], axis=dim)
        from_lo, from_hi = neighbour_halos(head, tail, axis, closed)
        cells = jnp.concatenate([from_lo, cells, from_hi], axis=dim)
    return cells


def cubic_weights(fraction):
    first_term = -fraction * (fraction - 1.0) * (fraction - 2.0) / 6.0
    second_term = (fraction + 1.0) * (fraction - 1.0) * (fraction - 2.0) / 2.0
    third_term = -(fraction + 1.0) * fraction * (fraction - 2.0) / 2.0
    fourth_term = (fraction + 1.0) * fraction * (fraction - 1.0) / 6.0
    return (first_term, second_term, third_term, fourth_term)


def cubic_matrix(fraction, extent):
    places = jnp.arange(extent)
    running = jnp.zeros(fraction.shape + (extent, extent), jnp.float32)
    for offset, weight in zip(range(-1, 3), cubic_weights(fraction)):
        target_col = jnp.clip(places + offset, 0, extent - 1)
        indicator = (target_col[:, None] == places[None, :]).astype(jnp.float32)
        running = running + weight[..., None, None] * indicator
    return running


def tap_sources(target, extent):
    return sorted({min(max(target + offset, 0), extent - 1) for offset in range(-1, 3)})


def plane_weights(fraction_y, fraction_x):
    rows = lax.broadcasted_iota(jnp.int32, (1, 64, 64), 1)
    cols = lax.broadcasted_iota(jnp.int32, (1, 64, 64), 2)

    def along(fraction, source, target):
        running = jnp.zeros((fraction.shape[0], 64, 64), jnp.float32)
        for offset, weight in zip(range(-1, 3), cubic_weights(fraction)):
            indicator = (jnp.clip(source + offset, 0, 7) == target).astype(jnp.float32)
            running = running + weight[:, None, None] * indicator
        return running

    return along(fraction_y, rows // 8, cols // 8) * along(fraction_x, rows % 8, cols % 8)


def spatial(patches, fraction_y, fraction_x):
    return jnp.einsum(
        "nij,njv->niv",
        plane_weights(fraction_y, fraction_x),
        patches,
        precision=lax.Precision.HIGHEST,
    )


def levels(flat, fraction_z):
    value_count = flat.shape[2]
    per_level = value_count // LEV
    weight_z = cubic_matrix(fraction_z, LEV)
    blocks = [flat[:, :, m * per_level : (m + 1) * per_level] for m in range(LEV)]
    out = []
    for level in range(LEV):
        acc = None
        for m in tap_sources(level, LEV):
            term = weight_z[:, level, m][:, None, None] * blocks[m]
            acc = term if acc is None else acc + term
        out.append(acc)
    return jnp.concatenate(out, axis=2)


def to_patches(state_field):
    band_rows = state_field.shape[0] // 8
    band_cols = state_field.shape[1] // 8
    return (
        state_field.reshape(band_rows, 8, band_cols, 8, -1)
        .transpose(0, 2, 1, 3, 4)
        .reshape(band_rows * band_cols, 64, -1)
    )


def from_patches(patches, band_rows, band_cols):
    return (
        patches.reshape(band_rows, band_cols, 8, 8, -1)
        .transpose(0, 2, 1, 3, 4)
        .reshape(band_rows * 8, band_cols * 8, -1)
    )


def column_area(first_row, row_count, total_rows):
    latitude = ((first_row + jnp.arange(row_count)).astype(jnp.float32) + 0.5) * (
        math.pi / total_rows
    ) - 0.5 * math.pi
    return jnp.cos(latitude)


def column_mass(state_field, weights):
    return jnp.sum(weights[:, None, None] * state_field, axis=(0, 1))


def diffuse(advected, diffusivity, row_dim):
    col_dim = row_dim + 1
    rows = advected.shape[row_dim]
    cols = advected.shape[col_dim]
    lon_wide = extended(advected, (("lon", col_dim),), 1, True)
    lat_wide = extended(advected, (("lat", row_dim),), 1, False)
    laplace = (
        lax.slice_in_dim(lat_wide, 2, rows + 2, axis=row_dim)
        + lax.slice_in_dim(lat_wide, 0, rows, axis=row_dim)
        + lax.slice_in_dim(lon_wide, 2, cols + 2, axis=col_dim)
        + lax.slice_in_dim(lon_wide, 0, cols, axis=col_dim)
        - 4.0 * advected
    )
    k_shape = [1] * advected.ndim
    k_shape[row_dim] = rows
    return advected + diffusivity.reshape(k_shape) * laplace


def diffuse_first(advected, diffusivity):
    rows, cols, value_count = advected.shape
    count = lax.axis_size("lat")

    def pack(row, number):
        return jnp.concatenate(
            [row, jnp.broadcast_to(number, (1, 1, value_count))], axis=1
        )

    from_above, from_below = neighbour_halos(
        pack(advected[:1], diffusivity[0]),
        pack(advected[rows - 1 :], diffusivity[rows - 1]),
        "lat",
        False,
    )
    lat_wide = jnp.concatenate([from_above[:, :cols], advected, from_below[:, :cols]], axis=0)
    k_wide = jnp.concatenate([from_above[0, cols, :1], diffusivity, from_below[0, cols, :1]])
    lon_wide = extended(advected, (("lon", 1),), 1, True)
    laplace = (
        lat_wide[2:] + lat_wide[:-2] + lon_wide[:, 2:] + lon_wide[:, :-2] - 4.0 * advected
    )
    return advected + diffusivity[:, None, None] * laplace, k_wide


def departed(state_field, source_ids, shifts_now):
    lat_count = lax.axis_size("lat")
    lat_index = lax.axis_index("lat")
    lon_index = lax.axis_index("lon")
    row_count, col_count, value_count = state_field.shape
    band_rows = row_count // 8
    band_cols = col_count // 8
    per_device = band_rows * band_cols
    total_cols = source_ids.shape[1]
    devices = jnp.arange(lat_count)
    slot_range = jnp.arange(CAP)
    column_ids = lax.dynamic_slice_in_dim(
        source_ids, lon_index * band_cols, band_cols, 1
    ).reshape(lat_count, per_device)
    fractions = lax.dynamic_slice_in_dim(
        shifts_now, lon_index * band_cols, band_cols, 2
    ).reshape(3, lat_count, per_device)
    source_row = column_ids // total_cols
    source_dev = source_row // band_rows
    source_local = (
        source_row % band_rows * band_cols + column_ids % total_cols - lon_index * band_cols
    )
    remote = source_dev != devices[:, None]
    matches = (source_dev[:, :, None] == devices[None, None, :]) & remote[:, :, None]
    slot_ranks = jnp.cumsum(matches.astype(jnp.int32), axis=1) - 1
    slot_of = jnp.sum(jnp.where(matches, slot_ranks, 0), axis=2)
    owned_here = remote & (source_dev == lat_index)
    sending = owned_here[:, :, None] & (slot_of[:, :, None] == slot_range[None, None, :])
    send_local = jnp.sum(jnp.where(sending, source_local[:, :, None], 0), axis=1)
    own_patches = to_patches(state_field)
    outgoing = own_patches[send_local.reshape(-1)].reshape(lat_count, CAP, 64, value_count)
    my_dev = lax.dynamic_index_in_dim(source_dev, lat_index, 0, keepdims=False)
    my_slot = lax.dynamic_index_in_dim(slot_of, lat_index, 0, keepdims=False)
    my_local = lax.dynamic_index_in_dim(source_local, lat_index, 0, keepdims=False)
    my_remote = lax.dynamic_index_in_dim(remote, lat_index, 0, keepdims=False)
    my_frac = lax.dynamic_index_in_dim(fractions, lat_index, 1, keepdims=False)
    arrived = lax.all_to_all(outgoing, "lat", 0, 0, tiled=True).reshape(
        lat_count * CAP, 64, value_count
    )
    pick_index = my_dev * CAP + my_slot
    take_near = (my_local[:, None] == jnp.arange(per_device)[None, :]) & ~my_remote[:, None]
    take_far = (pick_index[:, None] == jnp.arange(lat_count * CAP)[None, :]) & my_remote[:, None]
    patches = (
        jnp.dot(
            take_near.astype(jnp.float32),
            own_patches.reshape(per_device, -1),
            precision=lax.Precision.HIGHEST,
        )
        + jnp.dot(
            take_far.astype(jnp.float32),
            arrived.reshape(lat_count * CAP, -1),
            precision=lax.Precision.HIGHEST,
        )
    ).reshape(per_device, 64, value_count)
    return patches, my_frac


def local(tracers, shifts, diffusivity, source_patch):
    lat_count = lax.axis_size("lat")
    lat_index = lax.axis_index("lat")
    row_count, col_count, value_count = tracers.shape
    band_rows = row_count // 8
    band_cols = col_count // 8
    per_device = band_rows * band_cols
    per_level = value_count // LEV
    total_rows = row_count * lat_count
    weights = column_area(lat_index * row_count, row_count, total_rows)
    target_part = column_mass(tracers, weights)

    patches, frac = departed(tracers, source_patch[0], shifts[0])
    advected = from_patches(levels(spatial(patches, frac[0], frac[1]), frac[2]), band_rows, band_cols)
    first, k_wide = diffuse_first(advected, diffusivity)
    first_part = column_mass(first, weights)

    patches, frac = departed(first, source_patch[1], shifts[1])
    planar = spatial(patches, frac[0], frac[1])
    weight_z = cubic_matrix(frac[2], LEV)

    area_wide = column_area(lat_index * row_count - 1, row_count + 2, total_rows)
    flux = area_wide * k_wide
    g = weights - 2.0 * flux[1:-1] + flux[:-2] + flux[2:]
    g_cols = jnp.broadcast_to(g.reshape(band_rows, 1, 8, 1), (band_rows, band_cols, 8, 8))
    weighted = jnp.einsum(
        "pi,piv->pv", g_cols.reshape(per_device, 64), planar, precision=lax.Precision.HIGHEST
    ).reshape(per_device, LEV, per_level)
    mix_part = jnp.einsum(
        "plm,pmt->lmt", weight_z, weighted, precision=lax.Precision.HIGHEST
    )
    partial = jnp.concatenate([target_part, first_part, mix_part.reshape(-1)])
    members = lat_count * lax.axis_size("lon")
    totals = jnp.sum(
        lax.all_to_all(
            jnp.broadcast_to(partial, (members,) + partial.shape), ("lat", "lon"), 0, 0, tiled=True
        ),
        axis=0,
    )
    target = totals[:value_count]
    first_mass = totals[value_count : 2 * value_count]
    mix = totals[2 * value_count :].reshape(LEV, LEV, per_level)
    first_ratio = target / first_mass
    second_mass = jnp.sum(first_ratio.reshape(LEV, per_level)[None] * mix, axis=1).reshape(
        value_count
    )
    second_ratio = target / second_mass
    advected = from_patches(
        levels(planar * first_ratio[None, None, :], frac[2]), band_rows, band_cols
    )
    return diffuse(advected, diffusivity, 0) * second_ratio[None, None, :]


def solution(mesh):
    return jax.shard_map(
        local,
        mesh=mesh,
        in_specs=(
            P(("groups", "lat"), "lon", None),
            P("groups", None, None, None),
            P("lat"),
            P("groups", None, None),
        ),
        out_specs=P(("groups", "lat"), "lon", None),
        check_vma=False,
    )
```

```python
import math

import jax
import jax.numpy as jnp
from jax import lax
from jax.sharding import PartitionSpec as P

LEV = 4
STEPS = 2
CAP = 4


def all_sum(value, axes, rider=None):
    rider_done = None
    for axis in axes:
        count = lax.axis_size(axis)
        if count & (count - 1):
            value = lax.psum(value, axis)
            continue
        distance = 1
        while distance < count:
            value = value + lax.ppermute(
                value, axis, [(i, i ^ distance) for i in range(count)]
            )
            if rider is not None:
                value, rider = lax.optimization_barrier((value, rider))
                rider_done, rider = rider, None
            distance *= 2
    if rider_done is None and rider is None:
        return value
    return value, rider if rider_done is None else rider_done


def neighbour_halos(lo_edge, hi_edge, axis, closed):
    count = lax.axis_size(axis)
    if count % 2:
        ends = count if closed else count - 1
        from_lo = lax.ppermute(hi_edge, axis, [(i, (i + 1) % count) for i in range(ends)])
        from_hi = lax.ppermute(lo_edge, axis, [((i + 1) % count, i) for i in range(ends)])
        return from_lo, from_hi
    even = lax.axis_index(axis) % 2 == 0
    first = lax.ppermute(
        jnp.where(even, hi_edge, lo_edge), axis, [(i, i ^ 1) for i in range(count)]
    )
    pairs = []
    for i in range(1, count, 2):
        if i + 1 < count:
            pairs += [(i, i + 1), (i + 1, i)]
        elif closed:
            pairs += [(i, 0), (0, i)]
    second = lax.ppermute(jnp.where(even, lo_edge, hi_edge), axis, pairs)
    return jnp.where(even, second, first), jnp.where(even, first, second)


def extended(cells, sides, width, closed):
    for axis, dim in sides:
        count = lax.axis_size(axis)
        ends = count if closed else count - 1
        head = lax.slice_in_dim(cells, 0, width, axis=dim)
        tail = lax.slice_in_dim(cells, cells.shape[dim] - width, cells.shape[dim], axis=dim)
        from_lo, from_hi = neighbour_halos(head, tail, axis, closed)
        cells = jnp.concatenate([from_lo, cells, from_hi], axis=dim)
    return cells


def cubic_weights(fraction):
    first_term = -fraction * (fraction - 1.0) * (fraction - 2.0) / 6.0
    second_term = (fraction + 1.0) * (fraction - 1.0) * (fraction - 2.0) / 2.0
    third_term = -(fraction + 1.0) * fraction * (fraction - 2.0) / 2.0
    fourth_term = (fraction + 1.0) * fraction * (fraction - 1.0) / 6.0
    return (first_term, second_term, third_term, fourth_term)


def cubic_matrix(fraction, extent):
    places = jnp.arange(extent)
    running = jnp.zeros(fraction.shape + (extent, extent), jnp.float32)
    for offset, weight in zip(range(-1, 3), cubic_weights(fraction)):
        target_col = jnp.clip(places + offset, 0, extent - 1)
        indicator = (target_col[:, None] == places[None, :]).astype(jnp.float32)
        running = running + weight[..., None, None] * indicator
    return running


def tap_sources(target, extent):
    return sorted({min(max(target + offset, 0), extent - 1) for offset in range(-1, 3)})


def plane_weights(fraction_y, fraction_x):
    rows = lax.broadcasted_iota(jnp.int32, (1, 64, 64), 1)
    cols = lax.broadcasted_iota(jnp.int32, (1, 64, 64), 2)

    def along(fraction, source, target):
        running = jnp.zeros((fraction.shape[0], 64, 64), jnp.float32)
        for offset, weight in zip(range(-1, 3), cubic_weights(fraction)):
            indicator = (jnp.clip(source + offset, 0, 7) == target).astype(jnp.float32)
            running = running + weight[:, None, None] * indicator
        return running

    return along(fraction_y, rows // 8, cols // 8) * along(fraction_x, rows % 8, cols % 8)


def spatial(patches, fraction_y, fraction_x):
    return jnp.einsum(
        "nij,njv->niv",
        plane_weights(fraction_y, fraction_x),
        patches,
        precision=lax.Precision.HIGHEST,
    )


def levels(flat, fraction_z):
    value_count = flat.shape[2]
    per_level = value_count // LEV
    weight_z = cubic_matrix(fraction_z, LEV)
    blocks = [flat[:, :, m * per_level : (m + 1) * per_level] for m in range(LEV)]
    out = []
    for level in range(LEV):
        acc = None
        for m in tap_sources(level, LEV):
            term = weight_z[:, level, m][:, None, None] * blocks[m]
            acc = term if acc is None else acc + term
        out.append(acc)
    return jnp.concatenate(out, axis=2)


def to_patches(state_field):
    band_rows = state_field.shape[0] // 8
    band_cols = state_field.shape[1] // 8
    return (
        state_field.reshape(band_rows, 8, band_cols, 8, -1)
        .transpose(0, 2, 1, 3, 4)
        .reshape(band_rows * band_cols, 64, -1)
    )


def from_patches(patches, band_rows, band_cols):
    return (
        patches.reshape(band_rows, band_cols, 8, 8, -1)
        .transpose(0, 2, 1, 3, 4)
        .reshape(band_rows * 8, band_cols * 8, -1)
    )


def column_area(first_row, row_count, total_rows):
    latitude = ((first_row + jnp.arange(row_count)).astype(jnp.float32) + 0.5) * (
        math.pi / total_rows
    ) - 0.5 * math.pi
    return jnp.cos(latitude)


def column_mass(state_field, weights):
    return jnp.sum(weights[:, None, None] * state_field, axis=(0, 1))


def diffuse(advected, diffusivity, row_dim):
    col_dim = row_dim + 1
    rows = advected.shape[row_dim]
    cols = advected.shape[col_dim]
    lon_wide = extended(advected, (("lon", col_dim),), 1, True)
    lat_wide = extended(advected, (("lat", row_dim),), 1, False)
    laplace = (
        lax.slice_in_dim(lat_wide, 2, rows + 2, axis=row_dim)
        + lax.slice_in_dim(lat_wide, 0, rows, axis=row_dim)
        + lax.slice_in_dim(lon_wide, 2, cols + 2, axis=col_dim)
        + lax.slice_in_dim(lon_wide, 0, cols, axis=col_dim)
        - 4.0 * advected
    )
    k_shape = [1] * advected.ndim
    k_shape[row_dim] = rows
    return advected + diffusivity.reshape(k_shape) * laplace


def levels_cols(values, weight_z):
    value_count = values.shape[-1]
    per_level = value_count // LEV
    blocks = [values[..., m * per_level : (m + 1) * per_level] for m in range(LEV)]
    out = []
    for level in range(LEV):
        acc = None
        for m in tap_sources(level, LEV):
            term = weight_z[..., level, m][..., None] * blocks[m]
            acc = term if acc is None else acc + term
        out.append(acc)
    return jnp.concatenate(out, axis=-1)


def diffuse_first(advected, diffusivity):
    rows, cols, value_count = advected.shape
    count = lax.axis_size("lat")

    def pack(row, number):
        return jnp.concatenate(
            [row, jnp.broadcast_to(number, (1, 1, value_count))], axis=1
        )

    from_above, from_below = neighbour_halos(
        pack(advected[:1], diffusivity[0]),
        pack(advected[rows - 1 :], diffusivity[rows - 1]),
        "lat",
        False,
    )
    lat_wide = jnp.concatenate([from_above[:, :cols], advected, from_below[:, :cols]], axis=0)
    k_wide = jnp.concatenate([from_above[0, cols, :1], diffusivity, from_below[0, cols, :1]])
    lon_wide = extended(advected, (("lon", 1),), 1, True)
    laplace = (
        lat_wide[2:] + lat_wide[:-2] + lon_wide[:, 2:] + lon_wide[:, :-2] - 4.0 * advected
    )
    return advected + diffusivity[:, None, None] * laplace, k_wide


def departed(state_field, source_ids, shifts_now):
    lat_count = lax.axis_size("lat")
    lat_index = lax.axis_index("lat")
    lon_index = lax.axis_index("lon")
    row_count, col_count, value_count = state_field.shape
    band_rows = row_count // 8
    band_cols = col_count // 8
    per_device = band_rows * band_cols
    total_cols = source_ids.shape[1]
    devices = jnp.arange(lat_count)
    slot_range = jnp.arange(CAP)
    column_ids = lax.dynamic_slice_in_dim(
        source_ids, lon_index * band_cols, band_cols, 1
    ).reshape(lat_count, per_device)
    fractions = lax.dynamic_slice_in_dim(
        shifts_now, lon_index * band_cols, band_cols, 2
    ).reshape(3, lat_count, per_device)
    source_row = column_ids // total_cols
    source_dev = source_row // band_rows
    source_local = (
        source_row % band_rows * band_cols + column_ids % total_cols - lon_index * band_cols
    )
    remote = source_dev != devices[:, None]
    matches = (source_dev[:, :, None] == devices[None, None, :]) & remote[:, :, None]
    slot_ranks = jnp.cumsum(matches.astype(jnp.int32), axis=1) - 1
    slot_of = jnp.sum(jnp.where(matches, slot_ranks, 0), axis=2)
    owned_here = remote & (source_dev == lat_index)
    sending = owned_here[:, :, None] & (slot_of[:, :, None] == slot_range[None, None, :])
    send_local = jnp.sum(jnp.where(sending, source_local[:, :, None], 0), axis=1)
    own_patches = to_patches(state_field)
    outgoing = own_patches[send_local.reshape(-1)].reshape(lat_count, CAP, 64, value_count)
    my_dev = lax.dynamic_index_in_dim(source_dev, lat_index, 0, keepdims=False)
    my_slot = lax.dynamic_index_in_dim(slot_of, lat_index, 0, keepdims=False)
    my_local = lax.dynamic_index_in_dim(source_local, lat_index, 0, keepdims=False)
    my_remote = lax.dynamic_index_in_dim(remote, lat_index, 0, keepdims=False)
    my_frac = lax.dynamic_index_in_dim(fractions, lat_index, 1, keepdims=False)
    arrived = lax.all_to_all(outgoing, "lat", 0, 0, tiled=True).reshape(
        lat_count * CAP, 64, value_count
    )
    pick_index = my_dev * CAP + my_slot
    take_near = (my_local[:, None] == jnp.arange(per_device)[None, :]) & ~my_remote[:, None]
    take_far = (pick_index[:, None] == jnp.arange(lat_count * CAP)[None, :]) & my_remote[:, None]
    patches = (
        jnp.dot(
            take_near.astype(jnp.float32),
            own_patches.reshape(per_device, -1),
            precision=lax.Precision.HIGHEST,
        )
        + jnp.dot(
            take_far.astype(jnp.float32),
            arrived.reshape(lat_count * CAP, -1),
            precision=lax.Precision.HIGHEST,
        )
    ).reshape(per_device, 64, value_count)
    return patches, my_frac


def local(tracers, shifts, diffusivity, source_patch):
    lat_count = lax.axis_size("lat")
    lat_index = lax.axis_index("lat")
    row_count, col_count, value_count = tracers.shape
    band_rows = row_count // 8
    band_cols = col_count // 8
    per_device = band_rows * band_cols
    per_level = value_count // LEV
    total_rows = row_count * lat_count
    weights = column_area(lat_index * row_count, row_count, total_rows)
    target_part = column_mass(tracers, weights)

    patches, frac = departed(tracers, source_patch[0], shifts[0])
    advected = from_patches(levels(spatial(patches, frac[0], frac[1]), frac[2]), band_rows, band_cols)
    first, k_wide = diffuse_first(advected, diffusivity)
    first_part = column_mass(first, weights)

    patches, frac = departed(first, source_patch[1], shifts[1])
    planar = spatial(patches, frac[0], frac[1])
    weight_z = cubic_matrix(frac[2], LEV)

    area_wide = column_area(lat_index * row_count - 1, row_count + 2, total_rows)
    flux = area_wide * k_wide
    g = weights - 2.0 * flux[1:-1] + flux[:-2] + flux[2:]
    g_cols = jnp.broadcast_to(g.reshape(band_rows, 1, 8, 1), (band_rows, band_cols, 8, 8))
    weighted = jnp.einsum(
        "pi,piv->pv", g_cols.reshape(per_device, 64), planar, precision=lax.Precision.HIGHEST
    ).reshape(per_device, LEV, per_level)
    mix_part = jnp.einsum(
        "plm,pmt->lmt", weight_z, weighted, precision=lax.Precision.HIGHEST
    )
    field_planar = from_patches(planar, band_rows, band_cols)
    above, below = neighbour_halos(field_planar[:1], field_planar[row_count - 1 :], "lat", False)
    left, right = neighbour_halos(
        field_planar[:, :1], field_planar[:, col_count - 1 :], "lon", True
    )
    corner = jnp.zeros((1, 1, value_count), jnp.float32)
    wide = jnp.concatenate(
        [
            jnp.concatenate([corner, left, corner], axis=0),
            jnp.concatenate([above, field_planar, below], axis=0),
            jnp.concatenate([corner, right, corner], axis=0),
        ],
        axis=1,
    )
    fraction_z = shifts[1, 2]
    patch_rows, patch_cols = fraction_z.shape
    lon_index = lax.axis_index("lon")
    wide_rows = jnp.clip(
        lat_index * band_rows + (jnp.arange(row_count + 2) - 1) // 8, 0, patch_rows - 1
    )
    wide_cols = (lon_index * band_cols + (jnp.arange(col_count + 2) - 1) // 8) % patch_cols
    weight_wide = cubic_matrix(fraction_z[wide_rows][:, wide_cols], LEV)
    partial = jnp.concatenate([target_part, first_part, mix_part.reshape(-1)])
    members = lat_count * lax.axis_size("lon")
    totals = jnp.sum(
        lax.all_to_all(
            jnp.broadcast_to(partial, (members,) + partial.shape), ("lat", "lon"), 0, 0, tiled=True
        ),
        axis=0,
    )
    target = totals[:value_count]
    first_mass = totals[value_count : 2 * value_count]
    mix = totals[2 * value_count :].reshape(LEV, LEV, per_level)
    first_ratio = target / first_mass
    second_mass = jnp.sum(first_ratio.reshape(LEV, per_level)[None] * mix, axis=1).reshape(
        value_count
    )
    second_ratio = target / second_mass
    mixed = levels_cols(wide * first_ratio, weight_wide)
    centre = mixed[1:-1, 1:-1]
    laplace = (
        mixed[2:, 1:-1] + mixed[:-2, 1:-1] + mixed[1:-1, 2:] + mixed[1:-1, :-2] - 4.0 * centre
    )
    second = centre + diffusivity[:, None, None] * laplace
    return second * second_ratio[None, None, :]


def solution(mesh):
    return jax.shard_map(
        local,
        mesh=mesh,
        in_specs=(
            P(("groups", "lat"), "lon", None),
            P("groups", None, None, None),
            P("lat"),
            P("groups", None, None),
        ),
        out_specs=P(("groups", "lat"), "lon", None),
        check_vma=False,
    )
```

```python
import math

import jax
import jax.numpy as jnp
from jax import lax
from jax.sharding import PartitionSpec as P

LEV = 4
STEPS = 2
CAP = 4


def all_sum(value, axes, rider=None):
    rider_done = None
    for axis in axes:
        count = lax.axis_size(axis)
        if count & (count - 1):
            value = lax.psum(value, axis)
            continue
        distance = 1
        while distance < count:
            value = value + lax.ppermute(
                value, axis, [(i, i ^ distance) for i in range(count)]
            )
            if rider is not None:
                value, rider = lax.optimization_barrier((value, rider))
                rider_done, rider = rider, None
            distance *= 2
    if rider_done is None and rider is None:
        return value
    return value, rider if rider_done is None else rider_done


def neighbour_halos(lo_edge, hi_edge, axis, closed):
    count = lax.axis_size(axis)
    if count % 2:
        ends = count if closed else count - 1
        from_lo = lax.ppermute(hi_edge, axis, [(i, (i + 1) % count) for i in range(ends)])
        from_hi = lax.ppermute(lo_edge, axis, [((i + 1) % count, i) for i in range(ends)])
        return from_lo, from_hi
    even = lax.axis_index(axis) % 2 == 0
    first = lax.ppermute(
        jnp.where(even, hi_edge, lo_edge), axis, [(i, i ^ 1) for i in range(count)]
    )
    pairs = []
    for i in range(1, count, 2):
        if i + 1 < count:
            pairs += [(i, i + 1), (i + 1, i)]
        elif closed:
            pairs += [(i, 0), (0, i)]
    second = lax.ppermute(jnp.where(even, lo_edge, hi_edge), axis, pairs)
    return jnp.where(even, second, first), jnp.where(even, first, second)


def extended(cells, sides, width, closed):
    for axis, dim in sides:
        count = lax.axis_size(axis)
        ends = count if closed else count - 1
        head = lax.slice_in_dim(cells, 0, width, axis=dim)
        tail = lax.slice_in_dim(cells, cells.shape[dim] - width, cells.shape[dim], axis=dim)
        from_lo, from_hi = neighbour_halos(head, tail, axis, closed)
        cells = jnp.concatenate([from_lo, cells, from_hi], axis=dim)
    return cells


def cubic_weights(fraction):
    first_term = -fraction * (fraction - 1.0) * (fraction - 2.0) / 6.0
    second_term = (fraction + 1.0) * (fraction - 1.0) * (fraction - 2.0) / 2.0
    third_term = -(fraction + 1.0) * fraction * (fraction - 2.0) / 2.0
    fourth_term = (fraction + 1.0) * fraction * (fraction - 1.0) / 6.0
    return (first_term, second_term, third_term, fourth_term)


def cubic_matrix(fraction, extent):
    places = jnp.arange(extent)
    running = jnp.zeros(fraction.shape + (extent, extent), jnp.float32)
    for offset, weight in zip(range(-1, 3), cubic_weights(fraction)):
        target_col = jnp.clip(places + offset, 0, extent - 1)
        indicator = (target_col[:, None] == places[None, :]).astype(jnp.float32)
        running = running + weight[..., None, None] * indicator
    return running


def tap_sources(target, extent):
    return sorted({min(max(target + offset, 0), extent - 1) for offset in range(-1, 3)})


def plane_weights(fraction_y, fraction_x):
    rows = lax.broadcasted_iota(jnp.int32, (1, 64, 64), 1)
    cols = lax.broadcasted_iota(jnp.int32, (1, 64, 64), 2)

    def along(fraction, source, target):
        running = jnp.zeros((fraction.shape[0], 64, 64), jnp.float32)
        for offset, weight in zip(range(-1, 3), cubic_weights(fraction)):
            indicator = (jnp.clip(source + offset, 0, 7) == target).astype(jnp.float32)
            running = running + weight[:, None, None] * indicator
        return running

    return along(fraction_y, rows // 8, cols // 8) * along(fraction_x, rows % 8, cols % 8)


def spatial(patches, fraction_y, fraction_x):
    return jnp.einsum(
        "nij,njv->niv",
        plane_weights(fraction_y, fraction_x),
        patches,
        precision=lax.Precision.HIGHEST,
    )


def levels(flat, fraction_z):
    value_count = flat.shape[2]
    per_level = value_count // LEV
    weight_z = cubic_matrix(fraction_z, LEV)
    blocks = [flat[:, :, m * per_level : (m + 1) * per_level] for m in range(LEV)]
    out = []
    for level in range(LEV):
        acc = None
        for m in tap_sources(level, LEV):
            term = weight_z[:, level, m][:, None, None] * blocks[m]
            acc = term if acc is None else acc + term
        out.append(acc)
    return jnp.concatenate(out, axis=2)


def to_patches(state_field):
    band_rows = state_field.shape[0] // 8
    band_cols = state_field.shape[1] // 8
    return (
        state_field.reshape(band_rows, 8, band_cols, 8, -1)
        .transpose(0, 2, 1, 3, 4)
        .reshape(band_rows * band_cols, 64, -1)
    )


def from_patches(patches, band_rows, band_cols):
    return (
        patches.reshape(band_rows, band_cols, 8, 8, -1)
        .transpose(0, 2, 1, 3, 4)
        .reshape(band_rows * 8, band_cols * 8, -1)
    )


def column_area(first_row, row_count, total_rows):
    latitude = ((first_row + jnp.arange(row_count)).astype(jnp.float32) + 0.5) * (
        math.pi / total_rows
    ) - 0.5 * math.pi
    return jnp.cos(latitude)


def column_mass(state_field, weights):
    return jnp.sum(weights[:, None, None] * state_field, axis=(0, 1))


def diffuse(advected, diffusivity, row_dim):
    col_dim = row_dim + 1
    rows = advected.shape[row_dim]
    cols = advected.shape[col_dim]
    lon_wide = extended(advected, (("lon", col_dim),), 1, True)
    lat_wide = extended(advected, (("lat", row_dim),), 1, False)
    laplace = (
        lax.slice_in_dim(lat_wide, 2, rows + 2, axis=row_dim)
        + lax.slice_in_dim(lat_wide, 0, rows, axis=row_dim)
        + lax.slice_in_dim(lon_wide, 2, cols + 2, axis=col_dim)
        + lax.slice_in_dim(lon_wide, 0, cols, axis=col_dim)
        - 4.0 * advected
    )
    k_shape = [1] * advected.ndim
    k_shape[row_dim] = rows
    return advected + diffusivity.reshape(k_shape) * laplace


def diffuse_first(advected, diffusivity):
    rows, cols, value_count = advected.shape
    count = lax.axis_size("lat")

    def pack(row, number):
        return jnp.concatenate(
            [row, jnp.broadcast_to(number, (1, 1, value_count))], axis=1
        )

    from_above, from_below = neighbour_halos(
        pack(advected[:1], diffusivity[0]),
        pack(advected[rows - 1 :], diffusivity[rows - 1]),
        "lat",
        False,
    )
    lat_wide = jnp.concatenate([from_above[:, :cols], advected, from_below[:, :cols]], axis=0)
    k_wide = jnp.concatenate([from_above[0, cols, :1], diffusivity, from_below[0, cols, :1]])
    lon_wide = extended(advected, (("lon", 1),), 1, True)
    laplace = (
        lat_wide[2:] + lat_wide[:-2] + lon_wide[:, 2:] + lon_wide[:, :-2] - 4.0 * advected
    )
    return advected + diffusivity[:, None, None] * laplace, k_wide


def departed(state_field, source_ids, shifts_now):
    lat_count = lax.axis_size("lat")
    lat_index = lax.axis_index("lat")
    lon_index = lax.axis_index("lon")
    row_count, col_count, value_count = state_field.shape
    band_rows = row_count // 8
    band_cols = col_count // 8
    per_device = band_rows * band_cols
    total_cols = source_ids.shape[1]
    devices = jnp.arange(lat_count)
    slot_range = jnp.arange(CAP)
    column_ids = lax.dynamic_slice_in_dim(
        source_ids, lon_index * band_cols, band_cols, 1
    ).reshape(lat_count, per_device)
    fractions = lax.dynamic_slice_in_dim(
        shifts_now, lon_index * band_cols, band_cols, 2
    ).reshape(3, lat_count, per_device)
    source_row = column_ids // total_cols
    source_dev = source_row // band_rows
    source_local = (
        source_row % band_rows * band_cols + column_ids % total_cols - lon_index * band_cols
    )
    remote = source_dev != devices[:, None]
    matches = (source_dev[:, :, None] == devices[None, None, :]) & remote[:, :, None]
    slot_ranks = jnp.cumsum(matches.astype(jnp.int32), axis=1) - 1
    slot_of = jnp.sum(jnp.where(matches, slot_ranks, 0), axis=2)
    owned_here = remote & (source_dev == lat_index)
    sending = owned_here[:, :, None] & (slot_of[:, :, None] == slot_range[None, None, :])
    send_local = jnp.sum(jnp.where(sending, source_local[:, :, None], 0), axis=1)
    own_patches = to_patches(state_field)
    outgoing = own_patches[send_local.reshape(-1)].reshape(lat_count, CAP, 64, value_count)
    my_dev = lax.dynamic_index_in_dim(source_dev, lat_index, 0, keepdims=False)
    my_slot = lax.dynamic_index_in_dim(slot_of, lat_index, 0, keepdims=False)
    my_local = lax.dynamic_index_in_dim(source_local, lat_index, 0, keepdims=False)
    my_remote = lax.dynamic_index_in_dim(remote, lat_index, 0, keepdims=False)
    my_frac = lax.dynamic_index_in_dim(fractions, lat_index, 1, keepdims=False)
    arrived = lax.all_to_all(outgoing, "lat", 0, 0, tiled=True).reshape(
        lat_count * CAP, 64, value_count
    )
    pick_index = my_dev * CAP + my_slot
    take_near = (my_local[:, None] == jnp.arange(per_device)[None, :]) & ~my_remote[:, None]
    take_far = (pick_index[:, None] == jnp.arange(lat_count * CAP)[None, :]) & my_remote[:, None]
    patches = (
        jnp.dot(
            take_near.astype(jnp.float32),
            own_patches.reshape(per_device, -1),
            precision=lax.Precision.HIGHEST,
        )
        + jnp.dot(
            take_far.astype(jnp.float32),
            arrived.reshape(lat_count * CAP, -1),
            precision=lax.Precision.HIGHEST,
        )
    ).reshape(per_device, 64, value_count)
    return patches, my_frac


def local(tracers, shifts, diffusivity, source_patch):
    lat_count = lax.axis_size("lat")
    lat_index = lax.axis_index("lat")
    row_count, col_count, value_count = tracers.shape
    band_rows = row_count // 8
    band_cols = col_count // 8
    per_device = band_rows * band_cols
    per_level = value_count // LEV
    total_rows = row_count * lat_count
    weights = column_area(lat_index * row_count, row_count, total_rows)
    target_part = column_mass(tracers, weights)

    patches, frac = departed(tracers, source_patch[0], shifts[0])
    advected = from_patches(levels(spatial(patches, frac[0], frac[1]), frac[2]), band_rows, band_cols)
    first = diffuse(advected, diffusivity, 0)
    first_part = column_mass(first, weights)

    patches, frac = departed(first, source_patch[1], shifts[1])
    planar = spatial(patches, frac[0], frac[1])
    weight_z = cubic_matrix(frac[2], LEV)

    flux = weights * diffusivity
    zero = jnp.zeros((1,), jnp.float32)
    g = (
        weights
        - 2.0 * flux
        + jnp.concatenate([zero, flux[:-1]])
        + jnp.concatenate([flux[1:], zero])
    )
    g_cols = jnp.broadcast_to(g.reshape(band_rows, 1, 8, 1), (band_rows, band_cols, 8, 8))
    weighted = jnp.einsum(
        "pi,piv->pv", g_cols.reshape(per_device, 64), planar, precision=lax.Precision.HIGHEST
    ).reshape(per_device, LEV, per_level)
    mix_part = jnp.einsum(
        "plm,pmt->lmt", weight_z, weighted, precision=lax.Precision.HIGHEST
    )
    top_row = jnp.sum(planar[:band_cols, :8], axis=1).reshape(band_cols, LEV, per_level)
    bottom_row = jnp.sum(planar[per_device - band_cols :, 56:], axis=1).reshape(
        band_cols, LEV, per_level
    )
    top_part = jnp.einsum(
        "plm,pmt->lmt", weight_z[:band_cols], top_row, precision=lax.Precision.HIGHEST
    )
    bottom_part = jnp.einsum(
        "plm,pmt->lmt",
        weight_z[per_device - band_cols :],
        bottom_row,
        precision=lax.Precision.HIGHEST,
    )
    mix_size = LEV * value_count
    tag = jnp.zeros((value_count,), jnp.float32)
    tag = tag.at[0].set(diffusivity[0]).at[1].set(diffusivity[row_count - 1])
    tag = tag.at[2].set(lat_index.astype(jnp.float32))
    partial = jnp.concatenate(
        [
            target_part,
            first_part,
            mix_part.reshape(-1),
            top_part.reshape(-1),
            bottom_part.reshape(-1),
            tag,
        ]
    )
    members = lat_count * lax.axis_size("lon")
    everyone = lax.all_to_all(
        jnp.broadcast_to(partial, (members,) + partial.shape), ("lat", "lon"), 0, 0, tiled=True
    ).reshape(members, -1)
    head = 2 * value_count + mix_size
    tags = everyone[:, head + 2 * mix_size :]
    band_of = tags[:, 2]
    k_first, k_last = tags[:, 0], tags[:, 1]
    above_k = jnp.max(
        jnp.where(band_of[None, :] == band_of[:, None] - 1.0, k_last[None, :], 0.0), axis=1
    )
    below_k = jnp.max(
        jnp.where(band_of[None, :] == band_of[:, None] + 1.0, k_first[None, :], 0.0), axis=1
    )
    angle = math.pi / total_rows
    above_area = jnp.cos((band_of * row_count - 0.5) * angle - 0.5 * math.pi)
    below_area = jnp.cos((band_of * row_count + row_count + 0.5) * angle - 0.5 * math.pi)
    edge_terms = jnp.sum(
        (above_area * above_k)[:, None] * everyone[:, head : head + mix_size]
        + (below_area * below_k)[:, None] * everyone[:, head + mix_size : head + 2 * mix_size],
        axis=0,
    )
    totals = jnp.sum(everyone[:, :head], axis=0)
    totals = totals.at[2 * value_count :].add(edge_terms)
    target = totals[:value_count]
    first_mass = totals[value_count : 2 * value_count]
    mix = totals[2 * value_count :].reshape(LEV, LEV, per_level)
    first_ratio = target / first_mass
    second_mass = jnp.sum(first_ratio.reshape(LEV, per_level)[None] * mix, axis=1).reshape(
        value_count
    )
    second_ratio = target / second_mass
    advected = from_patches(
        levels(planar * first_ratio[None, None, :], frac[2]), band_rows, band_cols
    )
    return diffuse(advected, diffusivity, 0) * second_ratio[None, None, :]


def solution(mesh):
    return jax.shard_map(
        local,
        mesh=mesh,
        in_specs=(
            P(("groups", "lat"), "lon", None),
            P("groups", None, None, None),
            P("lat"),
            P("groups", None, None),
        ),
        out_specs=P(("groups", "lat"), "lon", None),
        check_vma=False,
    )
```

```python
import math

import jax
import jax.numpy as jnp
from jax import lax
from jax.sharding import PartitionSpec as P

LEV = 4
STEPS = 2
CAP = 4


def all_sum(value, axes, rider=None):
    rider_done = None
    for axis in axes:
        count = lax.axis_size(axis)
        if count & (count - 1):
            value = lax.psum(value, axis)
            continue
        distance = 1
        while distance < count:
            value = value + lax.ppermute(
                value, axis, [(i, i ^ distance) for i in range(count)]
            )
            if rider is not None:
                value, rider = lax.optimization_barrier((value, rider))
                rider_done, rider = rider, None
            distance *= 2
    if rider_done is None and rider is None:
        return value
    return value, rider if rider_done is None else rider_done


def neighbour_halos(lo_edge, hi_edge, axis, closed):
    count = lax.axis_size(axis)
    if count % 2:
        ends = count if closed else count - 1
        from_lo = lax.ppermute(hi_edge, axis, [(i, (i + 1) % count) for i in range(ends)])
        from_hi = lax.ppermute(lo_edge, axis, [((i + 1) % count, i) for i in range(ends)])
        return from_lo, from_hi
    even = lax.axis_index(axis) % 2 == 0
    first = lax.ppermute(
        jnp.where(even, hi_edge, lo_edge), axis, [(i, i ^ 1) for i in range(count)]
    )
    pairs = []
    for i in range(1, count, 2):
        if i + 1 < count:
            pairs += [(i, i + 1), (i + 1, i)]
        elif closed:
            pairs += [(i, 0), (0, i)]
    second = lax.ppermute(jnp.where(even, lo_edge, hi_edge), axis, pairs)
    return jnp.where(even, second, first), jnp.where(even, first, second)


def extended(cells, sides, width, closed):
    for axis, dim in sides:
        count = lax.axis_size(axis)
        ends = count if closed else count - 1
        head = lax.slice_in_dim(cells, 0, width, axis=dim)
        tail = lax.slice_in_dim(cells, cells.shape[dim] - width, cells.shape[dim], axis=dim)
        from_lo, from_hi = neighbour_halos(head, tail, axis, closed)
        cells = jnp.concatenate([from_lo, cells, from_hi], axis=dim)
    return cells


def cubic_weights(fraction):
    first_term = -fraction * (fraction - 1.0) * (fraction - 2.0) / 6.0
    second_term = (fraction + 1.0) * (fraction - 1.0) * (fraction - 2.0) / 2.0
    third_term = -(fraction + 1.0) * fraction * (fraction - 2.0) / 2.0
    fourth_term = (fraction + 1.0) * fraction * (fraction - 1.0) / 6.0
    return (first_term, second_term, third_term, fourth_term)


def cubic_matrix(fraction, extent):
    places = jnp.arange(extent)
    running = jnp.zeros(fraction.shape + (extent, extent), jnp.float32)
    for offset, weight in zip(range(-1, 3), cubic_weights(fraction)):
        target_col = jnp.clip(places + offset, 0, extent - 1)
        indicator = (target_col[:, None] == places[None, :]).astype(jnp.float32)
        running = running + weight[..., None, None] * indicator
    return running


def tap_sources(target, extent):
    return sorted({min(max(target + offset, 0), extent - 1) for offset in range(-1, 3)})


def plane_weights(fraction_y, fraction_x):
    rows = lax.broadcasted_iota(jnp.int32, (1, 64, 64), 1)
    cols = lax.broadcasted_iota(jnp.int32, (1, 64, 64), 2)

    def along(fraction, source, target):
        running = jnp.zeros((fraction.shape[0], 64, 64), jnp.float32)
        for offset, weight in zip(range(-1, 3), cubic_weights(fraction)):
            indicator = (jnp.clip(source + offset, 0, 7) == target).astype(jnp.float32)
            running = running + weight[:, None, None] * indicator
        return running

    return along(fraction_y, rows // 8, cols // 8) * along(fraction_x, rows % 8, cols % 8)


def spatial(patches, fraction_y, fraction_x):
    return jnp.einsum(
        "nij,njv->niv",
        plane_weights(fraction_y, fraction_x),
        patches,
        precision=lax.Precision.HIGHEST,
    )


def levels(flat, fraction_z):
    value_count = flat.shape[2]
    per_level = value_count // LEV
    weight_z = cubic_matrix(fraction_z, LEV)
    blocks = [flat[:, :, m * per_level : (m + 1) * per_level] for m in range(LEV)]
    out = []
    for level in range(LEV):
        acc = None
        for m in tap_sources(level, LEV):
            term = weight_z[:, level, m][:, None, None] * blocks[m]
            acc = term if acc is None else acc + term
        out.append(acc)
    return jnp.concatenate(out, axis=2)


def to_patches(state_field):
    band_rows = state_field.shape[0] // 8
    band_cols = state_field.shape[1] // 8
    return (
        state_field.reshape(band_rows, 8, band_cols, 8, -1)
        .transpose(0, 2, 1, 3, 4)
        .reshape(band_rows * band_cols, 64, -1)
    )


def from_patches(patches, band_rows, band_cols):
    return (
        patches.reshape(band_rows, band_cols, 8, 8, -1)
        .transpose(0, 2, 1, 3, 4)
        .reshape(band_rows * 8, band_cols * 8, -1)
    )


def column_area(first_row, row_count, total_rows):
    latitude = ((first_row + jnp.arange(row_count)).astype(jnp.float32) + 0.5) * (
        math.pi / total_rows
    ) - 0.5 * math.pi
    return jnp.cos(latitude)


def column_mass(state_field, weights):
    return jnp.sum(weights[:, None, None] * state_field, axis=(0, 1))


def diffuse(advected, diffusivity, row_dim):
    col_dim = row_dim + 1
    rows = advected.shape[row_dim]
    cols = advected.shape[col_dim]
    lon_wide = extended(advected, (("lon", col_dim),), 1, True)
    lat_wide = extended(advected, (("lat", row_dim),), 1, False)
    laplace = (
        lax.slice_in_dim(lat_wide, 2, rows + 2, axis=row_dim)
        + lax.slice_in_dim(lat_wide, 0, rows, axis=row_dim)
        + lax.slice_in_dim(lon_wide, 2, cols + 2, axis=col_dim)
        + lax.slice_in_dim(lon_wide, 0, cols, axis=col_dim)
        - 4.0 * advected
    )
    k_shape = [1] * advected.ndim
    k_shape[row_dim] = rows
    return advected + diffusivity.reshape(k_shape) * laplace


def levels_cols(values, weight_z):
    value_count = values.shape[-1]
    per_level = value_count // LEV
    blocks = [values[..., m * per_level : (m + 1) * per_level] for m in range(LEV)]
    out = []
    for level in range(LEV):
        acc = None
        for m in tap_sources(level, LEV):
            term = weight_z[..., level, m][..., None] * blocks[m]
            acc = term if acc is None else acc + term
        out.append(acc)
    return jnp.concatenate(out, axis=-1)


def diffuse_first(advected, diffusivity):
    rows, cols, value_count = advected.shape
    count = lax.axis_size("lat")

    def pack(row, number):
        return jnp.concatenate(
            [row, jnp.broadcast_to(number, (1, 1, value_count))], axis=1
        )

    from_above, from_below = neighbour_halos(
        pack(advected[:1], diffusivity[0]),
        pack(advected[rows - 1 :], diffusivity[rows - 1]),
        "lat",
        False,
    )
    lat_wide = jnp.concatenate([from_above[:, :cols], advected, from_below[:, :cols]], axis=0)
    k_wide = jnp.concatenate([from_above[0, cols, :1], diffusivity, from_below[0, cols, :1]])
    lon_wide = extended(advected, (("lon", 1),), 1, True)
    laplace = (
        lat_wide[2:] + lat_wide[:-2] + lon_wide[:, 2:] + lon_wide[:, :-2] - 4.0 * advected
    )
    return advected + diffusivity[:, None, None] * laplace, k_wide


def departed(state_field, source_ids, shifts_now):
    lat_count = lax.axis_size("lat")
    lat_index = lax.axis_index("lat")
    lon_index = lax.axis_index("lon")
    row_count, col_count, value_count = state_field.shape
    band_rows = row_count // 8
    band_cols = col_count // 8
    per_device = band_rows * band_cols
    total_cols = source_ids.shape[1]
    devices = jnp.arange(lat_count)
    slot_range = jnp.arange(CAP)
    column_ids = lax.dynamic_slice_in_dim(
        source_ids, lon_index * band_cols, band_cols, 1
    ).reshape(lat_count, per_device)
    fractions = lax.dynamic_slice_in_dim(
        shifts_now, lon_index * band_cols, band_cols, 2
    ).reshape(3, lat_count, per_device)
    source_row = column_ids // total_cols
    source_dev = source_row // band_rows
    source_local = (
        source_row % band_rows * band_cols + column_ids % total_cols - lon_index * band_cols
    )
    remote = source_dev != devices[:, None]
    matches = (source_dev[:, :, None] == devices[None, None, :]) & remote[:, :, None]
    slot_ranks = jnp.cumsum(matches.astype(jnp.int32), axis=1) - 1
    slot_of = jnp.sum(jnp.where(matches, slot_ranks, 0), axis=2)
    owned_here = remote & (source_dev == lat_index)
    sending = owned_here[:, :, None] & (slot_of[:, :, None] == slot_range[None, None, :])
    send_local = jnp.sum(jnp.where(sending, source_local[:, :, None], 0), axis=1)
    own_patches = to_patches(state_field)
    outgoing = own_patches[send_local.reshape(-1)].reshape(lat_count, CAP, 64, value_count)
    my_dev = lax.dynamic_index_in_dim(source_dev, lat_index, 0, keepdims=False)
    my_slot = lax.dynamic_index_in_dim(slot_of, lat_index, 0, keepdims=False)
    my_local = lax.dynamic_index_in_dim(source_local, lat_index, 0, keepdims=False)
    my_remote = lax.dynamic_index_in_dim(remote, lat_index, 0, keepdims=False)
    my_frac = lax.dynamic_index_in_dim(fractions, lat_index, 1, keepdims=False)
    arrived = lax.all_to_all(outgoing, "lat", 0, 0, tiled=True).reshape(
        lat_count * CAP, 64, value_count
    )
    pick_index = my_dev * CAP + my_slot
    take_near = (my_local[:, None] == jnp.arange(per_device)[None, :]) & ~my_remote[:, None]
    take_far = (pick_index[:, None] == jnp.arange(lat_count * CAP)[None, :]) & my_remote[:, None]
    patches = (
        jnp.dot(
            take_near.astype(jnp.float32),
            own_patches.reshape(per_device, -1),
            precision=lax.Precision.HIGHEST,
        )
        + jnp.dot(
            take_far.astype(jnp.float32),
            arrived.reshape(lat_count * CAP, -1),
            precision=lax.Precision.HIGHEST,
        )
    ).reshape(per_device, 64, value_count)
    return patches, my_frac


def local(tracers, shifts, diffusivity, source_patch):
    lat_count = lax.axis_size("lat")
    lat_index = lax.axis_index("lat")
    row_count, col_count, value_count = tracers.shape
    band_rows = row_count // 8
    band_cols = col_count // 8
    per_device = band_rows * band_cols
    per_level = value_count // LEV
    total_rows = row_count * lat_count
    weights = column_area(lat_index * row_count, row_count, total_rows)
    target_part = column_mass(tracers, weights)

    patches, frac = departed(tracers, source_patch[0], shifts[0])
    advected = from_patches(levels(spatial(patches, frac[0], frac[1]), frac[2]), band_rows, band_cols)
    first, k_wide = diffuse_first(advected, diffusivity)
    first_part = column_mass(first, weights)

    patches, frac = departed(first, source_patch[1], shifts[1])
    planar = spatial(patches, frac[0], frac[1])
    weight_z = cubic_matrix(frac[2], LEV)

    area_wide = column_area(lat_index * row_count - 1, row_count + 2, total_rows)
    flux = area_wide * k_wide
    g = weights - 2.0 * flux[1:-1] + flux[:-2] + flux[2:]
    g_cols = jnp.broadcast_to(g.reshape(band_rows, 1, 8, 1), (band_rows, band_cols, 8, 8))
    weighted = jnp.einsum(
        "pi,piv->pv", g_cols.reshape(per_device, 64), planar, precision=lax.Precision.HIGHEST
    ).reshape(per_device, LEV, per_level)
    mix_part = jnp.einsum(
        "plm,pmt->lmt", weight_z, weighted, precision=lax.Precision.HIGHEST
    )
    field_planar = from_patches(planar, band_rows, band_cols)
    partial = jnp.concatenate([target_part, first_part, mix_part.reshape(-1)])
    members = lat_count * lax.axis_size("lon")
    totals = jnp.sum(
        lax.all_to_all(
            jnp.broadcast_to(partial, (members,) + partial.shape), ("lat", "lon"), 0, 0, tiled=True
        ),
        axis=0,
    )
    target = totals[:value_count]
    first_mass = totals[value_count : 2 * value_count]
    mix = totals[2 * value_count :].reshape(LEV, LEV, per_level)
    first_ratio = target / first_mass
    second_mass = jnp.sum(first_ratio.reshape(LEV, per_level)[None] * mix, axis=1).reshape(
        value_count
    )
    second_ratio = target / second_mass
    advected = levels_cols(
        (field_planar * first_ratio).reshape(band_rows, 8, band_cols, 8, value_count),
        weight_z.reshape(band_rows, 1, band_cols, 1, LEV, LEV),
    ).reshape(row_count, col_count, value_count)
    return diffuse(advected, diffusivity, 0) * second_ratio[None, None, :]


def solution(mesh):
    return jax.shard_map(
        local,
        mesh=mesh,
        in_specs=(
            P(("groups", "lat"), "lon", None),
            P("groups", None, None, None),
            P("lat"),
            P("groups", None, None),
        ),
        out_specs=P(("groups", "lat"), "lon", None),
        check_vma=False,
    )
```

```python
import math

import jax
import jax.numpy as jnp
from jax import lax
from jax.sharding import PartitionSpec as P

LEV = 4
STEPS = 2
CAP = 4


def all_sum(value, axes, rider=None):
    rider_done = None
    for axis in axes:
        count = lax.axis_size(axis)
        if count & (count - 1):
            value = lax.psum(value, axis)
            continue
        distance = 1
        while distance < count:
            value = value + lax.ppermute(
                value, axis, [(i, i ^ distance) for i in range(count)]
            )
            if rider is not None:
                value, rider = lax.optimization_barrier((value, rider))
                rider_done, rider = rider, None
            distance *= 2
    if rider_done is None and rider is None:
        return value
    return value, rider if rider_done is None else rider_done


def neighbour_halos(lo_edge, hi_edge, axis, closed):
    count = lax.axis_size(axis)
    if count % 2:
        ends = count if closed else count - 1
        from_lo = lax.ppermute(hi_edge, axis, [(i, (i + 1) % count) for i in range(ends)])
        from_hi = lax.ppermute(lo_edge, axis, [((i + 1) % count, i) for i in range(ends)])
        return from_lo, from_hi
    even = lax.axis_index(axis) % 2 == 0
    first = lax.ppermute(
        jnp.where(even, hi_edge, lo_edge), axis, [(i, i ^ 1) for i in range(count)]
    )
    pairs = []
    for i in range(1, count, 2):
        if i + 1 < count:
            pairs += [(i, i + 1), (i + 1, i)]
        elif closed:
            pairs += [(i, 0), (0, i)]
    second = lax.ppermute(jnp.where(even, lo_edge, hi_edge), axis, pairs)
    return jnp.where(even, second, first), jnp.where(even, first, second)


def extended(cells, sides, width, closed):
    for axis, dim in sides:
        count = lax.axis_size(axis)
        ends = count if closed else count - 1
        head = lax.slice_in_dim(cells, 0, width, axis=dim)
        tail = lax.slice_in_dim(cells, cells.shape[dim] - width, cells.shape[dim], axis=dim)
        from_lo, from_hi = neighbour_halos(head, tail, axis, closed)
        cells = jnp.concatenate([from_lo, cells, from_hi], axis=dim)
    return cells


def cubic_weights(fraction):
    first_term = -fraction * (fraction - 1.0) * (fraction - 2.0) / 6.0
    second_term = (fraction + 1.0) * (fraction - 1.0) * (fraction - 2.0) / 2.0
    third_term = -(fraction + 1.0) * fraction * (fraction - 2.0) / 2.0
    fourth_term = (fraction + 1.0) * fraction * (fraction - 1.0) / 6.0
    return (first_term, second_term, third_term, fourth_term)


def cubic_matrix(fraction, extent):
    places = jnp.arange(extent)
    running = jnp.zeros(fraction.shape + (extent, extent), jnp.float32)
    for offset, weight in zip(range(-1, 3), cubic_weights(fraction)):
        target_col = jnp.clip(places + offset, 0, extent - 1)
        indicator = (target_col[:, None] == places[None, :]).astype(jnp.float32)
        running = running + weight[..., None, None] * indicator
    return running


def tap_sources(target, extent):
    return sorted({min(max(target + offset, 0), extent - 1) for offset in range(-1, 3)})


def plane_weights(fraction_y, fraction_x):
    rows = lax.broadcasted_iota(jnp.int32, (1, 64, 64), 1)
    cols = lax.broadcasted_iota(jnp.int32, (1, 64, 64), 2)

    def along(fraction, source, target):
        running = jnp.zeros((fraction.shape[0], 64, 64), jnp.float32)
        for offset, weight in zip(range(-1, 3), cubic_weights(fraction)):
            indicator = (jnp.clip(source + offset, 0, 7) == target).astype(jnp.float32)
            running = running + weight[:, None, None] * indicator
        return running

    return along(fraction_y, rows // 8, cols // 8) * along(fraction_x, rows % 8, cols % 8)


def spatial(patches, fraction_y, fraction_x):
    return jnp.einsum(
        "nij,njv->niv",
        plane_weights(fraction_y, fraction_x),
        patches,
        precision=lax.Precision.HIGHEST,
    )


def levels(flat, fraction_z):
    value_count = flat.shape[2]
    per_level = value_count // LEV
    weight_z = cubic_matrix(fraction_z, LEV)
    blocks = [flat[:, :, m * per_level : (m + 1) * per_level] for m in range(LEV)]
    out = []
    for level in range(LEV):
        acc = None
        for m in tap_sources(level, LEV):
            term = weight_z[:, level, m][:, None, None] * blocks[m]
            acc = term if acc is None else acc + term
        out.append(acc)
    return jnp.concatenate(out, axis=2)


def to_patches(state_field):
    band_rows = state_field.shape[0] // 8
    band_cols = state_field.shape[1] // 8
    return (
        state_field.reshape(band_rows, 8, band_cols, 8, -1)
        .transpose(0, 2, 1, 3, 4)
        .reshape(band_rows * band_cols, 64, -1)
    )


def from_patches(patches, band_rows, band_cols):
    return (
        patches.reshape(band_rows, band_cols, 8, 8, -1)
        .transpose(0, 2, 1, 3, 4)
        .reshape(band_rows * 8, band_cols * 8, -1)
    )


def column_area(first_row, row_count, total_rows):
    latitude = ((first_row + jnp.arange(row_count)).astype(jnp.float32) + 0.5) * (
        math.pi / total_rows
    ) - 0.5 * math.pi
    return jnp.cos(latitude)


def column_mass(state_field, weights):
    return jnp.sum(weights[:, None, None] * state_field, axis=(0, 1))


def diffuse(advected, diffusivity, row_dim):
    col_dim = row_dim + 1
    rows = advected.shape[row_dim]
    cols = advected.shape[col_dim]
    lon_wide = extended(advected, (("lon", col_dim),), 1, True)
    lat_wide = extended(advected, (("lat", row_dim),), 1, False)
    laplace = (
        lax.slice_in_dim(lat_wide, 2, rows + 2, axis=row_dim)
        + lax.slice_in_dim(lat_wide, 0, rows, axis=row_dim)
        + lax.slice_in_dim(lon_wide, 2, cols + 2, axis=col_dim)
        + lax.slice_in_dim(lon_wide, 0, cols, axis=col_dim)
        - 4.0 * advected
    )
    k_shape = [1] * advected.ndim
    k_shape[row_dim] = rows
    return advected + diffusivity.reshape(k_shape) * laplace


def levels_cols(values, weight_z):
    value_count = values.shape[-1]
    per_level = value_count // LEV
    blocks = [values[..., m * per_level : (m + 1) * per_level] for m in range(LEV)]
    out = []
    for level in range(LEV):
        acc = None
        for m in tap_sources(level, LEV):
            term = weight_z[..., level, m][..., None] * blocks[m]
            acc = term if acc is None else acc + term
        out.append(acc)
    return jnp.concatenate(out, axis=-1)


def diffuse_first(advected, diffusivity):
    rows, cols, value_count = advected.shape
    count = lax.axis_size("lat")

    def pack(row, number):
        return jnp.concatenate(
            [row, jnp.broadcast_to(number, (1, 1, value_count))], axis=1
        )

    from_above, from_below = neighbour_halos(
        pack(advected[:1], diffusivity[0]),
        pack(advected[rows - 1 :], diffusivity[rows - 1]),
        "lat",
        False,
    )
    lat_wide = jnp.concatenate([from_above[:, :cols], advected, from_below[:, :cols]], axis=0)
    k_wide = jnp.concatenate([from_above[0, cols, :1], diffusivity, from_below[0, cols, :1]])
    lon_wide = extended(advected, (("lon", 1),), 1, True)
    laplace = (
        lat_wide[2:] + lat_wide[:-2] + lon_wide[:, 2:] + lon_wide[:, :-2] - 4.0 * advected
    )
    return advected + diffusivity[:, None, None] * laplace, k_wide


def departed(state_field, source_ids, shifts_now):
    lat_count = lax.axis_size("lat")
    lat_index = lax.axis_index("lat")
    lon_index = lax.axis_index("lon")
    row_count, col_count, value_count = state_field.shape
    band_rows = row_count // 8
    band_cols = col_count // 8
    per_device = band_rows * band_cols
    total_cols = source_ids.shape[1]
    devices = jnp.arange(lat_count)
    slot_range = jnp.arange(CAP)
    column_ids = lax.dynamic_slice_in_dim(
        source_ids, lon_index * band_cols, band_cols, 1
    ).reshape(lat_count, per_device)
    fractions = lax.dynamic_slice_in_dim(
        shifts_now, lon_index * band_cols, band_cols, 2
    ).reshape(3, lat_count, per_device)
    source_row = column_ids // total_cols
    source_dev = source_row // band_rows
    source_local = (
        source_row % band_rows * band_cols + column_ids % total_cols - lon_index * band_cols
    )
    remote = source_dev != devices[:, None]
    matches = (source_dev[:, :, None] == devices[None, None, :]) & remote[:, :, None]
    slot_ranks = jnp.cumsum(matches.astype(jnp.int32), axis=1) - 1
    slot_of = jnp.sum(jnp.where(matches, slot_ranks, 0), axis=2)
    owned_here = remote & (source_dev == lat_index)
    sending = owned_here[:, :, None] & (slot_of[:, :, None] == slot_range[None, None, :])
    send_local = jnp.sum(jnp.where(sending, source_local[:, :, None], 0), axis=1)
    own_patches = to_patches(state_field)
    outgoing = own_patches[send_local.reshape(-1)].reshape(lat_count, CAP, 64, value_count)
    my_dev = lax.dynamic_index_in_dim(source_dev, lat_index, 0, keepdims=False)
    my_slot = lax.dynamic_index_in_dim(slot_of, lat_index, 0, keepdims=False)
    my_local = lax.dynamic_index_in_dim(source_local, lat_index, 0, keepdims=False)
    my_remote = lax.dynamic_index_in_dim(remote, lat_index, 0, keepdims=False)
    my_frac = lax.dynamic_index_in_dim(fractions, lat_index, 1, keepdims=False)
    arrived = lax.all_to_all(outgoing, "lat", 0, 0, tiled=True).reshape(
        lat_count * CAP, 64, value_count
    )
    pick_index = my_dev * CAP + my_slot
    take_near = (my_local[:, None] == jnp.arange(per_device)[None, :]) & ~my_remote[:, None]
    take_far = (pick_index[:, None] == jnp.arange(lat_count * CAP)[None, :]) & my_remote[:, None]
    patches = (
        jnp.dot(
            take_near.astype(jnp.float32),
            own_patches.reshape(per_device, -1),
            precision=lax.Precision.HIGHEST,
        )
        + jnp.dot(
            take_far.astype(jnp.float32),
            arrived.reshape(lat_count * CAP, -1),
            precision=lax.Precision.HIGHEST,
        )
    ).reshape(per_device, 64, value_count)
    return patches, my_frac


def local(tracers, shifts, diffusivity, source_patch):
    lat_count = lax.axis_size("lat")
    lat_index = lax.axis_index("lat")
    row_count, col_count, value_count = tracers.shape
    band_rows = row_count // 8
    band_cols = col_count // 8
    per_device = band_rows * band_cols
    per_level = value_count // LEV
    total_rows = row_count * lat_count
    weights = column_area(lat_index * row_count, row_count, total_rows)
    target_part = column_mass(tracers, weights)

    patches, frac = departed(tracers, source_patch[0], shifts[0])
    advected = from_patches(levels(spatial(patches, frac[0], frac[1]), frac[2]), band_rows, band_cols)
    first, k_wide = diffuse_first(advected, diffusivity)
    first_part = column_mass(first, weights)

    patches, frac = departed(first, source_patch[1], shifts[1])
    plane = plane_weights(frac[0], frac[1])
    planar = jnp.einsum("nij,njv->niv", plane, patches, precision=lax.Precision.HIGHEST)
    weight_z = cubic_matrix(frac[2], LEV)

    area_wide = column_area(lat_index * row_count - 1, row_count + 2, total_rows)
    flux = area_wide * k_wide
    g = weights - 2.0 * flux[1:-1] + flux[:-2] + flux[2:]
    g_cols = jnp.broadcast_to(g.reshape(band_rows, 1, 8, 1), (band_rows, band_cols, 8, 8))
    row_weights = jnp.einsum(
        "pi,pij->pj", g_cols.reshape(per_device, 64), plane, precision=lax.Precision.HIGHEST
    )
    weighted = jnp.einsum(
        "pj,pjv->pv", row_weights, patches, precision=lax.Precision.HIGHEST
    ).reshape(per_device, LEV, per_level)
    mix_part = jnp.einsum(
        "plm,pmt->lmt", weight_z, weighted, precision=lax.Precision.HIGHEST
    )
    field_planar = from_patches(planar, band_rows, band_cols)
    partial = jnp.concatenate([target_part, first_part, mix_part.reshape(-1)])
    members = lat_count * lax.axis_size("lon")
    totals = jnp.sum(
        lax.all_to_all(
            jnp.broadcast_to(partial, (members,) + partial.shape), ("lat", "lon"), 0, 0, tiled=True
        ),
        axis=0,
    )
    target = totals[:value_count]
    first_mass = totals[value_count : 2 * value_count]
    mix = totals[2 * value_count :].reshape(LEV, LEV, per_level)
    first_ratio = target / first_mass
    second_mass = jnp.sum(first_ratio.reshape(LEV, per_level)[None] * mix, axis=1).reshape(
        value_count
    )
    second_ratio = target / second_mass
    advected = levels_cols(
        (field_planar * first_ratio).reshape(band_rows, 8, band_cols, 8, value_count),
        weight_z.reshape(band_rows, 1, band_cols, 1, LEV, LEV),
    ).reshape(row_count, col_count, value_count)
    return diffuse(advected, diffusivity, 0) * second_ratio[None, None, :]


def solution(mesh):
    return jax.shard_map(
        local,
        mesh=mesh,
        in_specs=(
            P(("groups", "lat"), "lon", None),
            P("groups", None, None, None),
            P("lat"),
            P("groups", None, None),
        ),
        out_specs=P(("groups", "lat"), "lon", None),
        check_vma=False,
    )
```

```python
import math

import jax
import jax.numpy as jnp
from jax import lax
from jax.sharding import PartitionSpec as P

LEV = 4
STEPS = 2
CAP = 4


def all_sum(value, axes, rider=None):
    rider_done = None
    for axis in axes:
        count = lax.axis_size(axis)
        if count & (count - 1):
            value = lax.psum(value, axis)
            continue
        distance = 1
        while distance < count:
            value = value + lax.ppermute(
                value, axis, [(i, i ^ distance) for i in range(count)]
            )
            if rider is not None:
                value, rider = lax.optimization_barrier((value, rider))
                rider_done, rider = rider, None
            distance *= 2
    if rider_done is None and rider is None:
        return value
    return value, rider if rider_done is None else rider_done


def neighbour_halos(lo_edge, hi_edge, axis, closed):
    count = lax.axis_size(axis)
    if count % 2:
        ends = count if closed else count - 1
        from_lo = lax.ppermute(hi_edge, axis, [(i, (i + 1) % count) for i in range(ends)])
        from_hi = lax.ppermute(lo_edge, axis, [((i + 1) % count, i) for i in range(ends)])
        return from_lo, from_hi
    even = lax.axis_index(axis) % 2 == 0
    first = lax.ppermute(
        jnp.where(even, hi_edge, lo_edge), axis, [(i, i ^ 1) for i in range(count)]
    )
    pairs = []
    for i in range(1, count, 2):
        if i + 1 < count:
            pairs += [(i, i + 1), (i + 1, i)]
        elif closed:
            pairs += [(i, 0), (0, i)]
    second = lax.ppermute(jnp.where(even, lo_edge, hi_edge), axis, pairs)
    return jnp.where(even, second, first), jnp.where(even, first, second)


def extended(cells, sides, width, closed):
    for axis, dim in sides:
        count = lax.axis_size(axis)
        ends = count if closed else count - 1
        head = lax.slice_in_dim(cells, 0, width, axis=dim)
        tail = lax.slice_in_dim(cells, cells.shape[dim] - width, cells.shape[dim], axis=dim)
        from_lo, from_hi = neighbour_halos(head, tail, axis, closed)
        cells = jnp.concatenate([from_lo, cells, from_hi], axis=dim)
    return cells


def cubic_weights(fraction):
    first_term = -fraction * (fraction - 1.0) * (fraction - 2.0) / 6.0
    second_term = (fraction + 1.0) * (fraction - 1.0) * (fraction - 2.0) / 2.0
    third_term = -(fraction + 1.0) * fraction * (fraction - 2.0) / 2.0
    fourth_term = (fraction + 1.0) * fraction * (fraction - 1.0) / 6.0
    return (first_term, second_term, third_term, fourth_term)


def cubic_matrix(fraction, extent):
    places = jnp.arange(extent)
    running = jnp.zeros(fraction.shape + (extent, extent), jnp.float32)
    for offset, weight in zip(range(-1, 3), cubic_weights(fraction)):
        target_col = jnp.clip(places + offset, 0, extent - 1)
        indicator = (target_col[:, None] == places[None, :]).astype(jnp.float32)
        running = running + weight[..., None, None] * indicator
    return running


def tap_sources(target, extent):
    return sorted({min(max(target + offset, 0), extent - 1) for offset in range(-1, 3)})


def plane_weights(fraction_y, fraction_x):
    rows = lax.broadcasted_iota(jnp.int32, (1, 64, 64), 1)
    cols = lax.broadcasted_iota(jnp.int32, (1, 64, 64), 2)

    def along(fraction, source, target):
        running = jnp.zeros((fraction.shape[0], 64, 64), jnp.float32)
        for offset, weight in zip(range(-1, 3), cubic_weights(fraction)):
            indicator = (jnp.clip(source + offset, 0, 7) == target).astype(jnp.float32)
            running = running + weight[:, None, None] * indicator
        return running

    return along(fraction_y, rows // 8, cols // 8) * along(fraction_x, rows % 8, cols % 8)


def spatial(patches, fraction_y, fraction_x):
    return jnp.einsum(
        "nij,njv->niv",
        plane_weights(fraction_y, fraction_x),
        patches,
        precision=lax.Precision.HIGHEST,
    )


def levels(flat, fraction_z):
    value_count = flat.shape[2]
    per_level = value_count // LEV
    weight_z = cubic_matrix(fraction_z, LEV)
    blocks = [flat[:, :, m * per_level : (m + 1) * per_level] for m in range(LEV)]
    out = []
    for level in range(LEV):
        acc = None
        for m in tap_sources(level, LEV):
            term = weight_z[:, level, m][:, None, None] * blocks[m]
            acc = term if acc is None else acc + term
        out.append(acc)
    return jnp.concatenate(out, axis=2)


def to_patches(state_field):
    band_rows = state_field.shape[0] // 8
    band_cols = state_field.shape[1] // 8
    return (
        state_field.reshape(band_rows, 8, band_cols, 8, -1)
        .transpose(0, 2, 1, 3, 4)
        .reshape(band_rows * band_cols, 64, -1)
    )


def from_patches(patches, band_rows, band_cols):
    return (
        patches.reshape(band_rows, band_cols, 8, 8, -1)
        .transpose(0, 2, 1, 3, 4)
        .reshape(band_rows * 8, band_cols * 8, -1)
    )


def column_area(first_row, row_count, total_rows):
    latitude = ((first_row + jnp.arange(row_count)).astype(jnp.float32) + 0.5) * (
        math.pi / total_rows
    ) - 0.5 * math.pi
    return jnp.cos(latitude)


def column_mass(state_field, weights):
    return jnp.sum(weights[:, None, None] * state_field, axis=(0, 1))


def diffuse(advected, diffusivity, row_dim):
    col_dim = row_dim + 1
    rows = advected.shape[row_dim]
    cols = advected.shape[col_dim]
    lon_wide = extended(advected, (("lon", col_dim),), 1, True)
    lat_wide = extended(advected, (("lat", row_dim),), 1, False)
    laplace = (
        lax.slice_in_dim(lat_wide, 2, rows + 2, axis=row_dim)
        + lax.slice_in_dim(lat_wide, 0, rows, axis=row_dim)
        + lax.slice_in_dim(lon_wide, 2, cols + 2, axis=col_dim)
        + lax.slice_in_dim(lon_wide, 0, cols, axis=col_dim)
        - 4.0 * advected
    )
    k_shape = [1] * advected.ndim
    k_shape[row_dim] = rows
    return advected + diffusivity.reshape(k_shape) * laplace


def levels_cols(values, weight_z):
    value_count = values.shape[-1]
    per_level = value_count // LEV
    blocks = [values[..., m * per_level : (m + 1) * per_level] for m in range(LEV)]
    out = []
    for level in range(LEV):
        acc = None
        for m in tap_sources(level, LEV):
            term = weight_z[..., level, m][..., None] * blocks[m]
            acc = term if acc is None else acc + term
        out.append(acc)
    return jnp.concatenate(out, axis=-1)


def diffuse_first(advected, diffusivity):
    rows, cols, value_count = advected.shape
    count = lax.axis_size("lat")

    def pack(row, number):
        return jnp.concatenate(
            [row, jnp.broadcast_to(number, (1, 1, value_count))], axis=1
        )

    from_above, from_below = neighbour_halos(
        pack(advected[:1], diffusivity[0]),
        pack(advected[rows - 1 :], diffusivity[rows - 1]),
        "lat",
        False,
    )
    lat_wide = jnp.concatenate([from_above[:, :cols], advected, from_below[:, :cols]], axis=0)
    k_wide = jnp.concatenate([from_above[0, cols, :1], diffusivity, from_below[0, cols, :1]])
    lon_wide = extended(advected, (("lon", 1),), 1, True)
    laplace = (
        lat_wide[2:] + lat_wide[:-2] + lon_wide[:, 2:] + lon_wide[:, :-2] - 4.0 * advected
    )
    return advected + diffusivity[:, None, None] * laplace, k_wide


def departed(state_field, source_ids, shifts_now):
    lat_count = lax.axis_size("lat")
    lat_index = lax.axis_index("lat")
    lon_index = lax.axis_index("lon")
    row_count, col_count, value_count = state_field.shape
    band_rows = row_count // 8
    band_cols = col_count // 8
    per_device = band_rows * band_cols
    total_cols = source_ids.shape[1]
    devices = jnp.arange(lat_count)
    slot_range = jnp.arange(CAP)
    column_ids = lax.dynamic_slice_in_dim(
        source_ids, lon_index * band_cols, band_cols, 1
    ).reshape(lat_count, per_device)
    fractions = lax.dynamic_slice_in_dim(
        shifts_now, lon_index * band_cols, band_cols, 2
    ).reshape(3, lat_count, per_device)
    source_row = column_ids // total_cols
    source_dev = source_row // band_rows
    source_local = (
        source_row % band_rows * band_cols + column_ids % total_cols - lon_index * band_cols
    )
    remote = source_dev != devices[:, None]
    matches = (source_dev[:, :, None] == devices[None, None, :]) & remote[:, :, None]
    slot_ranks = jnp.cumsum(matches.astype(jnp.int32), axis=1) - 1
    slot_of = jnp.sum(jnp.where(matches, slot_ranks, 0), axis=2)
    owned_here = remote & (source_dev == lat_index)
    sending = owned_here[:, :, None] & (slot_of[:, :, None] == slot_range[None, None, :])
    send_local = jnp.sum(jnp.where(sending, source_local[:, :, None], 0), axis=1)
    own_patches = to_patches(state_field)
    outgoing = own_patches[send_local.reshape(-1)].reshape(lat_count, CAP, 64, value_count)
    my_dev = lax.dynamic_index_in_dim(source_dev, lat_index, 0, keepdims=False)
    my_slot = lax.dynamic_index_in_dim(slot_of, lat_index, 0, keepdims=False)
    my_local = lax.dynamic_index_in_dim(source_local, lat_index, 0, keepdims=False)
    my_remote = lax.dynamic_index_in_dim(remote, lat_index, 0, keepdims=False)
    my_frac = lax.dynamic_index_in_dim(fractions, lat_index, 1, keepdims=False)
    arrived = lax.all_to_all(outgoing, "lat", 0, 0, tiled=True).reshape(
        lat_count * CAP, 64, value_count
    )
    pick_index = my_dev * CAP + my_slot
    take_near = (my_local[:, None] == jnp.arange(per_device)[None, :]) & ~my_remote[:, None]
    take_far = (pick_index[:, None] == jnp.arange(lat_count * CAP)[None, :]) & my_remote[:, None]
    patches = (
        jnp.dot(
            take_near.astype(jnp.float32),
            own_patches.reshape(per_device, -1),
            precision=lax.Precision.HIGHEST,
        )
        + jnp.dot(
            take_far.astype(jnp.float32),
            arrived.reshape(lat_count * CAP, -1),
            precision=lax.Precision.HIGHEST,
        )
    ).reshape(per_device, 64, value_count)
    return patches, my_frac


def local(tracers, shifts, diffusivity, source_patch):
    lat_count = lax.axis_size("lat")
    lat_index = lax.axis_index("lat")
    row_count, col_count, value_count = tracers.shape
    band_rows = row_count // 8
    band_cols = col_count // 8
    per_device = band_rows * band_cols
    per_level = value_count // LEV
    total_rows = row_count * lat_count
    weights = column_area(lat_index * row_count, row_count, total_rows)
    target_part = column_mass(tracers, weights)

    patches, frac = departed(tracers, source_patch[0], shifts[0])
    advected = from_patches(levels(spatial(patches, frac[0], frac[1]), frac[2]), band_rows, band_cols)
    first, k_wide = diffuse_first(advected, diffusivity)
    first_part = column_mass(first, weights)

    patches, frac = departed(first, source_patch[1], shifts[1])
    plane = plane_weights(frac[0], frac[1])
    planar = jnp.einsum("nij,njv->niv", plane, patches, precision=lax.Precision.HIGHEST)
    weight_z = cubic_matrix(frac[2], LEV)

    area_wide = column_area(lat_index * row_count - 1, row_count + 2, total_rows)
    flux = area_wide * k_wide
    g = weights - 2.0 * flux[1:-1] + flux[:-2] + flux[2:]
    g_cols = jnp.broadcast_to(g.reshape(band_rows, 1, 8, 1), (band_rows, band_cols, 8, 8))
    row_weights = jnp.einsum(
        "pi,pij->pj", g_cols.reshape(per_device, 64), plane, precision=lax.Precision.HIGHEST
    )
    weighted = jnp.einsum(
        "pj,pjv->pv", row_weights, patches, precision=lax.Precision.HIGHEST
    ).reshape(per_device, LEV, per_level)
    mix_part = jnp.einsum(
        "plm,pmt->lmt", weight_z, weighted, precision=lax.Precision.HIGHEST
    )
    field_planar = lax.optimization_barrier(from_patches(planar, band_rows, band_cols))
    partial = jnp.concatenate([target_part, first_part, mix_part.reshape(-1)])
    members = lat_count * lax.axis_size("lon")
    totals = jnp.sum(
        lax.all_to_all(
            jnp.broadcast_to(partial, (members,) + partial.shape), ("lat", "lon"), 0, 0, tiled=True
        ),
        axis=0,
    )
    target = totals[:value_count]
    first_mass = totals[value_count : 2 * value_count]
    mix = totals[2 * value_count :].reshape(LEV, LEV, per_level)
    first_ratio = target / first_mass
    second_mass = jnp.sum(first_ratio.reshape(LEV, per_level)[None] * mix, axis=1).reshape(
        value_count
    )
    second_ratio = target / second_mass
    advected = levels_cols(
        (field_planar * first_ratio).reshape(band_rows, 8, band_cols, 8, value_count),
        weight_z.reshape(band_rows, 1, band_cols, 1, LEV, LEV),
    ).reshape(row_count, col_count, value_count)
    return diffuse(advected, diffusivity, 0) * second_ratio[None, None, :]


def solution(mesh):
    return jax.shard_map(
        local,
        mesh=mesh,
        in_specs=(
            P(("groups", "lat"), "lon", None),
            P("groups", None, None, None),
            P("lat"),
            P("groups", None, None),
        ),
        out_specs=P(("groups", "lat"), "lon", None),
        check_vma=False,
    )
```

```python
import math

import jax
import jax.numpy as jnp
from jax import lax
from jax.sharding import PartitionSpec as P

LEV = 4
STEPS = 2
CAP = 4


def all_sum(value, axes, rider=None):
    rider_done = None
    for axis in axes:
        count = lax.axis_size(axis)
        if count & (count - 1):
            value = lax.psum(value, axis)
            continue
        distance = 1
        while distance < count:
            value = value + lax.ppermute(
                value, axis, [(i, i ^ distance) for i in range(count)]
            )
            if rider is not None:
                value, rider = lax.optimization_barrier((value, rider))
                rider_done, rider = rider, None
            distance *= 2
    if rider_done is None and rider is None:
        return value
    return value, rider if rider_done is None else rider_done


def neighbour_halos(lo_edge, hi_edge, axis, closed):
    count = lax.axis_size(axis)
    if count % 2:
        ends = count if closed else count - 1
        from_lo = lax.ppermute(hi_edge, axis, [(i, (i + 1) % count) for i in range(ends)])
        from_hi = lax.ppermute(lo_edge, axis, [((i + 1) % count, i) for i in range(ends)])
        return from_lo, from_hi
    even = lax.axis_index(axis) % 2 == 0
    first = lax.ppermute(
        jnp.where(even, hi_edge, lo_edge), axis, [(i, i ^ 1) for i in range(count)]
    )
    pairs = []
    for i in range(1, count, 2):
        if i + 1 < count:
            pairs += [(i, i + 1), (i + 1, i)]
        elif closed:
            pairs += [(i, 0), (0, i)]
    second = lax.ppermute(jnp.where(even, lo_edge, hi_edge), axis, pairs)
    return jnp.where(even, second, first), jnp.where(even, first, second)


def extended(cells, sides, width, closed):
    for axis, dim in sides:
        count = lax.axis_size(axis)
        ends = count if closed else count - 1
        head = lax.slice_in_dim(cells, 0, width, axis=dim)
        tail = lax.slice_in_dim(cells, cells.shape[dim] - width, cells.shape[dim], axis=dim)
        from_lo, from_hi = neighbour_halos(head, tail, axis, closed)
        cells = jnp.concatenate([from_lo, cells, from_hi], axis=dim)
    return cells


def cubic_weights(fraction):
    first_term = -fraction * (fraction - 1.0) * (fraction - 2.0) / 6.0
    second_term = (fraction + 1.0) * (fraction - 1.0) * (fraction - 2.0) / 2.0
    third_term = -(fraction + 1.0) * fraction * (fraction - 2.0) / 2.0
    fourth_term = (fraction + 1.0) * fraction * (fraction - 1.0) / 6.0
    return (first_term, second_term, third_term, fourth_term)


def cubic_matrix(fraction, extent):
    places = jnp.arange(extent)
    running = jnp.zeros(fraction.shape + (extent, extent), jnp.float32)
    for offset, weight in zip(range(-1, 3), cubic_weights(fraction)):
        target_col = jnp.clip(places + offset, 0, extent - 1)
        indicator = (target_col[:, None] == places[None, :]).astype(jnp.float32)
        running = running + weight[..., None, None] * indicator
    return running


def tap_sources(target, extent):
    return sorted({min(max(target + offset, 0), extent - 1) for offset in range(-1, 3)})


def plane_weights(fraction_y, fraction_x):
    rows = lax.broadcasted_iota(jnp.int32, (1, 64, 64), 1)
    cols = lax.broadcasted_iota(jnp.int32, (1, 64, 64), 2)

    def along(fraction, source, target):
        running = jnp.zeros((fraction.shape[0], 64, 64), jnp.float32)
        for offset, weight in zip(range(-1, 3), cubic_weights(fraction)):
            indicator = (jnp.clip(source + offset, 0, 7) == target).astype(jnp.float32)
            running = running + weight[:, None, None] * indicator
        return running

    return along(fraction_y, rows // 8, cols // 8) * along(fraction_x, rows % 8, cols % 8)


def spatial(patches, fraction_y, fraction_x):
    return jnp.einsum(
        "nij,njv->niv",
        plane_weights(fraction_y, fraction_x),
        patches,
        precision=lax.Precision.HIGHEST,
    )


def levels(flat, fraction_z):
    value_count = flat.shape[2]
    per_level = value_count // LEV
    weight_z = cubic_matrix(fraction_z, LEV)
    blocks = [flat[:, :, m * per_level : (m + 1) * per_level] for m in range(LEV)]
    out = []
    for level in range(LEV):
        acc = None
        for m in tap_sources(level, LEV):
            term = weight_z[:, level, m][:, None, None] * blocks[m]
            acc = term if acc is None else acc + term
        out.append(acc)
    return jnp.concatenate(out, axis=2)


def to_patches(state_field):
    band_rows = state_field.shape[0] // 8
    band_cols = state_field.shape[1] // 8
    return (
        state_field.reshape(band_rows, 8, band_cols, 8, -1)
        .transpose(0, 2, 1, 3, 4)
        .reshape(band_rows * band_cols, 64, -1)
    )


def from_patches(patches, band_rows, band_cols):
    return (
        patches.reshape(band_rows, band_cols, 8, 8, -1)
        .transpose(0, 2, 1, 3, 4)
        .reshape(band_rows * 8, band_cols * 8, -1)
    )


def column_area(first_row, row_count, total_rows):
    latitude = ((first_row + jnp.arange(row_count)).astype(jnp.float32) + 0.5) * (
        math.pi / total_rows
    ) - 0.5 * math.pi
    return jnp.cos(latitude)


def column_mass(state_field, weights):
    return jnp.sum(weights[:, None, None] * state_field, axis=(0, 1))


def diffuse(advected, diffusivity, row_dim):
    col_dim = row_dim + 1
    rows = advected.shape[row_dim]
    cols = advected.shape[col_dim]
    lon_wide = extended(advected, (("lon", col_dim),), 1, True)
    lat_wide = extended(advected, (("lat", row_dim),), 1, False)
    laplace = (
        lax.slice_in_dim(lat_wide, 2, rows + 2, axis=row_dim)
        + lax.slice_in_dim(lat_wide, 0, rows, axis=row_dim)
        + lax.slice_in_dim(lon_wide, 2, cols + 2, axis=col_dim)
        + lax.slice_in_dim(lon_wide, 0, cols, axis=col_dim)
        - 4.0 * advected
    )
    k_shape = [1] * advected.ndim
    k_shape[row_dim] = rows
    return advected + diffusivity.reshape(k_shape) * laplace


def levels_cols(values, weight_z, scale=None):
    value_count = values.shape[-1]
    per_level = value_count // LEV
    blocks = [values[..., m * per_level : (m + 1) * per_level] for m in range(LEV)]
    if scale is not None:
        blocks = [
            block * scale[m * per_level : (m + 1) * per_level] for m, block in enumerate(blocks)
        ]
    out = []
    for level in range(LEV):
        acc = None
        for m in tap_sources(level, LEV):
            term = weight_z[..., level, m][..., None] * blocks[m]
            acc = term if acc is None else acc + term
        out.append(acc)
    return jnp.concatenate(out, axis=-1)


def diffuse_first(advected, diffusivity):
    rows, cols, value_count = advected.shape
    count = lax.axis_size("lat")

    def pack(row, number):
        return jnp.concatenate(
            [row, jnp.broadcast_to(number, (1, 1, value_count))], axis=1
        )

    from_above, from_below = neighbour_halos(
        pack(advected[:1], diffusivity[0]),
        pack(advected[rows - 1 :], diffusivity[rows - 1]),
        "lat",
        False,
    )
    lat_wide = jnp.concatenate([from_above[:, :cols], advected, from_below[:, :cols]], axis=0)
    k_wide = jnp.concatenate([from_above[0, cols, :1], diffusivity, from_below[0, cols, :1]])
    lon_wide = extended(advected, (("lon", 1),), 1, True)
    laplace = (
        lat_wide[2:] + lat_wide[:-2] + lon_wide[:, 2:] + lon_wide[:, :-2] - 4.0 * advected
    )
    return advected + diffusivity[:, None, None] * laplace, k_wide


def departed(state_field, source_ids, shifts_now):
    lat_count = lax.axis_size("lat")
    lat_index = lax.axis_index("lat")
    lon_index = lax.axis_index("lon")
    row_count, col_count, value_count = state_field.shape
    band_rows = row_count // 8
    band_cols = col_count // 8
    per_device = band_rows * band_cols
    total_cols = source_ids.shape[1]
    devices = jnp.arange(lat_count)
    slot_range = jnp.arange(CAP)
    column_ids = lax.dynamic_slice_in_dim(
        source_ids, lon_index * band_cols, band_cols, 1
    ).reshape(lat_count, per_device)
    fractions = lax.dynamic_slice_in_dim(
        shifts_now, lon_index * band_cols, band_cols, 2
    ).reshape(3, lat_count, per_device)
    source_row = column_ids // total_cols
    source_dev = source_row // band_rows
    source_local = (
        source_row % band_rows * band_cols + column_ids % total_cols - lon_index * band_cols
    )
    remote = source_dev != devices[:, None]
    matches = (source_dev[:, :, None] == devices[None, None, :]) & remote[:, :, None]
    slot_ranks = jnp.cumsum(matches.astype(jnp.int32), axis=1) - 1
    slot_of = jnp.sum(jnp.where(matches, slot_ranks, 0), axis=2)
    owned_here = remote & (source_dev == lat_index)
    sending = owned_here[:, :, None] & (slot_of[:, :, None] == slot_range[None, None, :])
    send_local = jnp.sum(jnp.where(sending, source_local[:, :, None], 0), axis=1)
    own_patches = to_patches(state_field)
    outgoing = own_patches[send_local.reshape(-1)].reshape(lat_count, CAP, 64, value_count)
    my_dev = lax.dynamic_index_in_dim(source_dev, lat_index, 0, keepdims=False)
    my_slot = lax.dynamic_index_in_dim(slot_of, lat_index, 0, keepdims=False)
    my_local = lax.dynamic_index_in_dim(source_local, lat_index, 0, keepdims=False)
    my_remote = lax.dynamic_index_in_dim(remote, lat_index, 0, keepdims=False)
    my_frac = lax.dynamic_index_in_dim(fractions, lat_index, 1, keepdims=False)
    arrived = lax.all_to_all(outgoing, "lat", 0, 0, tiled=True).reshape(
        lat_count * CAP, 64, value_count
    )
    pick_index = my_dev * CAP + my_slot
    take_near = (my_local[:, None] == jnp.arange(per_device)[None, :]) & ~my_remote[:, None]
    take_far = (pick_index[:, None] == jnp.arange(lat_count * CAP)[None, :]) & my_remote[:, None]
    patches = (
        jnp.dot(
            take_near.astype(jnp.float32),
            own_patches.reshape(per_device, -1),
            precision=lax.Precision.HIGHEST,
        )
        + jnp.dot(
            take_far.astype(jnp.float32),
            arrived.reshape(lat_count * CAP, -1),
            precision=lax.Precision.HIGHEST,
        )
    ).reshape(per_device, 64, value_count)
    return patches, my_frac


def local(tracers, shifts, diffusivity, source_patch):
    lat_count = lax.axis_size("lat")
    lat_index = lax.axis_index("lat")
    row_count, col_count, value_count = tracers.shape
    band_rows = row_count // 8
    band_cols = col_count // 8
    per_device = band_rows * band_cols
    per_level = value_count // LEV
    total_rows = row_count * lat_count
    weights = column_area(lat_index * row_count, row_count, total_rows)
    target_part = column_mass(tracers, weights)

    patches, frac = departed(tracers, source_patch[0], shifts[0])
    advected = from_patches(levels(spatial(patches, frac[0], frac[1]), frac[2]), band_rows, band_cols)
    first, k_wide = diffuse_first(advected, diffusivity)
    first_part = column_mass(first, weights)

    patches, frac = departed(first, source_patch[1], shifts[1])
    plane = plane_weights(frac[0], frac[1])
    planar = jnp.einsum("nij,njv->niv", plane, patches, precision=lax.Precision.HIGHEST)
    weight_z = cubic_matrix(frac[2], LEV)

    area_wide = column_area(lat_index * row_count - 1, row_count + 2, total_rows)
    flux = area_wide * k_wide
    g = weights - 2.0 * flux[1:-1] + flux[:-2] + flux[2:]
    g_cols = jnp.broadcast_to(g.reshape(band_rows, 1, 8, 1), (band_rows, band_cols, 8, 8))
    row_weights = jnp.einsum(
        "pi,pij->pj", g_cols.reshape(per_device, 64), plane, precision=lax.Precision.HIGHEST
    )
    weighted = jnp.einsum(
        "pj,pjv->pv", row_weights, patches, precision=lax.Precision.HIGHEST
    ).reshape(per_device, LEV, per_level)
    mix_part = jnp.einsum(
        "plm,pmt->lmt", weight_z, weighted, precision=lax.Precision.HIGHEST
    )
    field_planar = lax.optimization_barrier(from_patches(planar, band_rows, band_cols))
    partial = jnp.concatenate([target_part, first_part, mix_part.reshape(-1)])
    members = lat_count * lax.axis_size("lon")
    totals = jnp.sum(
        lax.all_to_all(
            jnp.broadcast_to(partial, (members,) + partial.shape), ("lat", "lon"), 0, 0, tiled=True
        ),
        axis=0,
    )
    target = totals[:value_count]
    first_mass = totals[value_count : 2 * value_count]
    mix = totals[2 * value_count :].reshape(LEV, LEV, per_level)
    first_ratio = target / first_mass
    second_mass = jnp.sum(first_ratio.reshape(LEV, per_level)[None] * mix, axis=1).reshape(
        value_count
    )
    second_ratio = target / second_mass
    advected = levels_cols(
        field_planar.reshape(band_rows, 8, band_cols, 8, value_count),
        weight_z.reshape(band_rows, 1, band_cols, 1, LEV, LEV),
        first_ratio,
    ).reshape(row_count, col_count, value_count)
    return diffuse(advected, diffusivity, 0) * second_ratio[None, None, :]


def solution(mesh):
    return jax.shard_map(
        local,
        mesh=mesh,
        in_specs=(
            P(("groups", "lat"), "lon", None),
            P("groups", None, None, None),
            P("lat"),
            P("groups", None, None),
        ),
        out_specs=P(("groups", "lat"), "lon", None),
        check_vma=False,
    )
```

```python
import math

import jax
import jax.numpy as jnp
from jax import lax
from jax.sharding import PartitionSpec as P

LEV = 4
STEPS = 2
CAP = 4


def all_sum(value, axes, rider=None):
    rider_done = None
    for axis in axes:
        count = lax.axis_size(axis)
        if count & (count - 1):
            value = lax.psum(value, axis)
            continue
        distance = 1
        while distance < count:
            value = value + lax.ppermute(
                value, axis, [(i, i ^ distance) for i in range(count)]
            )
            if rider is not None:
                value, rider = lax.optimization_barrier((value, rider))
                rider_done, rider = rider, None
            distance *= 2
    if rider_done is None and rider is None:
        return value
    return value, rider if rider_done is None else rider_done


def neighbour_halos(lo_edge, hi_edge, axis, closed):
    count = lax.axis_size(axis)
    if count % 2:
        ends = count if closed else count - 1
        from_lo = lax.ppermute(hi_edge, axis, [(i, (i + 1) % count) for i in range(ends)])
        from_hi = lax.ppermute(lo_edge, axis, [((i + 1) % count, i) for i in range(ends)])
        return from_lo, from_hi
    even = lax.axis_index(axis) % 2 == 0
    first = lax.ppermute(
        jnp.where(even, hi_edge, lo_edge), axis, [(i, i ^ 1) for i in range(count)]
    )
    pairs = []
    for i in range(1, count, 2):
        if i + 1 < count:
            pairs += [(i, i + 1), (i + 1, i)]
        elif closed:
            pairs += [(i, 0), (0, i)]
    second = lax.ppermute(jnp.where(even, lo_edge, hi_edge), axis, pairs)
    return jnp.where(even, second, first), jnp.where(even, first, second)


def extended(cells, sides, width, closed):
    for axis, dim in sides:
        count = lax.axis_size(axis)
        ends = count if closed else count - 1
        head = lax.slice_in_dim(cells, 0, width, axis=dim)
        tail = lax.slice_in_dim(cells, cells.shape[dim] - width, cells.shape[dim], axis=dim)
        from_lo, from_hi = neighbour_halos(head, tail, axis, closed)
        cells = jnp.concatenate([from_lo, cells, from_hi], axis=dim)
    return cells


def cubic_weights(fraction):
    first_term = -fraction * (fraction - 1.0) * (fraction - 2.0) / 6.0
    second_term = (fraction + 1.0) * (fraction - 1.0) * (fraction - 2.0) / 2.0
    third_term = -(fraction + 1.0) * fraction * (fraction - 2.0) / 2.0
    fourth_term = (fraction + 1.0) * fraction * (fraction - 1.0) / 6.0
    return (first_term, second_term, third_term, fourth_term)


def cubic_matrix(fraction, extent):
    places = jnp.arange(extent)
    running = jnp.zeros(fraction.shape + (extent, extent), jnp.float32)
    for offset, weight in zip(range(-1, 3), cubic_weights(fraction)):
        target_col = jnp.clip(places + offset, 0, extent - 1)
        indicator = (target_col[:, None] == places[None, :]).astype(jnp.float32)
        running = running + weight[..., None, None] * indicator
    return running


def tap_sources(target, extent):
    return sorted({min(max(target + offset, 0), extent - 1) for offset in range(-1, 3)})


def plane_weights(fraction_y, fraction_x):
    rows = lax.broadcasted_iota(jnp.int32, (1, 64, 64), 1)
    cols = lax.broadcasted_iota(jnp.int32, (1, 64, 64), 2)

    def along(fraction, source, target):
        running = jnp.zeros((fraction.shape[0], 64, 64), jnp.float32)
        for offset, weight in zip(range(-1, 3), cubic_weights(fraction)):
            indicator = (jnp.clip(source + offset, 0, 7) == target).astype(jnp.float32)
            running = running + weight[:, None, None] * indicator
        return running

    return along(fraction_y, rows // 8, cols // 8) * along(fraction_x, rows % 8, cols % 8)


def spatial(patches, fraction_y, fraction_x):
    return jnp.einsum(
        "nij,njv->niv",
        plane_weights(fraction_y, fraction_x),
        patches,
        precision=lax.Precision.HIGHEST,
    )


def levels(flat, fraction_z):
    value_count = flat.shape[2]
    per_level = value_count // LEV
    weight_z = cubic_matrix(fraction_z, LEV)
    blocks = [flat[:, :, m * per_level : (m + 1) * per_level] for m in range(LEV)]
    out = []
    for level in range(LEV):
        acc = None
        for m in tap_sources(level, LEV):
            term = weight_z[:, level, m][:, None, None] * blocks[m]
            acc = term if acc is None else acc + term
        out.append(acc)
    return jnp.concatenate(out, axis=2)


def to_patches(state_field):
    band_rows = state_field.shape[0] // 8
    band_cols = state_field.shape[1] // 8
    return (
        state_field.reshape(band_rows, 8, band_cols, 8, -1)
        .transpose(0, 2, 1, 3, 4)
        .reshape(band_rows * band_cols, 64, -1)
    )


def from_patches(patches, band_rows, band_cols):
    return (
        patches.reshape(band_rows, band_cols, 8, 8, -1)
        .transpose(0, 2, 1, 3, 4)
        .reshape(band_rows * 8, band_cols * 8, -1)
    )


def column_area(first_row, row_count, total_rows):
    latitude = ((first_row + jnp.arange(row_count)).astype(jnp.float32) + 0.5) * (
        math.pi / total_rows
    ) - 0.5 * math.pi
    return jnp.cos(latitude)


def column_mass(state_field, weights):
    return jnp.sum(weights[:, None, None] * state_field, axis=(0, 1))


def diffuse(advected, diffusivity, row_dim):
    col_dim = row_dim + 1
    rows = advected.shape[row_dim]
    cols = advected.shape[col_dim]
    lon_wide = extended(advected, (("lon", col_dim),), 1, True)
    lat_wide = extended(advected, (("lat", row_dim),), 1, False)
    laplace = (
        lax.slice_in_dim(lat_wide, 2, rows + 2, axis=row_dim)
        + lax.slice_in_dim(lat_wide, 0, rows, axis=row_dim)
        + lax.slice_in_dim(lon_wide, 2, cols + 2, axis=col_dim)
        + lax.slice_in_dim(lon_wide, 0, cols, axis=col_dim)
        - 4.0 * advected
    )
    k_shape = [1] * advected.ndim
    k_shape[row_dim] = rows
    return advected + diffusivity.reshape(k_shape) * laplace


def levels_cols(values, weight_z):
    value_count = values.shape[-1]
    per_level = value_count // LEV
    blocks = [values[..., m * per_level : (m + 1) * per_level] for m in range(LEV)]
    out = []
    for level in range(LEV):
        acc = None
        for m in tap_sources(level, LEV):
            term = weight_z[..., level, m][..., None] * blocks[m]
            acc = term if acc is None else acc + term
        out.append(acc)
    return jnp.concatenate(out, axis=-1)


def diffuse_first(advected, diffusivity):
    rows, cols, value_count = advected.shape
    count = lax.axis_size("lat")

    def pack(row, number):
        return jnp.concatenate(
            [row, jnp.broadcast_to(number, (1, 1, value_count))], axis=1
        )

    from_above, from_below = neighbour_halos(
        pack(advected[:1], diffusivity[0]),
        pack(advected[rows - 1 :], diffusivity[rows - 1]),
        "lat",
        False,
    )
    lat_wide = jnp.concatenate([from_above[:, :cols], advected, from_below[:, :cols]], axis=0)
    k_wide = jnp.concatenate([from_above[0, cols, :1], diffusivity, from_below[0, cols, :1]])
    lon_wide = extended(advected, (("lon", 1),), 1, True)
    laplace = (
        lat_wide[2:] + lat_wide[:-2] + lon_wide[:, 2:] + lon_wide[:, :-2] - 4.0 * advected
    )
    return advected + diffusivity[:, None, None] * laplace, k_wide


def departed(state_field, source_ids, shifts_now, premix=False):
    lat_count = lax.axis_size("lat")
    lat_index = lax.axis_index("lat")
    lon_index = lax.axis_index("lon")
    row_count, col_count, value_count = state_field.shape
    band_rows = row_count // 8
    band_cols = col_count // 8
    per_device = band_rows * band_cols
    total_cols = source_ids.shape[1]
    devices = jnp.arange(lat_count)
    slot_range = jnp.arange(CAP)
    column_ids = lax.dynamic_slice_in_dim(
        source_ids, lon_index * band_cols, band_cols, 1
    ).reshape(lat_count, per_device)
    fractions = lax.dynamic_slice_in_dim(
        shifts_now, lon_index * band_cols, band_cols, 2
    ).reshape(3, lat_count, per_device)
    source_row = column_ids // total_cols
    source_dev = source_row // band_rows
    source_local = (
        source_row % band_rows * band_cols + column_ids % total_cols - lon_index * band_cols
    )
    remote = source_dev != devices[:, None]
    matches = (source_dev[:, :, None] == devices[None, None, :]) & remote[:, :, None]
    slot_ranks = jnp.cumsum(matches.astype(jnp.int32), axis=1) - 1
    slot_of = jnp.sum(jnp.where(matches, slot_ranks, 0), axis=2)
    owned_here = remote & (source_dev == lat_index)
    sending = owned_here[:, :, None] & (slot_of[:, :, None] == slot_range[None, None, :])
    send_local = jnp.sum(jnp.where(sending, source_local[:, :, None], 0), axis=1)
    own_patches = to_patches(state_field)
    outgoing = own_patches[send_local.reshape(-1)].reshape(lat_count, CAP, 64, value_count)
    my_dev = lax.dynamic_index_in_dim(source_dev, lat_index, 0, keepdims=False)
    my_slot = lax.dynamic_index_in_dim(slot_of, lat_index, 0, keepdims=False)
    my_local = lax.dynamic_index_in_dim(source_local, lat_index, 0, keepdims=False)
    my_remote = lax.dynamic_index_in_dim(remote, lat_index, 0, keepdims=False)
    my_frac = lax.dynamic_index_in_dim(fractions, lat_index, 1, keepdims=False)
    arrived = lax.all_to_all(outgoing, "lat", 0, 0, tiled=True).reshape(
        lat_count * CAP, 64, value_count
    )
    pick_index = my_dev * CAP + my_slot
    take_near = (my_local[:, None] == jnp.arange(per_device)[None, :]) & ~my_remote[:, None]
    take_far = (pick_index[:, None] == jnp.arange(lat_count * CAP)[None, :]) & my_remote[:, None]
    near = jnp.dot(
        take_near.astype(jnp.float32),
        own_patches.reshape(per_device, -1),
        precision=lax.Precision.HIGHEST,
    ).reshape(per_device, 64, value_count)
    if premix:
        near = levels(near, my_frac[2])
        slot_z = jnp.sum(jnp.where(take_far, my_frac[2][:, None], 0.0), axis=0)
        arrived = levels(arrived, slot_z)
    patches = near + jnp.dot(
        take_far.astype(jnp.float32),
        arrived.reshape(lat_count * CAP, -1),
        precision=lax.Precision.HIGHEST,
    ).reshape(per_device, 64, value_count)
    return patches, my_frac


def local(tracers, shifts, diffusivity, source_patch):
    lat_count = lax.axis_size("lat")
    lat_index = lax.axis_index("lat")
    row_count, col_count, value_count = tracers.shape
    band_rows = row_count // 8
    band_cols = col_count // 8
    per_device = band_rows * band_cols
    per_level = value_count // LEV
    total_rows = row_count * lat_count
    weights = column_area(lat_index * row_count, row_count, total_rows)
    target_part = column_mass(tracers, weights)

    patches, frac = departed(tracers, source_patch[0], shifts[0], premix=True)
    advected = from_patches(spatial(patches, frac[0], frac[1]), band_rows, band_cols)
    first, k_wide = diffuse_first(advected, diffusivity)
    first_part = column_mass(first, weights)

    patches, frac = departed(first, source_patch[1], shifts[1])
    plane = plane_weights(frac[0], frac[1])
    planar = jnp.einsum("nij,njv->niv", plane, patches, precision=lax.Precision.HIGHEST)
    weight_z = cubic_matrix(frac[2], LEV)

    area_wide = column_area(lat_index * row_count - 1, row_count + 2, total_rows)
    flux = area_wide * k_wide
    g = weights - 2.0 * flux[1:-1] + flux[:-2] + flux[2:]
    g_cols = jnp.broadcast_to(g.reshape(band_rows, 1, 8, 1), (band_rows, band_cols, 8, 8))
    row_weights = jnp.einsum(
        "pi,pij->pj", g_cols.reshape(per_device, 64), plane, precision=lax.Precision.HIGHEST
    )
    weighted = jnp.einsum(
        "pj,pjv->pv", row_weights, patches, precision=lax.Precision.HIGHEST
    ).reshape(per_device, LEV, per_level)
    mix_part = jnp.einsum(
        "plm,pmt->lmt", weight_z, weighted, precision=lax.Precision.HIGHEST
    )
    field_planar = lax.optimization_barrier(from_patches(planar, band_rows, band_cols))
    partial = jnp.concatenate([target_part, first_part, mix_part.reshape(-1)])
    members = lat_count * lax.axis_size("lon")
    totals = jnp.sum(
        lax.all_to_all(
            jnp.broadcast_to(partial, (members,) + partial.shape), ("lat", "lon"), 0, 0, tiled=True
        ),
        axis=0,
    )
    target = totals[:value_count]
    first_mass = totals[value_count : 2 * value_count]
    mix = totals[2 * value_count :].reshape(LEV, LEV, per_level)
    first_ratio = target / first_mass
    second_mass = jnp.sum(first_ratio.reshape(LEV, per_level)[None] * mix, axis=1).reshape(
        value_count
    )
    second_ratio = target / second_mass
    advected = levels_cols(
        (field_planar * first_ratio).reshape(band_rows, 8, band_cols, 8, value_count),
        weight_z.reshape(band_rows, 1, band_cols, 1, LEV, LEV),
    ).reshape(row_count, col_count, value_count)
    return diffuse(advected, diffusivity, 0) * second_ratio[None, None, :]


def solution(mesh):
    return jax.shard_map(
        local,
        mesh=mesh,
        in_specs=(
            P(("groups", "lat"), "lon", None),
            P("groups", None, None, None),
            P("lat"),
            P("groups", None, None),
        ),
        out_specs=P(("groups", "lat"), "lon", None),
        check_vma=False,
    )
```

```python
import math

import jax
import jax.numpy as jnp
from jax import lax
from jax.sharding import PartitionSpec as P

LEV = 4
STEPS = 2
CAP = 4


def all_sum(value, axes, rider=None):
    rider_done = None
    for axis in axes:
        count = lax.axis_size(axis)
        if count & (count - 1):
            value = lax.psum(value, axis)
            continue
        distance = 1
        while distance < count:
            value = value + lax.ppermute(
                value, axis, [(i, i ^ distance) for i in range(count)]
            )
            if rider is not None:
                value, rider = lax.optimization_barrier((value, rider))
                rider_done, rider = rider, None
            distance *= 2
    if rider_done is None and rider is None:
        return value
    return value, rider if rider_done is None else rider_done


def neighbour_halos(lo_edge, hi_edge, axis, closed):
    count = lax.axis_size(axis)
    if count % 2:
        ends = count if closed else count - 1
        from_lo = lax.ppermute(hi_edge, axis, [(i, (i + 1) % count) for i in range(ends)])
        from_hi = lax.ppermute(lo_edge, axis, [((i + 1) % count, i) for i in range(ends)])
        return from_lo, from_hi
    even = lax.axis_index(axis) % 2 == 0
    first = lax.ppermute(
        jnp.where(even, hi_edge, lo_edge), axis, [(i, i ^ 1) for i in range(count)]
    )
    pairs = []
    for i in range(1, count, 2):
        if i + 1 < count:
            pairs += [(i, i + 1), (i + 1, i)]
        elif closed:
            pairs += [(i, 0), (0, i)]
    second = lax.ppermute(jnp.where(even, lo_edge, hi_edge), axis, pairs)
    return jnp.where(even, second, first), jnp.where(even, first, second)


def extended(cells, sides, width, closed):
    for axis, dim in sides:
        count = lax.axis_size(axis)
        ends = count if closed else count - 1
        head = lax.slice_in_dim(cells, 0, width, axis=dim)
        tail = lax.slice_in_dim(cells, cells.shape[dim] - width, cells.shape[dim], axis=dim)
        from_lo, from_hi = neighbour_halos(head, tail, axis, closed)
        cells = jnp.concatenate([from_lo, cells, from_hi], axis=dim)
    return cells


def cubic_weights(fraction):
    first_term = -fraction * (fraction - 1.0) * (fraction - 2.0) / 6.0
    second_term = (fraction + 1.0) * (fraction - 1.0) * (fraction - 2.0) / 2.0
    third_term = -(fraction + 1.0) * fraction * (fraction - 2.0) / 2.0
    fourth_term = (fraction + 1.0) * fraction * (fraction - 1.0) / 6.0
    return (first_term, second_term, third_term, fourth_term)


def cubic_matrix(fraction, extent):
    places = jnp.arange(extent)
    running = jnp.zeros(fraction.shape + (extent, extent), jnp.float32)
    for offset, weight in zip(range(-1, 3), cubic_weights(fraction)):
        target_col = jnp.clip(places + offset, 0, extent - 1)
        indicator = (target_col[:, None] == places[None, :]).astype(jnp.float32)
        running = running + weight[..., None, None] * indicator
    return running


def tap_sources(target, extent):
    return sorted({min(max(target + offset, 0), extent - 1) for offset in range(-1, 3)})


def plane_weights(fraction_y, fraction_x):
    rows = lax.broadcasted_iota(jnp.int32, (1, 64, 64), 1)
    cols = lax.broadcasted_iota(jnp.int32, (1, 64, 64), 2)

    def along(fraction, source, target):
        running = jnp.zeros((fraction.shape[0], 64, 64), jnp.float32)
        for offset, weight in zip(range(-1, 3), cubic_weights(fraction)):
            indicator = (jnp.clip(source + offset, 0, 7) == target).astype(jnp.float32)
            running = running + weight[:, None, None] * indicator
        return running

    return along(fraction_y, rows // 8, cols // 8) * along(fraction_x, rows % 8, cols % 8)


def spatial(patches, fraction_y, fraction_x):
    return jnp.einsum(
        "nij,njv->niv",
        plane_weights(fraction_y, fraction_x),
        patches,
        precision=lax.Precision.HIGHEST,
    )


def levels(flat, fraction_z):
    value_count = flat.shape[2]
    per_level = value_count // LEV
    weight_z = cubic_matrix(fraction_z, LEV)
    blocks = [flat[:, :, m * per_level : (m + 1) * per_level] for m in range(LEV)]
    out = []
    for level in range(LEV):
        acc = None
        for m in tap_sources(level, LEV):
            term = weight_z[:, level, m][:, None, None] * blocks[m]
            acc = term if acc is None else acc + term
        out.append(acc)
    return jnp.concatenate(out, axis=2)


def to_patches(state_field):
    band_rows = state_field.shape[0] // 8
    band_cols = state_field.shape[1] // 8
    return (
        state_field.reshape(band_rows, 8, band_cols, 8, -1)
        .transpose(0, 2, 1, 3, 4)
        .reshape(band_rows * band_cols, 64, -1)
    )


def from_patches(patches, band_rows, band_cols):
    return (
        patches.reshape(band_rows, band_cols, 8, 8, -1)
        .transpose(0, 2, 1, 3, 4)
        .reshape(band_rows * 8, band_cols * 8, -1)
    )


def column_area(first_row, row_count, total_rows):
    latitude = ((first_row + jnp.arange(row_count)).astype(jnp.float32) + 0.5) * (
        math.pi / total_rows
    ) - 0.5 * math.pi
    return jnp.cos(latitude)


def column_mass(state_field, weights):
    return jnp.sum(weights[:, None, None] * state_field, axis=(0, 1))


def diffuse(advected, diffusivity, row_dim):
    col_dim = row_dim + 1
    rows = advected.shape[row_dim]
    cols = advected.shape[col_dim]
    lon_wide = extended(advected, (("lon", col_dim),), 1, True)
    lat_wide = extended(advected, (("lat", row_dim),), 1, False)
    laplace = (
        lax.slice_in_dim(lat_wide, 2, rows + 2, axis=row_dim)
        + lax.slice_in_dim(lat_wide, 0, rows, axis=row_dim)
        + lax.slice_in_dim(lon_wide, 2, cols + 2, axis=col_dim)
        + lax.slice_in_dim(lon_wide, 0, cols, axis=col_dim)
        - 4.0 * advected
    )
    k_shape = [1] * advected.ndim
    k_shape[row_dim] = rows
    return advected + diffusivity.reshape(k_shape) * laplace


def levels_cols(values, weight_z):
    value_count = values.shape[-1]
    per_level = value_count // LEV
    blocks = [values[..., m * per_level : (m + 1) * per_level] for m in range(LEV)]
    out = []
    for level in range(LEV):
        acc = None
        for m in tap_sources(level, LEV):
            term = weight_z[..., level, m][..., None] * blocks[m]
            acc = term if acc is None else acc + term
        out.append(acc)
    return jnp.concatenate(out, axis=-1)


def diffuse_first(advected, diffusivity):
    rows, cols, value_count = advected.shape
    count = lax.axis_size("lat")

    def pack(row, number):
        return jnp.concatenate(
            [row, jnp.broadcast_to(number, (1, 1, value_count))], axis=1
        )

    from_above, from_below = neighbour_halos(
        pack(advected[:1], diffusivity[0]),
        pack(advected[rows - 1 :], diffusivity[rows - 1]),
        "lat",
        False,
    )
    lat_wide = jnp.concatenate([from_above[:, :cols], advected, from_below[:, :cols]], axis=0)
    k_wide = jnp.concatenate([from_above[0, cols, :1], diffusivity, from_below[0, cols, :1]])
    lon_wide = extended(advected, (("lon", 1),), 1, True)
    laplace = (
        lat_wide[2:] + lat_wide[:-2] + lon_wide[:, 2:] + lon_wide[:, :-2] - 4.0 * advected
    )
    return advected + diffusivity[:, None, None] * laplace, k_wide


def departed(state_field, source_ids, shifts_now):
    lat_count = lax.axis_size("lat")
    lat_index = lax.axis_index("lat")
    lon_index = lax.axis_index("lon")
    row_count, col_count, value_count = state_field.shape
    band_rows = row_count // 8
    band_cols = col_count // 8
    per_device = band_rows * band_cols
    total_cols = source_ids.shape[1]
    devices = jnp.arange(lat_count)
    slot_range = jnp.arange(CAP)
    column_ids = lax.dynamic_slice_in_dim(
        source_ids, lon_index * band_cols, band_cols, 1
    ).reshape(lat_count, per_device)
    fractions = lax.dynamic_slice_in_dim(
        shifts_now, lon_index * band_cols, band_cols, 2
    ).reshape(3, lat_count, per_device)
    source_row = column_ids // total_cols
    source_dev = source_row // band_rows
    source_local = (
        source_row % band_rows * band_cols + column_ids % total_cols - lon_index * band_cols
    )
    remote = source_dev != devices[:, None]
    matches = (source_dev[:, :, None] == devices[None, None, :]) & remote[:, :, None]
    slot_ranks = jnp.cumsum(matches.astype(jnp.int32), axis=1) - 1
    slot_of = jnp.sum(jnp.where(matches, slot_ranks, 0), axis=2)
    owned_here = remote & (source_dev == lat_index)
    sending = owned_here[:, :, None] & (slot_of[:, :, None] == slot_range[None, None, :])
    send_local = jnp.sum(jnp.where(sending, source_local[:, :, None], 0), axis=1)
    own_patches = to_patches(state_field)
    outgoing = own_patches[send_local.reshape(-1)].reshape(lat_count, CAP, 64, value_count)
    my_dev = lax.dynamic_index_in_dim(source_dev, lat_index, 0, keepdims=False)
    my_slot = lax.dynamic_index_in_dim(slot_of, lat_index, 0, keepdims=False)
    my_local = lax.dynamic_index_in_dim(source_local, lat_index, 0, keepdims=False)
    my_remote = lax.dynamic_index_in_dim(remote, lat_index, 0, keepdims=False)
    my_frac = lax.dynamic_index_in_dim(fractions, lat_index, 1, keepdims=False)
    arrived = lax.all_to_all(outgoing, "lat", 0, 0, tiled=True).reshape(
        lat_count * CAP, 64, value_count
    )
    pick_index = my_dev * CAP + my_slot
    take_near = (my_local[:, None] == jnp.arange(per_device)[None, :]) & ~my_remote[:, None]
    take_far = (pick_index[:, None] == jnp.arange(lat_count * CAP)[None, :]) & my_remote[:, None]
    patches = (
        jnp.dot(
            take_near.astype(jnp.float32),
            own_patches.reshape(per_device, -1),
            precision=lax.Precision.HIGHEST,
        )
        + jnp.dot(
            take_far.astype(jnp.float32),
            arrived.reshape(lat_count * CAP, -1),
            precision=lax.Precision.HIGHEST,
        )
    ).reshape(per_device, 64, value_count)
    return patches, my_frac


def local(tracers, shifts, diffusivity, source_patch):
    lat_count = lax.axis_size("lat")
    lat_index = lax.axis_index("lat")
    row_count, col_count, value_count = tracers.shape
    band_rows = row_count // 8
    band_cols = col_count // 8
    per_device = band_rows * band_cols
    per_level = value_count // LEV
    total_rows = row_count * lat_count
    weights = column_area(lat_index * row_count, row_count, total_rows)
    target_part = column_mass(tracers, weights)

    patches, frac = departed(tracers, source_patch[0], shifts[0])
    advected = from_patches(levels(spatial(patches, frac[0], frac[1]), frac[2]), band_rows, band_cols)
    first, k_wide = diffuse_first(advected, diffusivity)
    first_part = column_mass(first, weights)

    patches, frac = departed(first, source_patch[1], shifts[1])
    plane = plane_weights(frac[0], frac[1])
    planar = jnp.einsum("nij,njv->niv", plane, patches, precision=lax.Precision.HIGHEST)
    weight_z = cubic_matrix(frac[2], LEV)

    area_wide = column_area(lat_index * row_count - 1, row_count + 2, total_rows)
    flux = area_wide * k_wide
    g = weights - 2.0 * flux[1:-1] + flux[:-2] + flux[2:]
    g_cols = jnp.broadcast_to(g.reshape(band_rows, 1, 8, 1), (band_rows, band_cols, 8, 8))
    row_weights = jnp.einsum(
        "pi,pij->pj", g_cols.reshape(per_device, 64), plane, precision=lax.Precision.HIGHEST
    )
    weighted = jnp.einsum(
        "pj,pjv->pv", row_weights, patches, precision=lax.Precision.HIGHEST
    ).reshape(per_device, LEV, per_level)
    mix_part = jnp.einsum(
        "plm,pmt->lmt", weight_z, weighted, precision=lax.Precision.HIGHEST
    )
    field_planar = lax.optimization_barrier(from_patches(planar, band_rows, band_cols))
    partial = jnp.concatenate([target_part, first_part, mix_part.reshape(-1)])
    members = lat_count * lax.axis_size("lon")
    rows = partial.reshape(-1, value_count)
    totals = jnp.sum(
        lax.all_to_all(
            jnp.broadcast_to(rows[None], (members,) + rows.shape), ("lat", "lon"), 0, 0, tiled=True
        ).reshape(members, -1),
        axis=0,
    )
    target = totals[:value_count]
    first_mass = totals[value_count : 2 * value_count]
    mix = totals[2 * value_count :].reshape(LEV, LEV, per_level)
    first_ratio = target / first_mass
    second_mass = jnp.sum(first_ratio.reshape(LEV, per_level)[None] * mix, axis=1).reshape(
        value_count
    )
    second_ratio = target / second_mass
    advected = levels_cols(
        (field_planar * first_ratio).reshape(band_rows, 8, band_cols, 8, value_count),
        weight_z.reshape(band_rows, 1, band_cols, 1, LEV, LEV),
    ).reshape(row_count, col_count, value_count)
    return diffuse(advected, diffusivity, 0) * second_ratio[None, None, :]


def solution(mesh):
    return jax.shard_map(
        local,
        mesh=mesh,
        in_specs=(
            P(("groups", "lat"), "lon", None),
            P("groups", None, None, None),
            P("lat"),
            P("groups", None, None),
        ),
        out_specs=P(("groups", "lat"), "lon", None),
        check_vma=False,
    )
```

```python
import math

import jax
import jax.numpy as jnp
from jax import lax
from jax.sharding import PartitionSpec as P

LEV = 4
STEPS = 2
CAP = 4


def all_sum(value, axes, rider=None):
    rider_done = None
    for axis in axes:
        count = lax.axis_size(axis)
        if count & (count - 1):
            value = lax.psum(value, axis)
            continue
        distance = 1
        while distance < count:
            value = value + lax.ppermute(
                value, axis, [(i, i ^ distance) for i in range(count)]
            )
            if rider is not None:
                value, rider = lax.optimization_barrier((value, rider))
                rider_done, rider = rider, None
            distance *= 2
    if rider_done is None and rider is None:
        return value
    return value, rider if rider_done is None else rider_done


def neighbour_halos(lo_edge, hi_edge, axis, closed):
    count = lax.axis_size(axis)
    if count % 2:
        ends = count if closed else count - 1
        from_lo = lax.ppermute(hi_edge, axis, [(i, (i + 1) % count) for i in range(ends)])
        from_hi = lax.ppermute(lo_edge, axis, [((i + 1) % count, i) for i in range(ends)])
        return from_lo, from_hi
    even = lax.axis_index(axis) % 2 == 0
    first = lax.ppermute(
        jnp.where(even, hi_edge, lo_edge), axis, [(i, i ^ 1) for i in range(count)]
    )
    pairs = []
    for i in range(1, count, 2):
        if i + 1 < count:
            pairs += [(i, i + 1), (i + 1, i)]
        elif closed:
            pairs += [(i, 0), (0, i)]
    second = lax.ppermute(jnp.where(even, lo_edge, hi_edge), axis, pairs)
    return jnp.where(even, second, first), jnp.where(even, first, second)


def extended(cells, sides, width, closed):
    for axis, dim in sides:
        count = lax.axis_size(axis)
        ends = count if closed else count - 1
        head = lax.slice_in_dim(cells, 0, width, axis=dim)
        tail = lax.slice_in_dim(cells, cells.shape[dim] - width, cells.shape[dim], axis=dim)
        from_lo, from_hi = neighbour_halos(head, tail, axis, closed)
        cells = jnp.concatenate([from_lo, cells, from_hi], axis=dim)
    return cells


def cubic_weights(fraction):
    first_term = -fraction * (fraction - 1.0) * (fraction - 2.0) / 6.0
    second_term = (fraction + 1.0) * (fraction - 1.0) * (fraction - 2.0) / 2.0
    third_term = -(fraction + 1.0) * fraction * (fraction - 2.0) / 2.0
    fourth_term = (fraction + 1.0) * fraction * (fraction - 1.0) / 6.0
    return (first_term, second_term, third_term, fourth_term)


def cubic_matrix(fraction, extent):
    places = jnp.arange(extent)
    running = jnp.zeros(fraction.shape + (extent, extent), jnp.float32)
    for offset, weight in zip(range(-1, 3), cubic_weights(fraction)):
        target_col = jnp.clip(places + offset, 0, extent - 1)
        indicator = (target_col[:, None] == places[None, :]).astype(jnp.float32)
        running = running + weight[..., None, None] * indicator
    return running


def tap_sources(target, extent):
    return sorted({min(max(target + offset, 0), extent - 1) for offset in range(-1, 3)})


def plane_weights(fraction_y, fraction_x):
    rows = lax.broadcasted_iota(jnp.int32, (1, 64, 64), 1)
    cols = lax.broadcasted_iota(jnp.int32, (1, 64, 64), 2)

    def along(fraction, source, target):
        running = jnp.zeros((fraction.shape[0], 64, 64), jnp.float32)
        for offset, weight in zip(range(-1, 3), cubic_weights(fraction)):
            indicator = (jnp.clip(source + offset, 0, 7) == target).astype(jnp.float32)
            running = running + weight[:, None, None] * indicator
        return running

    return along(fraction_y, rows // 8, cols // 8) * along(fraction_x, rows % 8, cols % 8)


def spatial(patches, fraction_y, fraction_x):
    return jnp.einsum(
        "nij,njv->niv",
        plane_weights(fraction_y, fraction_x),
        patches,
        precision=lax.Precision.HIGHEST,
    )


def levels(flat, fraction_z):
    value_count = flat.shape[2]
    per_level = value_count // LEV
    weight_z = cubic_matrix(fraction_z, LEV)
    blocks = [flat[:, :, m * per_level : (m + 1) * per_level] for m in range(LEV)]
    out = []
    for level in range(LEV):
        acc = None
        for m in tap_sources(level, LEV):
            term = weight_z[:, level, m][:, None, None] * blocks[m]
            acc = term if acc is None else acc + term
        out.append(acc)
    return jnp.concatenate(out, axis=2)


def to_patches(state_field):
    band_rows = state_field.shape[0] // 8
    band_cols = state_field.shape[1] // 8
    return (
        state_field.reshape(band_rows, 8, band_cols, 8, -1)
        .transpose(0, 2, 1, 3, 4)
        .reshape(band_rows * band_cols, 64, -1)
    )


def from_patches(patches, band_rows, band_cols):
    return (
        patches.reshape(band_rows, band_cols, 8, 8, -1)
        .transpose(0, 2, 1, 3, 4)
        .reshape(band_rows * 8, band_cols * 8, -1)
    )


def column_area(first_row, row_count, total_rows):
    latitude = ((first_row + jnp.arange(row_count)).astype(jnp.float32) + 0.5) * (
        math.pi / total_rows
    ) - 0.5 * math.pi
    return jnp.cos(latitude)


def column_mass(state_field, weights):
    return jnp.sum(weights[:, None, None] * state_field, axis=(0, 1))


def diffuse(advected, diffusivity, row_dim):
    col_dim = row_dim + 1
    rows = advected.shape[row_dim]
    cols = advected.shape[col_dim]
    lon_wide = extended(advected, (("lon", col_dim),), 1, True)
    lat_wide = extended(advected, (("lat", row_dim),), 1, False)
    laplace = (
        lax.slice_in_dim(lat_wide, 2, rows + 2, axis=row_dim)
        + lax.slice_in_dim(lat_wide, 0, rows, axis=row_dim)
        + lax.slice_in_dim(lon_wide, 2, cols + 2, axis=col_dim)
        + lax.slice_in_dim(lon_wide, 0, cols, axis=col_dim)
        - 4.0 * advected
    )
    k_shape = [1] * advected.ndim
    k_shape[row_dim] = rows
    return advected + diffusivity.reshape(k_shape) * laplace


def levels_cols(values, weight_z):
    value_count = values.shape[-1]
    per_level = value_count // LEV
    blocks = [values[..., m * per_level : (m + 1) * per_level] for m in range(LEV)]
    out = []
    for level in range(LEV):
        acc = None
        for m in tap_sources(level, LEV):
            term = weight_z[..., level, m][..., None] * blocks[m]
            acc = term if acc is None else acc + term
        out.append(acc)
    return jnp.concatenate(out, axis=-1)


def diffuse_first(advected, diffusivity):
    rows, cols, value_count = advected.shape
    count = lax.axis_size("lat")

    def pack(row, number):
        return jnp.concatenate(
            [row, jnp.broadcast_to(number, (1, 1, value_count))], axis=1
        )

    from_above, from_below = neighbour_halos(
        pack(advected[:1], diffusivity[0]),
        pack(advected[rows - 1 :], diffusivity[rows - 1]),
        "lat",
        False,
    )
    lat_wide = jnp.concatenate([from_above[:, :cols], advected, from_below[:, :cols]], axis=0)
    k_wide = jnp.concatenate([from_above[0, cols, :1], diffusivity, from_below[0, cols, :1]])
    lon_wide = extended(advected, (("lon", 1),), 1, True)
    laplace = (
        lat_wide[2:] + lat_wide[:-2] + lon_wide[:, 2:] + lon_wide[:, :-2] - 4.0 * advected
    )
    return advected + diffusivity[:, None, None] * laplace, k_wide


def departed(state_field, source_ids, shifts_now, parts=False):
    lat_count = lax.axis_size("lat")
    lat_index = lax.axis_index("lat")
    lon_index = lax.axis_index("lon")
    row_count, col_count, value_count = state_field.shape
    band_rows = row_count // 8
    band_cols = col_count // 8
    per_device = band_rows * band_cols
    total_cols = source_ids.shape[1]
    devices = jnp.arange(lat_count)
    slot_range = jnp.arange(CAP)
    column_ids = lax.dynamic_slice_in_dim(
        source_ids, lon_index * band_cols, band_cols, 1
    ).reshape(lat_count, per_device)
    fractions = lax.dynamic_slice_in_dim(
        shifts_now, lon_index * band_cols, band_cols, 2
    ).reshape(3, lat_count, per_device)
    source_row = column_ids // total_cols
    source_dev = source_row // band_rows
    source_local = (
        source_row % band_rows * band_cols + column_ids % total_cols - lon_index * band_cols
    )
    remote = source_dev != devices[:, None]
    matches = (source_dev[:, :, None] == devices[None, None, :]) & remote[:, :, None]
    slot_ranks = jnp.cumsum(matches.astype(jnp.int32), axis=1) - 1
    slot_of = jnp.sum(jnp.where(matches, slot_ranks, 0), axis=2)
    owned_here = remote & (source_dev == lat_index)
    sending = owned_here[:, :, None] & (slot_of[:, :, None] == slot_range[None, None, :])
    send_local = jnp.sum(jnp.where(sending, source_local[:, :, None], 0), axis=1)
    own_patches = to_patches(state_field)
    outgoing = own_patches[send_local.reshape(-1)].reshape(lat_count, CAP, 64, value_count)
    my_dev = lax.dynamic_index_in_dim(source_dev, lat_index, 0, keepdims=False)
    my_slot = lax.dynamic_index_in_dim(slot_of, lat_index, 0, keepdims=False)
    my_local = lax.dynamic_index_in_dim(source_local, lat_index, 0, keepdims=False)
    my_remote = lax.dynamic_index_in_dim(remote, lat_index, 0, keepdims=False)
    my_frac = lax.dynamic_index_in_dim(fractions, lat_index, 1, keepdims=False)
    arrived = lax.all_to_all(outgoing, "lat", 0, 0, tiled=True).reshape(
        lat_count * CAP, 64, value_count
    )
    pick_index = my_dev * CAP + my_slot
    take_near = (my_local[:, None] == jnp.arange(per_device)[None, :]) & ~my_remote[:, None]
    take_far = (pick_index[:, None] == jnp.arange(lat_count * CAP)[None, :]) & my_remote[:, None]
    near = jnp.dot(
        take_near.astype(jnp.float32),
        own_patches.reshape(per_device, -1),
        precision=lax.Precision.HIGHEST,
    ).reshape(per_device, 64, value_count)
    patches = near + jnp.dot(
        take_far.astype(jnp.float32),
        arrived.reshape(lat_count * CAP, -1),
        precision=lax.Precision.HIGHEST,
    ).reshape(per_device, 64, value_count)
    if parts:
        return patches, my_frac, (near, take_far.astype(jnp.float32), arrived)
    return patches, my_frac


def local(tracers, shifts, diffusivity, source_patch):
    lat_count = lax.axis_size("lat")
    lat_index = lax.axis_index("lat")
    row_count, col_count, value_count = tracers.shape
    band_rows = row_count // 8
    band_cols = col_count // 8
    per_device = band_rows * band_cols
    per_level = value_count // LEV
    total_rows = row_count * lat_count
    weights = column_area(lat_index * row_count, row_count, total_rows)
    target_part = column_mass(tracers, weights)

    patches, frac = departed(tracers, source_patch[0], shifts[0])
    advected = from_patches(levels(spatial(patches, frac[0], frac[1]), frac[2]), band_rows, band_cols)
    first, k_wide = diffuse_first(advected, diffusivity)
    first_part = column_mass(first, weights)

    patches, frac, (near, take_far, arrived) = departed(
        first, source_patch[1], shifts[1], parts=True
    )
    plane = plane_weights(frac[0], frac[1])
    planar = jnp.einsum("nij,njv->niv", plane, patches, precision=lax.Precision.HIGHEST)
    weight_z = cubic_matrix(frac[2], LEV)

    area_wide = column_area(lat_index * row_count - 1, row_count + 2, total_rows)
    flux = area_wide * k_wide
    g = weights - 2.0 * flux[1:-1] + flux[:-2] + flux[2:]
    g_cols = jnp.broadcast_to(g.reshape(band_rows, 1, 8, 1), (band_rows, band_cols, 8, 8))
    row_weights = jnp.einsum(
        "pi,pij->pj", g_cols.reshape(per_device, 64), plane, precision=lax.Precision.HIGHEST
    )
    hi = lax.Precision.HIGHEST
    weighted_near = jnp.einsum("pj,pjv->pv", row_weights, near, precision=hi)
    mix_near = jnp.einsum(
        "plm,pmt->lmt", weight_z, weighted_near.reshape(per_device, LEV, per_level), precision=hi
    )
    slot_rows = jnp.einsum("ps,pj->sj", take_far, row_weights, precision=hi)
    slot_z = jnp.einsum("ps,plm->slm", take_far, weight_z, precision=hi)
    weighted_far = jnp.einsum("sj,sjv->sv", slot_rows, arrived, precision=hi)
    mix_part = mix_near + jnp.einsum(
        "slm,smt->lmt",
        slot_z,
        weighted_far.reshape(slot_z.shape[0], LEV, per_level),
        precision=hi,
    )
    field_planar = lax.optimization_barrier(from_patches(planar, band_rows, band_cols))
    partial = jnp.concatenate([target_part, first_part, mix_part.reshape(-1)])
    members = lat_count * lax.axis_size("lon")
    totals = jnp.sum(
        lax.all_to_all(
            jnp.broadcast_to(partial, (members,) + partial.shape), ("lat", "lon"), 0, 0, tiled=True
        ),
        axis=0,
    )
    target = totals[:value_count]
    first_mass = totals[value_count : 2 * value_count]
    mix = totals[2 * value_count :].reshape(LEV, LEV, per_level)
    first_ratio = target / first_mass
    second_mass = jnp.sum(first_ratio.reshape(LEV, per_level)[None] * mix, axis=1).reshape(
        value_count
    )
    second_ratio = target / second_mass
    advected = levels_cols(
        (field_planar * first_ratio).reshape(band_rows, 8, band_cols, 8, value_count),
        weight_z.reshape(band_rows, 1, band_cols, 1, LEV, LEV),
    ).reshape(row_count, col_count, value_count)
    return diffuse(advected, diffusivity, 0) * second_ratio[None, None, :]


def solution(mesh):
    return jax.shard_map(
        local,
        mesh=mesh,
        in_specs=(
            P(("groups", "lat"), "lon", None),
            P("groups", None, None, None),
            P("lat"),
            P("groups", None, None),
        ),
        out_specs=P(("groups", "lat"), "lon", None),
        check_vma=False,
    )
```
